32 devices in a mesh: gx: 2 (over core), ga: 4 (over y, x), gz: 4 (over z).
Axes of the slice: x: 2, y: 2, z: 4, core: 2. Of those that a mesh axis runs over, the one named last changes fastest.
Arguments:
- right_side: float32 [32, 64, 512], P('gx', 'ga', 'gz'), may hold values from -15 to 15
- diagonal: float32 [32, 64, 512], P('gx', 'ga', 'gz'), may hold values from 0.25 to 2
- basis_tables: float32 [3, 12, 12], replicated, may hold values from -1.75 to 1.75
- eigenvalues: float32 [3, 12], replicated, may hold values from 0.3 to 3
- coarse_blocks: float32 [2, 4, 4, 2, 64, 64], P('gx', 'ga', 'gz'), may hold values from -1 to 1
- coarse_columns: int32 [2, 4, 4, 2], P('gx', 'ga', 'gz'), may hold values from 0 to 15
Outputs:
- solution: float32 [32, 64, 512], P('gx', 'ga', 'gz')
- residual: float32 [32, 64, 512], P('gx', 'ga', 'gz')
The draws below stay inside these ranges and needn't reach their ends.
All inputs are finite; a program needn't handle non-finite values.
Results may differ from the reference program's by a relative error of at most 0.0003.
Values sent between devices are 32-bit elements; how exact they have to be, the bound alone decides.
No kernel may reach another device: no remote copies, remote signals or barrier semaphores. Data moves between devices by JAX's collectives and lax.ppermute only.
A program may use at most 64 MiB of HBM per device.

```python
import math
import jax
import jax.numpy as jnp
from jax import lax

PTS = 8
RIM = 2
WIDE = 12
EXD = 2
EYD = 2
EZD = 16
KBLK = 2
CYCLES = 2
CB = 64
NX = 32
NY = 64
NZ = 512
N_GX = 2
N_GA = 4
N_GZ = 4


def draw_right_side(key, part):
    ramp = 1.0 + 2.0 * jnp.arange(NX, dtype=jnp.float32) / (NX - 1)
    noise = jax.random.normal(key, (NX, NY, NZ), jnp.float32)
    values = noise * ramp[:, None, None]
    return jnp.clip(values, -15.0, 15.0)


def plant(drawn, rng, low, largest):
    place = [jax.random.randint(jax.random.fold_in(rng, axis), (), 0, length) for axis, length in enumerate(drawn.shape)]
    longest = drawn.shape.index(max(drawn.shape))
    beside = place[:longest] + [(place[longest] + 1) % drawn.shape[longest]] + place[longest + 1:]
    return drawn.at[tuple(place)].set(low).at[tuple(beside)].set(largest)


def levels(stream_key, shape, split, least, largest):
    factor_of = 1.0
    for position, shards_of in split:
        steps = jax.random.uniform(jax.random.fold_in(jax.random.fold_in(stream_key, 6), position), (shards_of,), jnp.float32, least / len(split), largest / len(split))
        factor_of = factor_of * jnp.repeat(jnp.exp(steps), shape[position] // shards_of).reshape((-1,) + (1,) * (len(shape) - 1 - position))
    return factor_of


def normal_values(own_key, extent, spread, bound, cuts=(), kind=jnp.bfloat16):
    result = spread * jax.random.normal(own_key, extent, jnp.float32)
    if cuts:
        result = result * levels(own_key, extent, cuts, -0.22, 0.18)
    return jnp.clip(result, -bound, bound).astype(kind)


def setup_inputs(seed: int = 0) -> dict:
    arg_keys = jax.random.split(jax.random.key(seed), 7)
    right_side = draw_right_side(jax.random.fold_in(arg_keys[6], 71), 0)
    diagonal = jnp.clip(0.25 + 1.75 * jax.random.uniform(arg_keys[1], (NX, NY, NZ), jnp.float32) ** levels(arg_keys[1], (NX, NY, NZ), ((0, 2), (1, 4), (2, 4)), -0.2, 0.2), 0.25, 2.0)
    basis_tables = normal_values(arg_keys[2], (3, WIDE, WIDE), WIDE ** -0.5, 1.75, (), jnp.float32)
    eigenvalues = jnp.clip(jnp.exp(jax.random.uniform(arg_keys[3], (3, WIDE), jnp.float32, math.log(0.3), math.log(3.0))), 0.3, 3.0)
    coarse_blocks = normal_values(arg_keys[4], (N_GX, N_GA, N_GZ, KBLK, CB, CB), (max(KBLK * CB // 4, 1)) ** -0.5, 1.0, ((0, 2), (1, 4), (2, 4)), jnp.float32)
    coarse_columns = plant(jax.random.randint(arg_keys[5], (N_GX, N_GA, N_GZ, KBLK), 0, N_GA * N_GZ), jax.random.fold_in(arg_keys[5], 1), 0, (N_GA * N_GZ) - 1).astype(jnp.int32)
    return dict(right_side=right_side, diagonal=diagonal, basis_tables=basis_tables, eigenvalues=eigenvalues, coarse_blocks=coarse_blocks, coarse_columns=coarse_columns)


PRECISE = lax.Precision.HIGHEST

def operate(field, diagonal):
    padded = jnp.pad(field, 1)
    beside = padded[2:, 1:-1, 1:-1] + padded[:-2, 1:-1, 1:-1]
    beside = beside + padded[1:-1, 2:, 1:-1] + padded[1:-1, :-2, 1:-1]
    beside = beside + padded[1:-1, 1:-1, 2:] + padded[1:-1, 1:-1, :-2]
    return (6.0 + diagonal) * field - beside

def windows(padded, axis, count):
    pieces = [lax.slice_in_dim(padded, offset, offset + PTS * (count - 1) + 1, PTS, axis) for offset in range(WIDE)]
    return jnp.stack(pieces, axis=axis + 1)

def schwarz_part(field, basis_tables, eigenvalues):
    count_x = NX // PTS
    count_y = NY // PTS
    count_z = NZ // PTS
    padded = jnp.pad(field, RIM)
    blocks = windows(padded, 0, count_x)
    blocks = windows(blocks, 2, count_y)
    blocks = windows(blocks, 4, count_z)
    spectral = jnp.einsum('ajbkcl,jm->ambkcl', blocks, basis_tables[0], precision=PRECISE)
    spectral = jnp.einsum('ambkcl,kn->ambncl', spectral, basis_tables[1], precision=PRECISE)
    spectral = jnp.einsum('ambncl,lo->ambnco', spectral, basis_tables[2], precision=PRECISE)
    denominator = eigenvalues[0][:, None, None] + eigenvalues[1][None, :, None] + eigenvalues[2][None, None, :]
    spectral = spectral / denominator[None, :, None, :, None, :]
    inner_rows = basis_tables[:, RIM:RIM + PTS, :]
    local_part = jnp.einsum('ambnco,im->aibnco', spectral, inner_rows[0], precision=PRECISE)
    local_part = jnp.einsum('aibnco,jn->aibjco', local_part, inner_rows[1], precision=PRECISE)
    local_part = jnp.einsum('aibjco,ko->aibjck', local_part, inner_rows[2], precision=PRECISE)
    return local_part.reshape(NX, NY, NZ)

def coarse_part(field, coarse_blocks, coarse_columns):
    count_x = NX // PTS
    count_y = NY // PTS
    count_z = NZ // PTS
    group = N_GA * N_GZ
    cells = EXD * EYD * EZD
    means = lax.optimization_barrier(jnp.mean(field.reshape(count_x, PTS, count_y, PTS, count_z, PTS), axis=(1, 3, 5)))
    restricted = means.reshape(N_GX, EXD, N_GA, EYD, N_GZ, EZD).transpose(0, 2, 4, 1, 3, 5).reshape(N_GX, group, cells)
    matrices = coarse_blocks.reshape(N_GX, group, KBLK, cells, cells)
    selector = (coarse_columns.reshape(N_GX, group, KBLK)[..., None] == jnp.arange(group, dtype=jnp.int32)).astype(restricted.dtype)
    terms = jnp.einsum('gikpq,gip->gikq', matrices, restricted, precision=PRECISE)
    shared = jnp.einsum('gikq,gikj->gjq', terms, selector, precision=PRECISE)
    picked = jnp.einsum('gikj,gjq->gikq', selector, shared, precision=PRECISE)
    coarse = jnp.einsum('gikpq,gikq->gip', matrices, picked, precision=PRECISE)
    coarse = coarse.reshape(N_GX, N_GA, N_GZ, EXD, EYD, EZD).transpose(0, 3, 1, 4, 2, 5)
    coarse = coarse.reshape(count_x, 1, count_y, 1, count_z, 1)
    return jnp.broadcast_to(coarse, (count_x, PTS, count_y, PTS, count_z, PTS)).reshape(NX, NY, NZ)

def precondition(field, basis_tables, eigenvalues, coarse_blocks, coarse_columns):
    return schwarz_part(field, basis_tables, eigenvalues) + coarse_part(field, coarse_blocks, coarse_columns)

def reference(right_side, diagonal, basis_tables, eigenvalues, coarse_blocks, coarse_columns):
    solution = jnp.zeros_like(right_side)
    residual = right_side
    for restart in range(CYCLES):
        initial_norm = jnp.sqrt(jnp.sum(residual * residual))
        first_vector = residual / initial_norm
        first_zed = precondition(first_vector, basis_tables, eigenvalues, coarse_blocks, coarse_columns)
        first_image = operate(first_zed, diagonal)
        first_proj = jnp.sum(first_vector * first_image)
        first_ortho = first_image - first_proj * first_vector
        first_len = jnp.sqrt(jnp.sum(first_ortho * first_ortho))
        second_vector = first_ortho / first_len
        second_zed = precondition(second_vector, basis_tables, eigenvalues, coarse_blocks, coarse_columns)
        second_image = operate(second_zed, diagonal)
        upper_proj = jnp.sum(first_vector * second_image)
        lower_proj = jnp.sum(second_vector * second_image)
        second_ortho = second_image - upper_proj * first_vector - lower_proj * second_vector
        second_len = jnp.sqrt(jnp.sum(second_ortho * second_ortho))
        gram_first = first_proj * first_proj + first_len * first_len
        gram_cross = first_proj * upper_proj + first_len * lower_proj
        gram_second = upper_proj * upper_proj + lower_proj * lower_proj + second_len * second_len
        target_first = initial_norm * first_proj
        target_second = initial_norm * upper_proj
        determinant = gram_first * gram_second - gram_cross * gram_cross
        weight_first = (gram_second * target_first - gram_cross * target_second) / determinant
        weight_second = (gram_first * target_second - gram_cross * target_first) / determinant
        solution = solution + weight_first * first_zed + weight_second * second_zed
        residual = right_side - operate(solution, diagonal)
    return (solution, residual)
```

```python
import jax
import jax.numpy as jnp
from jax import lax
from jax.sharding import PartitionSpec as P

PTS = 8
RIM = 2
WIDE = 12
CYCLES = 2


PRECISE = lax.Precision.HIGHEST


def padded_2(value, sides, width):
    for axis, dim in sides:
        size, length = (lax.axis_size(axis), value.shape[dim])
        up = [(i, (i + 1) % size) for i in range(size - 1)]
        down = [(j, i) for i, j in up]
        last = lax.slice_in_dim(value, length - width, length, axis=dim)
        leading = lax.slice_in_dim(value, 0, width, axis=dim)
        before = lax.ppermute(last, axis, up)
        after = lax.ppermute(leading, axis, down)
        value = jnp.concatenate([before, value, after], axis=dim)
    return value


def operate(field, diagonal):
    padded = padded_2(field, (("gx", 0), ("ga", 1), ("gz", 2)), 1)
    beside = padded[2:, 1:-1, 1:-1] + padded[:-2, 1:-1, 1:-1]
    beside = beside + padded[1:-1, 2:, 1:-1] + padded[1:-1, :-2, 1:-1]
    beside = beside + padded[1:-1, 1:-1, 2:] + padded[1:-1, 1:-1, :-2]
    return (6.0 + diagonal) * field - beside


def forward_table(count, basis):
    row_index = jnp.arange(PTS * count + 2 * RIM, dtype=jnp.int32)
    element = jnp.arange(count, dtype=jnp.int32)
    offset = jnp.arange(WIDE, dtype=jnp.int32)
    select = (
        row_index[:, None, None] == PTS * element[None, :, None] + offset[None, None, :]
    ).astype(jnp.float32)
    table = jnp.einsum("rcj,jm->rcm", select, basis, precision=PRECISE)
    return table.reshape(PTS * count + 2 * RIM, count * WIDE)


def backward_table(count, basis):
    same = jnp.eye(count, dtype=jnp.float32)
    table = jnp.einsum("cd,im->cmdi", same, basis[RIM : RIM + PTS], precision=PRECISE)
    return table.reshape(count * WIDE, count * PTS)


def schwarz_part(field, basis_tables, eigenvalues):
    count_x = field.shape[0] // PTS
    count_y = field.shape[1] // PTS
    count_z = field.shape[2] // PTS
    padded = padded_2(field, (("gx", 0), ("ga", 1), ("gz", 2)), RIM)
    spectral = jnp.einsum(
        "pqr,rc->pqc", padded, forward_table(count_z, basis_tables[2]), precision=PRECISE
    )
    spectral = jnp.einsum(
        "pqc,pa->aqc", spectral, forward_table(count_x, basis_tables[0]), precision=PRECISE
    )
    spectral = jnp.einsum(
        "aqc,qb->abc", spectral, forward_table(count_y, basis_tables[1]), precision=PRECISE
    )
    denominator = (
        jnp.tile(eigenvalues[0], count_x)[:, None, None]
        + jnp.tile(eigenvalues[1], count_y)[None, :, None]
    )
    denominator = denominator + jnp.tile(eigenvalues[2], count_z)[None, None, :]
    spectral = spectral / denominator
    local_part = jnp.einsum(
        "abc,cr->abr", spectral, backward_table(count_z, basis_tables[2]), precision=PRECISE
    )
    local_part = jnp.einsum(
        "abr,ap->pbr", local_part, backward_table(count_x, basis_tables[0]), precision=PRECISE
    )
    local_part = jnp.einsum(
        "pbr,bq->pqr", local_part, backward_table(count_y, basis_tables[1]), precision=PRECISE
    )
    return local_part


def coarse_terms(field, blocks, selector):
    count_x = field.shape[0] // PTS
    count_y = field.shape[1] // PTS
    count_z = field.shape[2] // PTS
    cells = count_x * count_y * count_z
    means = jnp.mean(field.reshape(count_x, PTS, count_y, PTS, count_z, PTS), axis=(1, 3, 5))
    restricted = means.reshape(cells)
    terms = jnp.einsum("kpq,p->kq", blocks, restricted, precision=PRECISE)
    return jnp.einsum("kj,kq->jq", selector, terms, precision=PRECISE)


def coarse_apply(whole, blocks, selector, shape):
    count_x = shape[0] // PTS
    count_y = shape[1] // PTS
    count_z = shape[2] // PTS
    picked = jnp.dot(selector, whole, precision=PRECISE)
    coarse = jnp.einsum("kpq,kq->p", blocks, picked, precision=PRECISE)
    coarse = coarse.reshape(count_x, 1, count_y, 1, count_z, 1)
    spread = jnp.broadcast_to(coarse, (count_x, PTS, count_y, PTS, count_z, PTS))
    return spread.reshape(shape)


ALL = ("gx", "ga", "gz")


def reduce_all(buffer, scalars):
    n_gx = lax.axis_size("gx")
    me = lax.axis_index("gx")
    slot = (jnp.arange(n_gx, dtype=jnp.int32) == me).astype(jnp.float32)
    parts = [] if buffer is None else [(slot[:, None, None] * buffer[None]).reshape(-1)]
    payload = jnp.concatenate(parts + [jnp.stack(scalars)])
    total = lax.psum(payload, ALL)
    sums = [total[total.shape[0] - len(scalars) + i] for i in range(len(scalars))]
    if buffer is None:
        return None, sums
    wide = total[: total.shape[0] - len(scalars)].reshape((n_gx,) + buffer.shape)
    return lax.dynamic_index_in_dim(wide, me, 0, keepdims=False), sums


def body(right_side, diagonal, basis_tables, eigenvalues, coarse_blocks, coarse_columns):
    blocks = coarse_blocks.reshape(coarse_blocks.shape[3:])
    columns = coarse_columns.reshape(coarse_columns.shape[3])
    group = lax.axis_size(("ga", "gz"))
    selector = (columns[:, None] == jnp.arange(group, dtype=jnp.int32)[None, :]).astype(jnp.float32)
    shape = right_side.shape

    solution = jnp.zeros_like(right_side)
    residual = right_side
    for restart in range(CYCLES):
        whole_r, (square,) = reduce_all(
            coarse_terms(residual, blocks, selector), [jnp.sum(residual * residual)]
        )
        initial_norm = jnp.sqrt(square)
        first_vector = residual / initial_norm
        first_zed = (
            schwarz_part(residual, basis_tables, eigenvalues)
            + coarse_apply(whole_r, blocks, selector, shape)
        ) / initial_norm
        first_image = operate(first_zed, diagonal)
        whole_w, (first_proj, image_square) = reduce_all(
            coarse_terms(first_image, blocks, selector),
            [jnp.sum(first_vector * first_image), jnp.sum(first_image * first_image)],
        )
        first_len = jnp.sqrt(image_square - first_proj * first_proj)
        image_zed = schwarz_part(first_image, basis_tables, eigenvalues) + coarse_apply(
            whole_w, blocks, selector, shape
        )
        second_vector = (first_image - first_proj * first_vector) / first_len
        second_zed = (image_zed - first_proj * first_zed) / first_len
        second_image = operate(second_zed, diagonal)
        _, (upper_proj, lower_proj, second_square) = reduce_all(
            None,
            [
                jnp.sum(first_vector * second_image),
                jnp.sum(second_vector * second_image),
                jnp.sum(second_image * second_image),
            ],
        )
        second_len = jnp.sqrt(second_square - upper_proj * upper_proj - lower_proj * lower_proj)
        gram_first = first_proj * first_proj + first_len * first_len
        gram_cross = first_proj * upper_proj + first_len * lower_proj
        gram_second = upper_proj * upper_proj + lower_proj * lower_proj + second_len * second_len
        target_first = initial_norm * first_proj
        target_second = initial_norm * upper_proj
        determinant = gram_first * gram_second - gram_cross * gram_cross
        weight_first = (gram_second * target_first - gram_cross * target_second) / determinant
        weight_second = (gram_first * target_second - gram_cross * target_first) / determinant
        solution = solution + weight_first * first_zed + weight_second * second_zed
        residual = right_side - operate(solution, diagonal)
    return (solution, residual)


def solution(mesh):
    in_specs = (
        P("gx", "ga", "gz"),
        P("gx", "ga", "gz"),
        P(),
        P(),
        P("gx", "ga", "gz", None, None, None),
        P("gx", "ga", "gz", None),
    )
    out_specs = (P("gx", "ga", "gz"), P("gx", "ga", "gz"))
    return jax.shard_map(body, mesh=mesh, in_specs=in_specs, out_specs=out_specs, check_vma=False)
```

```python
import jax
import jax.numpy as jnp
from jax import lax
from jax.sharding import PartitionSpec as P

PTS = 8
RIM = 2
WIDE = 12
CYCLES = 2


PRECISE = lax.Precision.HIGHEST


def padded_2(value, sides, width):
    for axis, dim in sides:
        size, length = (lax.axis_size(axis), value.shape[dim])
        up = [(i, (i + 1) % size) for i in range(size - 1)]
        down = [(j, i) for i, j in up]
        last = lax.slice_in_dim(value, length - width, length, axis=dim)
        leading = lax.slice_in_dim(value, 0, width, axis=dim)
        before = lax.ppermute(last, axis, up)
        after = lax.ppermute(leading, axis, down)
        value = jnp.concatenate([before, value, after], axis=dim)
    return value


SIDES = (("gx", 0), ("ga", 1), ("gz", 2))


def operate_rim(zed, diagonal, inside):
    centre = zed[1:-1, 1:-1, 1:-1]
    beside = zed[2:, 1:-1, 1:-1] + zed[:-2, 1:-1, 1:-1]
    beside = beside + zed[1:-1, 2:, 1:-1] + zed[1:-1, :-2, 1:-1]
    beside = beside + zed[1:-1, 1:-1, 2:] + zed[1:-1, 1:-1, :-2]
    return ((6.0 + diagonal) * centre - beside) * inside


def inside_grid(shape, width):
    result = None
    for axis, dim in SIDES:
        length = shape[dim]
        place = lax.axis_index(axis) * length - width + jnp.arange(length + 2 * width, dtype=jnp.int32)
        line = ((place >= 0) & (place < lax.axis_size(axis) * length)).astype(jnp.float32)
        view = [1, 1, 1]
        view[dim] = length + 2 * width
        line = line.reshape(view)
        result = line if result is None else result * line
    return result


def interior(value, width):
    return value[width:-width, width:-width, width:-width]


def forward_table(count, basis):
    row_index = jnp.arange(PTS * count + 2 * RIM, dtype=jnp.int32)
    element = jnp.arange(count, dtype=jnp.int32)
    offset = jnp.arange(WIDE, dtype=jnp.int32)
    select = (
        row_index[:, None, None] == PTS * element[None, :, None] + offset[None, None, :]
    ).astype(jnp.float32)
    table = jnp.einsum("rcj,jm->rcm", select, basis, precision=PRECISE)
    return table.reshape(PTS * count + 2 * RIM, count * WIDE)


def backward_table(count, basis):
    same = jnp.eye(count, dtype=jnp.float32)
    table = jnp.einsum("cd,im->cmdi", same, basis[RIM : RIM + PTS], precision=PRECISE)
    return table.reshape(count * WIDE, count * PTS)


def schwarz_part(padded, basis_tables, eigenvalues):
    count_x = (padded.shape[0] - 2 * RIM) // PTS
    count_y = (padded.shape[1] - 2 * RIM) // PTS
    count_z = (padded.shape[2] - 2 * RIM) // PTS
    spectral = jnp.einsum(
        "pqr,rc->pqc", padded, forward_table(count_z, basis_tables[2]), precision=PRECISE
    )
    spectral = jnp.einsum(
        "pqc,pa->aqc", spectral, forward_table(count_x, basis_tables[0]), precision=PRECISE
    )
    spectral = jnp.einsum(
        "aqc,qb->abc", spectral, forward_table(count_y, basis_tables[1]), precision=PRECISE
    )
    denominator = (
        jnp.tile(eigenvalues[0], count_x)[:, None, None]
        + jnp.tile(eigenvalues[1], count_y)[None, :, None]
    )
    denominator = denominator + jnp.tile(eigenvalues[2], count_z)[None, None, :]
    spectral = spectral / denominator
    local_part = jnp.einsum(
        "abc,cr->abr", spectral, backward_table(count_z, basis_tables[2]), precision=PRECISE
    )
    local_part = jnp.einsum(
        "abr,ap->pbr", local_part, backward_table(count_x, basis_tables[0]), precision=PRECISE
    )
    local_part = jnp.einsum(
        "pbr,bq->pqr", local_part, backward_table(count_y, basis_tables[1]), precision=PRECISE
    )
    return local_part


def coarse_terms(field, blocks, selector):
    count_x = field.shape[0] // PTS
    count_y = field.shape[1] // PTS
    count_z = field.shape[2] // PTS
    cells = count_x * count_y * count_z
    means = jnp.mean(field.reshape(count_x, PTS, count_y, PTS, count_z, PTS), axis=(1, 3, 5))
    restricted = means.reshape(cells)
    terms = jnp.einsum("kpq,p->kq", blocks, restricted, precision=PRECISE)
    return jnp.einsum("kj,kq->jq", selector, terms, precision=PRECISE)


def coarse_apply(whole, blocks, selector, shape):
    count_x = shape[0] // PTS
    count_y = shape[1] // PTS
    count_z = shape[2] // PTS
    picked = jnp.dot(selector, whole, precision=PRECISE)
    coarse = jnp.einsum("kpq,kq->p", blocks, picked, precision=PRECISE)
    coarse = coarse.reshape(count_x, 1, count_y, 1, count_z, 1)
    spread = jnp.broadcast_to(coarse, (count_x, PTS, count_y, PTS, count_z, PTS))
    return spread.reshape(shape)


ALL = ("gx", "ga", "gz")


def reduce_all(buffer, scalars):
    n_gx = lax.axis_size("gx")
    me = lax.axis_index("gx")
    slot = (jnp.arange(n_gx, dtype=jnp.int32) == me).astype(jnp.float32)
    parts = [] if buffer is None else [(slot[:, None, None] * buffer[None]).reshape(-1)]
    payload = jnp.concatenate(parts + [jnp.stack(scalars)])
    total = lax.psum(payload, ALL)
    sums = [total[total.shape[0] - len(scalars) + i] for i in range(len(scalars))]
    if buffer is None:
        return None, sums
    wide = total[: total.shape[0] - len(scalars)].reshape((n_gx,) + buffer.shape)
    return lax.dynamic_index_in_dim(wide, me, 0, keepdims=False), sums


def body(right_side, diagonal, basis_tables, eigenvalues, coarse_blocks, coarse_columns):
    blocks = coarse_blocks.reshape(coarse_blocks.shape[3:])
    columns = coarse_columns.reshape(coarse_columns.shape[3])
    group = lax.axis_size(("ga", "gz"))
    selector = (columns[:, None] == jnp.arange(group, dtype=jnp.int32)[None, :]).astype(jnp.float32)
    shape = right_side.shape
    wide_diagonal = padded_2(diagonal, SIDES, RIM)
    inside = inside_grid(shape, RIM)
    wide_residual = padded_2(right_side, SIDES, RIM)

    solution = jnp.zeros_like(right_side)
    for restart in range(CYCLES):
        residual = interior(wide_residual, RIM)
        whole_r, (square,) = reduce_all(
            coarse_terms(residual, blocks, selector), [jnp.sum(residual * residual)]
        )
        initial_norm = jnp.sqrt(square)
        first_vector = residual / initial_norm
        first_zed = (
            schwarz_part(wide_residual, basis_tables, eigenvalues)
            + coarse_apply(whole_r, blocks, selector, shape)
        ) / initial_norm
        wide_first = operate_rim(padded_2(first_zed, SIDES, RIM + 1), wide_diagonal, inside)
        first_image = interior(wide_first, RIM)
        whole_w, (first_proj, image_square) = reduce_all(
            coarse_terms(first_image, blocks, selector),
            [jnp.sum(first_vector * first_image), jnp.sum(first_image * first_image)],
        )
        first_len = jnp.sqrt(image_square - first_proj * first_proj)
        image_zed = schwarz_part(wide_first, basis_tables, eigenvalues) + coarse_apply(
            whole_w, blocks, selector, shape
        )
        second_vector = (first_image - first_proj * first_vector) / first_len
        second_zed = (image_zed - first_proj * first_zed) / first_len
        wide_second = operate_rim(padded_2(second_zed, SIDES, RIM + 1), wide_diagonal, inside)
        second_image = interior(wide_second, RIM)
        _, (upper_proj, lower_proj, second_square) = reduce_all(
            None,
            [
                jnp.sum(first_vector * second_image),
                jnp.sum(second_vector * second_image),
                jnp.sum(second_image * second_image),
            ],
        )
        second_len = jnp.sqrt(second_square - upper_proj * upper_proj - lower_proj * lower_proj)
        gram_first = first_proj * first_proj + first_len * first_len
        gram_cross = first_proj * upper_proj + first_len * lower_proj
        gram_second = upper_proj * upper_proj + lower_proj * lower_proj + second_len * second_len
        target_first = initial_norm * first_proj
        target_second = initial_norm * upper_proj
        determinant = gram_first * gram_second - gram_cross * gram_cross
        weight_first = (gram_second * target_first - gram_cross * target_second) / determinant
        weight_second = (gram_first * target_second - gram_cross * target_first) / determinant
        solution = solution + weight_first * first_zed + weight_second * second_zed
        wide_residual = wide_residual - weight_first * wide_first - weight_second * wide_second
    return (solution, interior(wide_residual, RIM))


def solution(mesh):
    in_specs = (
        P("gx", "ga", "gz"),
        P("gx", "ga", "gz"),
        P(),
        P(),
        P("gx", "ga", "gz", None, None, None),
        P("gx", "ga", "gz", None),
    )
    out_specs = (P("gx", "ga", "gz"), P("gx", "ga", "gz"))
    return jax.shard_map(body, mesh=mesh, in_specs=in_specs, out_specs=out_specs, check_vma=False)
```

```python
import jax
import jax.numpy as jnp
from jax import lax
from jax.sharding import PartitionSpec as P

PTS = 8
RIM = 2
WIDE = 12
CYCLES = 2


PRECISE = lax.Precision.HIGHEST


def padded_2(value, sides, width):
    for axis, dim in sides:
        size, length = (lax.axis_size(axis), value.shape[dim])
        up = [(i, (i + 1) % size) for i in range(size - 1)]
        down = [(j, i) for i, j in up]
        last = lax.slice_in_dim(value, length - width, length, axis=dim)
        leading = lax.slice_in_dim(value, 0, width, axis=dim)
        before = lax.ppermute(last, axis, up)
        after = lax.ppermute(leading, axis, down)
        value = jnp.concatenate([before, value, after], axis=dim)
    return value


SIDES = (("gx", 0), ("ga", 1), ("gz", 2))


def operate_rim(zed, diagonal, inside):
    centre = zed[1:-1, 1:-1, 1:-1]
    beside = zed[2:, 1:-1, 1:-1] + zed[:-2, 1:-1, 1:-1]
    beside = beside + zed[1:-1, 2:, 1:-1] + zed[1:-1, :-2, 1:-1]
    beside = beside + zed[1:-1, 1:-1, 2:] + zed[1:-1, 1:-1, :-2]
    return ((6.0 + diagonal) * centre - beside) * inside


def inside_grid(shape, width):
    result = None
    for axis, dim in SIDES:
        length = shape[dim]
        place = lax.axis_index(axis) * length - width + jnp.arange(length + 2 * width, dtype=jnp.int32)
        line = ((place >= 0) & (place < lax.axis_size(axis) * length)).astype(jnp.float32)
        view = [1, 1, 1]
        view[dim] = length + 2 * width
        line = line.reshape(view)
        result = line if result is None else result * line
    return result


def interior(value, width):
    return value[width:-width, width:-width, width:-width]


def forward_table(count, basis):
    row_index = jnp.arange(PTS * count + 2 * RIM, dtype=jnp.int32)
    element = jnp.arange(count, dtype=jnp.int32)
    offset = jnp.arange(WIDE, dtype=jnp.int32)
    select = (
        row_index[:, None, None] == PTS * element[None, :, None] + offset[None, None, :]
    ).astype(jnp.float32)
    table = jnp.einsum("rcj,jm->rcm", select, basis, precision=PRECISE)
    return table.reshape(PTS * count + 2 * RIM, count * WIDE)


def backward_table(count, basis):
    same = jnp.eye(count, dtype=jnp.float32)
    table = jnp.einsum("cd,im->cmdi", same, basis[RIM : RIM + PTS], precision=PRECISE)
    return table.reshape(count * WIDE, count * PTS)


def schwarz_part(padded, basis_tables, eigenvalues):
    count_x = (padded.shape[0] - 2 * RIM) // PTS
    count_y = (padded.shape[1] - 2 * RIM) // PTS
    count_z = (padded.shape[2] - 2 * RIM) // PTS
    spectral = jnp.einsum(
        "pqr,rc->pqc", padded, forward_table(count_z, basis_tables[2]), precision=PRECISE
    )
    spectral = jnp.einsum(
        "pqc,pa->aqc", spectral, forward_table(count_x, basis_tables[0]), precision=PRECISE
    )
    spectral = jnp.einsum(
        "aqc,qb->abc", spectral, forward_table(count_y, basis_tables[1]), precision=PRECISE
    )
    denominator = (
        jnp.tile(eigenvalues[0], count_x)[:, None, None]
        + jnp.tile(eigenvalues[1], count_y)[None, :, None]
    )
    denominator = denominator + jnp.tile(eigenvalues[2], count_z)[None, None, :]
    spectral = spectral / denominator
    local_part = jnp.einsum(
        "abc,cr->abr", spectral, backward_table(count_z, basis_tables[2]), precision=PRECISE
    )
    local_part = jnp.einsum(
        "abr,ap->pbr", local_part, backward_table(count_x, basis_tables[0]), precision=PRECISE
    )
    local_part = jnp.einsum(
        "pbr,bq->pqr", local_part, backward_table(count_y, basis_tables[1]), precision=PRECISE
    )
    return local_part


def coarse_terms(field, blocks, selector):
    count_x = field.shape[0] // PTS
    count_y = field.shape[1] // PTS
    count_z = field.shape[2] // PTS
    cells = count_x * count_y * count_z
    means = jnp.mean(field.reshape(count_x, PTS, count_y, PTS, count_z, PTS), axis=(1, 3, 5))
    restricted = means.reshape(cells)
    terms = jnp.einsum("kpq,p->kq", blocks, restricted, precision=PRECISE)
    return jnp.einsum("kj,kq->jq", selector, terms, precision=PRECISE)


def coarse_apply(whole, blocks, selector, shape):
    count_x = shape[0] // PTS
    count_y = shape[1] // PTS
    count_z = shape[2] // PTS
    picked = jnp.dot(selector, whole, precision=PRECISE)
    coarse = jnp.einsum("kpq,kq->p", blocks, picked, precision=PRECISE)
    coarse = coarse.reshape(count_x, 1, count_y, 1, count_z, 1)
    spread = jnp.broadcast_to(coarse, (count_x, PTS, count_y, PTS, count_z, PTS))
    return spread.reshape(shape)


ALL = ("gx", "ga", "gz")


def butterfly(value, axes):
    for axis in axes:
        size = lax.axis_size(axis)
        if size & (size - 1):
            value = lax.psum(value, axis)
            continue
        step = 1
        while step < size:
            value = value + lax.ppermute(value, axis, [(i, i ^ step) for i in range(size)])
            step *= 2
    return value


def reduce_all(buffer, scalars):
    count = len(scalars)
    if buffer is None:
        total = butterfly(jnp.stack(scalars), ALL)
        return None, [total[i] for i in range(count)]
    payload = jnp.concatenate([buffer.reshape(-1), jnp.stack(scalars)])
    payload = butterfly(payload, ("ga", "gz"))
    size = payload.shape[0] - count
    total = butterfly(payload[size:], ("gx",))
    return payload[:size].reshape(buffer.shape), [total[i] for i in range(count)]


def body(right_side, diagonal, basis_tables, eigenvalues, coarse_blocks, coarse_columns):
    blocks = coarse_blocks.reshape(coarse_blocks.shape[3:])
    columns = coarse_columns.reshape(coarse_columns.shape[3])
    group = lax.axis_size(("ga", "gz"))
    selector = (columns[:, None] == jnp.arange(group, dtype=jnp.int32)[None, :]).astype(jnp.float32)
    shape = right_side.shape
    wide_diagonal = padded_2(diagonal, SIDES, RIM)
    inside = inside_grid(shape, RIM)
    wide_residual = padded_2(right_side, SIDES, RIM)

    solution = jnp.zeros_like(right_side)
    for restart in range(CYCLES):
        residual = interior(wide_residual, RIM)
        whole_r, (square,) = reduce_all(
            coarse_terms(residual, blocks, selector), [jnp.sum(residual * residual)]
        )
        initial_norm = jnp.sqrt(square)
        first_vector = residual / initial_norm
        first_zed = (
            schwarz_part(wide_residual, basis_tables, eigenvalues)
            + coarse_apply(whole_r, blocks, selector, shape)
        ) / initial_norm
        wide_first = operate_rim(padded_2(first_zed, SIDES, RIM + 1), wide_diagonal, inside)
        first_image = interior(wide_first, RIM)
        whole_w, (first_proj, image_square) = reduce_all(
            coarse_terms(first_image, blocks, selector),
            [jnp.sum(first_vector * first_image), jnp.sum(first_image * first_image)],
        )
        first_len = jnp.sqrt(image_square - first_proj * first_proj)
        image_zed = schwarz_part(wide_first, basis_tables, eigenvalues) + coarse_apply(
            whole_w, blocks, selector, shape
        )
        second_vector = (first_image - first_proj * first_vector) / first_len
        second_zed = (image_zed - first_proj * first_zed) / first_len
        wide_second = operate_rim(padded_2(second_zed, SIDES, RIM + 1), wide_diagonal, inside)
        second_image = interior(wide_second, RIM)
        _, (upper_proj, lower_proj, second_square) = reduce_all(
            None,
            [
                jnp.sum(first_vector * second_image),
                jnp.sum(second_vector * second_image),
                jnp.sum(second_image * second_image),
            ],
        )
        second_len = jnp.sqrt(second_square - upper_proj * upper_proj - lower_proj * lower_proj)
        gram_first = first_proj * first_proj + first_len * first_len
        gram_cross = first_proj * upper_proj + first_len * lower_proj
        gram_second = upper_proj * upper_proj + lower_proj * lower_proj + second_len * second_len
        target_first = initial_norm * first_proj
        target_second = initial_norm * upper_proj
        determinant = gram_first * gram_second - gram_cross * gram_cross
        weight_first = (gram_second * target_first - gram_cross * target_second) / determinant
        weight_second = (gram_first * target_second - gram_cross * target_first) / determinant
        solution = solution + weight_first * first_zed + weight_second * second_zed
        wide_residual = wide_residual - weight_first * wide_first - weight_second * wide_second
    return (solution, interior(wide_residual, RIM))


def solution(mesh):
    in_specs = (
        P("gx", "ga", "gz"),
        P("gx", "ga", "gz"),
        P(),
        P(),
        P("gx", "ga", "gz", None, None, None),
        P("gx", "ga", "gz", None),
    )
    out_specs = (P("gx", "ga", "gz"), P("gx", "ga", "gz"))
    return jax.shard_map(body, mesh=mesh, in_specs=in_specs, out_specs=out_specs, check_vma=False)
```

```python
import jax
import jax.numpy as jnp
from jax import lax
from jax.sharding import PartitionSpec as P

PTS = 8
RIM = 2
WIDE = 12
CYCLES = 2


PRECISE = lax.Precision.HIGHEST


def padded_2(value, sides, width):
    for axis, dim in sides:
        size, length = (lax.axis_size(axis), value.shape[dim])
        last = lax.slice_in_dim(value, length - width, length, axis=dim)
        leading = lax.slice_in_dim(value, 0, width, axis=dim)
        if size == 2:
            first = lax.axis_index(axis) == 0
            got = lax.ppermute(jnp.where(first, last, leading), axis, [(0, 1), (1, 0)])
            zero = jnp.zeros_like(got)
            before = jnp.where(first, zero, got)
            after = jnp.where(first, got, zero)
        else:
            up = [(i, (i + 1) % size) for i in range(size - 1)]
            down = [(j, i) for i, j in up]
            before = lax.ppermute(last, axis, up)
            after = lax.ppermute(leading, axis, down)
        value = jnp.concatenate([before, value, after], axis=dim)
    return value


SIDES = (("gx", 0), ("ga", 1), ("gz", 2))


def operate_rim(zed, diagonal, inside):
    centre = zed[1:-1, 1:-1, 1:-1]
    beside = zed[2:, 1:-1, 1:-1] + zed[:-2, 1:-1, 1:-1]
    beside = beside + zed[1:-1, 2:, 1:-1] + zed[1:-1, :-2, 1:-1]
    beside = beside + zed[1:-1, 1:-1, 2:] + zed[1:-1, 1:-1, :-2]
    return ((6.0 + diagonal) * centre - beside) * inside


def inside_grid(shape, width):
    result = None
    for axis, dim in SIDES:
        length = shape[dim]
        place = lax.axis_index(axis) * length - width + jnp.arange(length + 2 * width, dtype=jnp.int32)
        line = ((place >= 0) & (place < lax.axis_size(axis) * length)).astype(jnp.float32)
        view = [1, 1, 1]
        view[dim] = length + 2 * width
        line = line.reshape(view)
        result = line if result is None else result * line
    return result


def interior(value, width):
    return value[width:-width, width:-width, width:-width]


def forward_table(count, basis):
    row_index = jnp.arange(PTS * count + 2 * RIM, dtype=jnp.int32)
    element = jnp.arange(count, dtype=jnp.int32)
    offset = jnp.arange(WIDE, dtype=jnp.int32)
    select = (
        row_index[:, None, None] == PTS * element[None, :, None] + offset[None, None, :]
    ).astype(jnp.float32)
    table = jnp.einsum("rcj,jm->rcm", select, basis, precision=PRECISE)
    return table.reshape(PTS * count + 2 * RIM, count * WIDE)


def backward_table(count, basis):
    same = jnp.eye(count, dtype=jnp.float32)
    table = jnp.einsum("cd,im->cmdi", same, basis[RIM : RIM + PTS], precision=PRECISE)
    return table.reshape(count * WIDE, count * PTS)


def schwarz_part(padded, basis_tables, eigenvalues):
    count_x = (padded.shape[0] - 2 * RIM) // PTS
    count_y = (padded.shape[1] - 2 * RIM) // PTS
    count_z = (padded.shape[2] - 2 * RIM) // PTS
    spectral = jnp.einsum(
        "pqr,rc->pqc", padded, forward_table(count_z, basis_tables[2]), precision=PRECISE
    )
    spectral = jnp.einsum(
        "pqc,pa->aqc", spectral, forward_table(count_x, basis_tables[0]), precision=PRECISE
    )
    spectral = jnp.einsum(
        "aqc,qb->abc", spectral, forward_table(count_y, basis_tables[1]), precision=PRECISE
    )
    denominator = (
        jnp.tile(eigenvalues[0], count_x)[:, None, None]
        + jnp.tile(eigenvalues[1], count_y)[None, :, None]
    )
    denominator = denominator + jnp.tile(eigenvalues[2], count_z)[None, None, :]
    spectral = spectral / denominator
    local_part = jnp.einsum(
        "abc,cr->abr", spectral, backward_table(count_z, basis_tables[2]), precision=PRECISE
    )
    local_part = jnp.einsum(
        "abr,ap->pbr", local_part, backward_table(count_x, basis_tables[0]), precision=PRECISE
    )
    local_part = jnp.einsum(
        "pbr,bq->pqr", local_part, backward_table(count_y, basis_tables[1]), precision=PRECISE
    )
    return local_part


def coarse_terms(field, blocks, selector):
    count_x = field.shape[0] // PTS
    count_y = field.shape[1] // PTS
    count_z = field.shape[2] // PTS
    cells = count_x * count_y * count_z
    means = jnp.mean(field.reshape(count_x, PTS, count_y, PTS, count_z, PTS), axis=(1, 3, 5))
    restricted = means.reshape(cells)
    terms = jnp.einsum("kpq,p->kq", blocks, restricted, precision=PRECISE)
    return jnp.einsum("kj,kq->jq", selector, terms, precision=PRECISE)


def coarse_apply(whole, blocks, selector, shape):
    count_x = shape[0] // PTS
    count_y = shape[1] // PTS
    count_z = shape[2] // PTS
    picked = jnp.dot(selector, whole, precision=PRECISE)
    coarse = jnp.einsum("kpq,kq->p", blocks, picked, precision=PRECISE)
    coarse = coarse.reshape(count_x, 1, count_y, 1, count_z, 1)
    spread = jnp.broadcast_to(coarse, (count_x, PTS, count_y, PTS, count_z, PTS))
    return spread.reshape(shape)


ALL = ("gx", "ga", "gz")


def butterfly(value, axes):
    for axis in axes:
        size = lax.axis_size(axis)
        if size & (size - 1):
            value = lax.psum(value, axis)
            continue
        step = 1
        while step < size:
            value = value + lax.ppermute(value, axis, [(i, i ^ step) for i in range(size)])
            step *= 2
    return value


def reduce_all(buffer, scalars):
    count = len(scalars)
    if buffer is None:
        total = butterfly(lax.optimization_barrier(jnp.stack(scalars)), ALL)
        return None, [total[i] for i in range(count)]
    payload = lax.optimization_barrier(jnp.concatenate([buffer.reshape(-1), jnp.stack(scalars)]))
    payload = butterfly(payload, ("ga", "gz"))
    size = payload.shape[0] - count
    total = butterfly(payload[size:], ("gx",))
    return payload[:size].reshape(buffer.shape), [total[i] for i in range(count)]


def body(right_side, diagonal, basis_tables, eigenvalues, coarse_blocks, coarse_columns):
    blocks = coarse_blocks.reshape(coarse_blocks.shape[3:])
    columns = coarse_columns.reshape(coarse_columns.shape[3])
    group = lax.axis_size(("ga", "gz"))
    selector = (columns[:, None] == jnp.arange(group, dtype=jnp.int32)[None, :]).astype(jnp.float32)
    shape = right_side.shape
    stacked = tuple((axis, dim + 1) for axis, dim in SIDES)
    wide_pair = padded_2(jnp.stack([diagonal, right_side]), stacked, RIM)
    wide_diagonal, wide_residual = wide_pair[0], wide_pair[1]
    inside = inside_grid(shape, RIM)

    solution = jnp.zeros_like(right_side)
    for restart in range(CYCLES):
        residual = interior(wide_residual, RIM)
        whole_r, (square,) = reduce_all(
            coarse_terms(residual, blocks, selector), [jnp.sum(residual * residual)]
        )
        initial_norm = jnp.sqrt(square)
        first_vector = residual / initial_norm
        first_zed = (
            schwarz_part(wide_residual, basis_tables, eigenvalues)
            + coarse_apply(whole_r, blocks, selector, shape)
        ) / initial_norm
        wide_first = operate_rim(padded_2(first_zed, SIDES, RIM + 1), wide_diagonal, inside)
        first_image = interior(wide_first, RIM)
        whole_w, (first_proj, image_square) = reduce_all(
            coarse_terms(first_image, blocks, selector),
            [jnp.sum(first_vector * first_image), jnp.sum(first_image * first_image)],
        )
        first_len = jnp.sqrt(image_square - first_proj * first_proj)
        image_zed = schwarz_part(wide_first, basis_tables, eigenvalues) + coarse_apply(
            whole_w, blocks, selector, shape
        )
        second_vector = (first_image - first_proj * first_vector) / first_len
        second_zed = (image_zed - first_proj * first_zed) / first_len
        wide_second = operate_rim(padded_2(second_zed, SIDES, RIM + 1), wide_diagonal, inside)
        second_image = interior(wide_second, RIM)
        _, (upper_proj, lower_proj, second_square) = reduce_all(
            None,
            [
                jnp.sum(first_vector * second_image),
                jnp.sum(second_vector * second_image),
                jnp.sum(second_image * second_image),
            ],
        )
        second_len = jnp.sqrt(second_square - upper_proj * upper_proj - lower_proj * lower_proj)
        gram_first = first_proj * first_proj + first_len * first_len
        gram_cross = first_proj * upper_proj + first_len * lower_proj
        gram_second = upper_proj * upper_proj + lower_proj * lower_proj + second_len * second_len
        target_first = initial_norm * first_proj
        target_second = initial_norm * upper_proj
        determinant = gram_first * gram_second - gram_cross * gram_cross
        weight_first = (gram_second * target_first - gram_cross * target_second) / determinant
        weight_second = (gram_first * target_second - gram_cross * target_first) / determinant
        solution = solution + weight_first * first_zed + weight_second * second_zed
        wide_residual = wide_residual - weight_first * wide_first - weight_second * wide_second
    return (solution, interior(wide_residual, RIM))


def solution(mesh):
    in_specs = (
        P("gx", "ga", "gz"),
        P("gx", "ga", "gz"),
        P(),
        P(),
        P("gx", "ga", "gz", None, None, None),
        P("gx", "ga", "gz", None),
    )
    out_specs = (P("gx", "ga", "gz"), P("gx", "ga", "gz"))
    return jax.shard_map(body, mesh=mesh, in_specs=in_specs, out_specs=out_specs, check_vma=False)
```

```python
import jax
import jax.numpy as jnp
from jax import lax
from jax.sharding import PartitionSpec as P

PTS = 8
RIM = 2
WIDE = 12
CYCLES = 2


PRECISE = lax.Precision.HIGHEST


def padded_2(value, sides, width):
    for axis, dim in sides:
        size, length = (lax.axis_size(axis), value.shape[dim])
        last = lax.slice_in_dim(value, length - width, length, axis=dim)
        leading = lax.slice_in_dim(value, 0, width, axis=dim)
        if size == 2:
            first = lax.axis_index(axis) == 0
            got = lax.ppermute(jnp.where(first, last, leading), axis, [(0, 1), (1, 0)])
            zero = jnp.zeros_like(got)
            before = jnp.where(first, zero, got)
            after = jnp.where(first, got, zero)
        else:
            up = [(i, (i + 1) % size) for i in range(size - 1)]
            down = [(j, i) for i, j in up]
            before = lax.ppermute(last, axis, up)
            after = lax.ppermute(leading, axis, down)
        value = jnp.concatenate([before, value, after], axis=dim)
    return value


SIDES = (("gx", 0), ("ga", 1), ("gz", 2))


def operate_rim(zed, diagonal, inside):
    centre = zed[1:-1, 1:-1, 1:-1]
    beside = zed[2:, 1:-1, 1:-1] + zed[:-2, 1:-1, 1:-1]
    beside = beside + zed[1:-1, 2:, 1:-1] + zed[1:-1, :-2, 1:-1]
    beside = beside + zed[1:-1, 1:-1, 2:] + zed[1:-1, 1:-1, :-2]
    return ((6.0 + diagonal) * centre - beside) * inside


def inside_grid(shape, width):
    result = None
    for axis, dim in SIDES:
        length = shape[dim]
        place = lax.axis_index(axis) * length - width + jnp.arange(length + 2 * width, dtype=jnp.int32)
        line = ((place >= 0) & (place < lax.axis_size(axis) * length)).astype(jnp.float32)
        view = [1, 1, 1]
        view[dim] = length + 2 * width
        line = line.reshape(view)
        result = line if result is None else result * line
    return result


def interior(value, width):
    return value[width:-width, width:-width, width:-width]


def forward_table(count, basis):
    row_index = jnp.arange(PTS * count + 2 * RIM, dtype=jnp.int32)
    element = jnp.arange(count, dtype=jnp.int32)
    offset = jnp.arange(WIDE, dtype=jnp.int32)
    select = (
        row_index[:, None, None] == PTS * element[None, :, None] + offset[None, None, :]
    ).astype(jnp.float32)
    table = jnp.einsum("rcj,jm->rcm", select, basis, precision=PRECISE)
    return table.reshape(PTS * count + 2 * RIM, count * WIDE)


def backward_table(count, basis):
    same = jnp.eye(count, dtype=jnp.float32)
    table = jnp.einsum("cd,im->cmdi", same, basis[RIM : RIM + PTS], precision=PRECISE)
    return table.reshape(count * WIDE, count * PTS)


def schwarz_part(padded, basis_tables, eigenvalues):
    count_x = (padded.shape[0] - 2 * RIM) // PTS
    count_y = (padded.shape[1] - 2 * RIM) // PTS
    count_z = (padded.shape[2] - 2 * RIM) // PTS
    spectral = jnp.einsum(
        "pqr,rc->pqc", padded, forward_table(count_z, basis_tables[2]), precision=PRECISE
    )
    spectral = jnp.einsum(
        "pqc,pa->aqc", spectral, forward_table(count_x, basis_tables[0]), precision=PRECISE
    )
    spectral = jnp.einsum(
        "aqc,qb->abc", spectral, forward_table(count_y, basis_tables[1]), precision=PRECISE
    )
    denominator = (
        jnp.tile(eigenvalues[0], count_x)[:, None, None]
        + jnp.tile(eigenvalues[1], count_y)[None, :, None]
    )
    denominator = denominator + jnp.tile(eigenvalues[2], count_z)[None, None, :]
    spectral = spectral / denominator
    local_part = jnp.einsum(
        "abc,cr->abr", spectral, backward_table(count_z, basis_tables[2]), precision=PRECISE
    )
    local_part = jnp.einsum(
        "abr,ap->pbr", local_part, backward_table(count_x, basis_tables[0]), precision=PRECISE
    )
    local_part = jnp.einsum(
        "pbr,bq->pqr", local_part, backward_table(count_y, basis_tables[1]), precision=PRECISE
    )
    return local_part


def coarse_terms(field, blocks, selector):
    count_x = field.shape[0] // PTS
    count_y = field.shape[1] // PTS
    count_z = field.shape[2] // PTS
    cells = count_x * count_y * count_z
    means = jnp.mean(field.reshape(count_x, PTS, count_y, PTS, count_z, PTS), axis=(1, 3, 5))
    restricted = means.reshape(cells)
    terms = jnp.einsum("kpq,p->kq", blocks, restricted, precision=PRECISE)
    return jnp.einsum("kj,kq->jq", selector, terms, precision=PRECISE)


def element_table(blocks, columns, shape):
    count = blocks.shape[0]
    grid = (shape[0] // PTS, shape[1] // PTS, shape[2] // PTS)
    rows = jnp.transpose(blocks, (1, 0, 2)).reshape(grid + (count * blocks.shape[2],))
    cols = jnp.broadcast_to(columns.astype(jnp.float32), grid + (count,))
    return jnp.concatenate([rows, cols], axis=-1)


def coarse_rim(wholes, table, count, group):
    lo, whole, hi = wholes
    grid = table.shape[:3]
    width = (table.shape[3] - count) // count
    rows = table[..., : count * width].reshape(grid + (count, width))
    cols = table[..., count * width :]
    onehot = (cols[..., None] == jnp.arange(group, dtype=jnp.float32)).astype(jnp.float32)
    stacked = jnp.stack([lo] + [whole] * (grid[0] - 2) + [hi])
    picked = jnp.einsum("abckg,agq->abckq", onehot, stacked, precision=PRECISE)
    return jnp.sum(rows * picked, axis=(3, 4))


def spread_rim(values, width, shape):
    def table(length, count):
        point = jnp.arange(length + 2 * width, dtype=jnp.int32) - width + PTS
        element = jnp.arange(count, dtype=jnp.int32)
        return (point[:, None] // PTS == element[None, :]).astype(jnp.float32)

    grid = values.shape
    out = jnp.einsum("abc,rc->abr", values, table(shape[2], grid[2]), precision=PRECISE)
    out = jnp.einsum("abr,pa->pbr", out, table(shape[0], grid[0]), precision=PRECISE)
    return jnp.einsum("pbr,qb->pqr", out, table(shape[1], grid[1]), precision=PRECISE)


ALL = ("gx", "ga", "gz")


def butterfly(value, axes):
    for axis in axes:
        size = lax.axis_size(axis)
        if size & (size - 1):
            value = lax.psum(value, axis)
            continue
        step = 1
        while step < size:
            value = value + lax.ppermute(value, axis, [(i, i ^ step) for i in range(size)])
            step *= 2
    return value


def reduce_scalars(scalars):
    total = butterfly(lax.optimization_barrier(jnp.stack(scalars)), ALL)
    return [total[i] for i in range(len(scalars))]


def reduce_coarse(buffer, scalars):
    count = len(scalars)
    payload = lax.optimization_barrier(jnp.concatenate([buffer.reshape(-1), jnp.stack(scalars)]))
    payload = butterfly(payload, ("ga", "gz"))
    size = payload.shape[0] - count
    whole = payload[:size].reshape(buffer.shape)
    if lax.axis_size("gx") == 2:
        got = lax.ppermute(payload, "gx", [(0, 1), (1, 0)])
        total = payload[size:] + got[size:]
        other = got[:size].reshape(buffer.shape)
        first = lax.axis_index("gx") == 0
        zero = jnp.zeros_like(other)
        lo, hi = jnp.where(first, zero, other), jnp.where(first, other, zero)
    else:
        total = butterfly(payload[size:], ("gx",))
        gx = lax.axis_size("gx")
        up = [(i, i + 1) for i in range(gx - 1)]
        lo = lax.ppermute(whole, "gx", up)
        hi = lax.ppermute(whole, "gx", [(j, i) for i, j in up])
    return (lo, whole, hi), [total[i] for i in range(count)]


def body(right_side, diagonal, basis_tables, eigenvalues, coarse_blocks, coarse_columns):
    blocks = coarse_blocks.reshape(coarse_blocks.shape[3:])
    columns = coarse_columns.reshape(coarse_columns.shape[3])
    count = blocks.shape[0]
    group = lax.axis_size(("ga", "gz"))
    selector = (columns[:, None] == jnp.arange(group, dtype=jnp.int32)[None, :]).astype(jnp.float32)
    shape = right_side.shape
    stacked = tuple((axis, dim + 1) for axis, dim in SIDES)
    wide_pair = padded_2(jnp.stack([diagonal, right_side]), stacked, RIM)
    wide_diagonal, wide_residual = wide_pair[0], wide_pair[1]
    inside = inside_grid(shape, RIM)
    table = padded_2(element_table(blocks, columns, shape), SIDES, 1)

    def precondition_rim(wide_field, field):
        local = schwarz_part(wide_field, basis_tables, eigenvalues)
        return padded_2(local, SIDES, RIM + 1), coarse_terms(field, blocks, selector)

    def coarse_on_rim(wholes):
        return spread_rim(coarse_rim(wholes, table, count, group), RIM + 1, shape)

    solution = jnp.zeros_like(right_side)
    for restart in range(CYCLES):
        residual = interior(wide_residual, RIM)
        wide_local, terms = precondition_rim(wide_residual, residual)
        wholes, (square,) = reduce_coarse(terms, [jnp.sum(residual * residual)])
        initial_norm = jnp.sqrt(square)
        first_vector = residual / initial_norm
        wide_zed = (wide_local + coarse_on_rim(wholes)) / initial_norm
        first_zed = interior(wide_zed, RIM + 1)
        wide_first = operate_rim(wide_zed, wide_diagonal, inside)
        first_image = interior(wide_first, RIM)
        wide_local, terms = precondition_rim(wide_first, first_image)
        wholes, (first_proj, image_square) = reduce_coarse(
            terms, [jnp.sum(first_vector * first_image), jnp.sum(first_image * first_image)]
        )
        first_len = jnp.sqrt(image_square - first_proj * first_proj)
        second_vector = (first_image - first_proj * first_vector) / first_len
        wide_second_zed = (wide_local + coarse_on_rim(wholes) - first_proj * wide_zed) / first_len
        second_zed = interior(wide_second_zed, RIM + 1)
        wide_second = operate_rim(wide_second_zed, wide_diagonal, inside)
        second_image = interior(wide_second, RIM)
        upper_proj, lower_proj, second_square = reduce_scalars(
            [
                jnp.sum(first_vector * second_image),
                jnp.sum(second_vector * second_image),
                jnp.sum(second_image * second_image),
            ]
        )
        second_len = jnp.sqrt(second_square - upper_proj * upper_proj - lower_proj * lower_proj)
        gram_first = first_proj * first_proj + first_len * first_len
        gram_cross = first_proj * upper_proj + first_len * lower_proj
        gram_second = upper_proj * upper_proj + lower_proj * lower_proj + second_len * second_len
        target_first = initial_norm * first_proj
        target_second = initial_norm * upper_proj
        determinant = gram_first * gram_second - gram_cross * gram_cross
        weight_first = (gram_second * target_first - gram_cross * target_second) / determinant
        weight_second = (gram_first * target_second - gram_cross * target_first) / determinant
        solution = solution + weight_first * first_zed + weight_second * second_zed
        wide_residual = wide_residual - weight_first * wide_first - weight_second * wide_second
    return (solution, interior(wide_residual, RIM))


def solution(mesh):
    in_specs = (
        P("gx", "ga", "gz"),
        P("gx", "ga", "gz"),
        P(),
        P(),
        P("gx", "ga", "gz", None, None, None),
        P("gx", "ga", "gz", None),
    )
    out_specs = (P("gx", "ga", "gz"), P("gx", "ga", "gz"))
    return jax.shard_map(body, mesh=mesh, in_specs=in_specs, out_specs=out_specs, check_vma=False)
```

```python
import jax
import jax.numpy as jnp
from jax import lax
from jax.sharding import PartitionSpec as P

PTS = 8
RIM = 2
WIDE = 12
CYCLES = 2


PRECISE = lax.Precision.HIGHEST


def padded_2(value, sides, width):
    for axis, dim in sides:
        size, length = (lax.axis_size(axis), value.shape[dim])
        last = lax.slice_in_dim(value, length - width, length, axis=dim)
        leading = lax.slice_in_dim(value, 0, width, axis=dim)
        if size == 2:
            first = lax.axis_index(axis) == 0
            got = lax.ppermute(jnp.where(first, last, leading), axis, [(0, 1), (1, 0)])
            zero = jnp.zeros_like(got)
            before = jnp.where(first, zero, got)
            after = jnp.where(first, got, zero)
        else:
            up = [(i, (i + 1) % size) for i in range(size - 1)]
            down = [(j, i) for i, j in up]
            before = lax.ppermute(last, axis, up)
            after = lax.ppermute(leading, axis, down)
        value = jnp.concatenate([before, value, after], axis=dim)
    return value


SIDES = (("gx", 0), ("ga", 1), ("gz", 2))


def operate_rim(zed, diagonal, inside):
    centre = zed[1:-1, 1:-1, 1:-1]
    beside = zed[2:, 1:-1, 1:-1] + zed[:-2, 1:-1, 1:-1]
    beside = beside + zed[1:-1, 2:, 1:-1] + zed[1:-1, :-2, 1:-1]
    beside = beside + zed[1:-1, 1:-1, 2:] + zed[1:-1, 1:-1, :-2]
    return ((6.0 + diagonal) * centre - beside) * inside


def inside_grid(shape, width):
    result = None
    for axis, dim in SIDES:
        length = shape[dim]
        place = lax.axis_index(axis) * length - width + jnp.arange(length + 2 * width, dtype=jnp.int32)
        line = ((place >= 0) & (place < lax.axis_size(axis) * length)).astype(jnp.float32)
        view = [1, 1, 1]
        view[dim] = length + 2 * width
        line = line.reshape(view)
        result = line if result is None else result * line
    return result


def interior(value, width):
    return value[width:-width, width:-width, width:-width]


def forward_table(count, basis):
    row_index = jnp.arange(PTS * count + 2 * RIM, dtype=jnp.int32)
    element = jnp.arange(count, dtype=jnp.int32)
    offset = jnp.arange(WIDE, dtype=jnp.int32)
    select = (
        row_index[:, None, None] == PTS * element[None, :, None] + offset[None, None, :]
    ).astype(jnp.float32)
    table = jnp.einsum("rcj,jm->rcm", select, basis, precision=PRECISE)
    return table.reshape(PTS * count + 2 * RIM, count * WIDE)


def backward_table(count, basis):
    same = jnp.eye(count, dtype=jnp.float32)
    table = jnp.einsum("cd,im->cmdi", same, basis[RIM : RIM + PTS], precision=PRECISE)
    return table.reshape(count * WIDE, count * PTS)


def schwarz_part(padded, basis_tables, eigenvalues):
    count_x = (padded.shape[0] - 2 * RIM) // PTS
    count_y = (padded.shape[1] - 2 * RIM) // PTS
    count_z = (padded.shape[2] - 2 * RIM) // PTS
    spectral = jnp.einsum(
        "pqr,rc->pqc", padded, forward_table(count_z, basis_tables[2]), precision=PRECISE
    )
    spectral = jnp.einsum(
        "pqc,pa->aqc", spectral, forward_table(count_x, basis_tables[0]), precision=PRECISE
    )
    spectral = jnp.einsum(
        "aqc,qb->abc", spectral, forward_table(count_y, basis_tables[1]), precision=PRECISE
    )
    denominator = (
        jnp.tile(eigenvalues[0], count_x)[:, None, None]
        + jnp.tile(eigenvalues[1], count_y)[None, :, None]
    )
    denominator = denominator + jnp.tile(eigenvalues[2], count_z)[None, None, :]
    spectral = spectral / denominator
    local_part = jnp.einsum(
        "abc,cr->abr", spectral, backward_table(count_z, basis_tables[2]), precision=PRECISE
    )
    local_part = jnp.einsum(
        "abr,ap->pbr", local_part, backward_table(count_x, basis_tables[0]), precision=PRECISE
    )
    local_part = jnp.einsum(
        "pbr,bq->pqr", local_part, backward_table(count_y, basis_tables[1]), precision=PRECISE
    )
    return local_part


def coarse_terms(field, blocks, selector):
    count_x = field.shape[0] // PTS
    count_y = field.shape[1] // PTS
    count_z = field.shape[2] // PTS
    cells = count_x * count_y * count_z
    point = jnp.arange(field.shape[2], dtype=jnp.int32)
    along = (point[:, None] // PTS == jnp.arange(count_z, dtype=jnp.int32)[None, :]).astype(jnp.float32)
    sums = jnp.einsum("pqr,rc->pqc", field, along, precision=PRECISE)
    sums = jnp.sum(sums.reshape(count_x, PTS, count_y, PTS, count_z), axis=(1, 3))
    restricted = sums.reshape(cells) * (1.0 / PTS**3)
    terms = jnp.einsum("kpq,p->kq", blocks, restricted, precision=PRECISE)
    return jnp.einsum("kj,kq->jq", selector, terms, precision=PRECISE)


def element_table(blocks, columns, shape):
    count = blocks.shape[0]
    grid = (shape[0] // PTS, shape[1] // PTS, shape[2] // PTS)
    rows = jnp.transpose(blocks, (1, 0, 2)).reshape(grid + (count * blocks.shape[2],))
    cols = jnp.broadcast_to(columns.astype(jnp.float32), grid + (count,))
    return jnp.concatenate([rows, cols], axis=-1)


def coarse_rim(wholes, table, count, group):
    lo, whole, hi = wholes
    grid = table.shape[:3]
    width = (table.shape[3] - count) // count
    rows = table[..., : count * width].reshape(grid + (count, width))
    cols = table[..., count * width :]
    onehot = (cols[..., None] == jnp.arange(group, dtype=jnp.float32)).astype(jnp.float32)
    stacked = jnp.stack([lo] + [whole] * (grid[0] - 2) + [hi])
    picked = jnp.einsum("abckg,agq->abckq", onehot, stacked, precision=PRECISE)
    return jnp.sum(rows * picked, axis=(3, 4))


def spread_rim(values, width, shape):
    def table(length, count):
        point = jnp.arange(length + 2 * width, dtype=jnp.int32) - width + PTS
        element = jnp.arange(count, dtype=jnp.int32)
        return (point[:, None] // PTS == element[None, :]).astype(jnp.float32)

    grid = values.shape
    out = jnp.einsum("abc,rc->abr", values, table(shape[2], grid[2]), precision=PRECISE)
    out = jnp.einsum("abr,pa->pbr", out, table(shape[0], grid[0]), precision=PRECISE)
    return jnp.einsum("pbr,qb->pqr", out, table(shape[1], grid[1]), precision=PRECISE)


ALL = ("gx", "ga", "gz")


def butterfly(value, axes):
    for axis in axes:
        size = lax.axis_size(axis)
        if size & (size - 1):
            value = lax.psum(value, axis)
            continue
        step = 1
        while step < size:
            value = value + lax.ppermute(value, axis, [(i, i ^ step) for i in range(size)])
            step *= 2
    return value


def reduce_scalars(scalars):
    total = butterfly(lax.optimization_barrier(jnp.stack(scalars)), ALL)
    return [total[i] for i in range(len(scalars))]


def reduce_coarse(buffer, scalars):
    count = len(scalars)
    payload = lax.optimization_barrier(jnp.concatenate([buffer.reshape(-1), jnp.stack(scalars)]))
    payload = butterfly(payload, ("ga", "gz"))
    size = payload.shape[0] - count
    whole = payload[:size].reshape(buffer.shape)
    if lax.axis_size("gx") == 2:
        got = lax.ppermute(payload, "gx", [(0, 1), (1, 0)])
        total = payload[size:] + got[size:]
        other = got[:size].reshape(buffer.shape)
        first = lax.axis_index("gx") == 0
        zero = jnp.zeros_like(other)
        lo, hi = jnp.where(first, zero, other), jnp.where(first, other, zero)
    else:
        total = butterfly(payload[size:], ("gx",))
        gx = lax.axis_size("gx")
        up = [(i, i + 1) for i in range(gx - 1)]
        lo = lax.ppermute(whole, "gx", up)
        hi = lax.ppermute(whole, "gx", [(j, i) for i, j in up])
    return (lo, whole, hi), [total[i] for i in range(count)]


def body(right_side, diagonal, basis_tables, eigenvalues, coarse_blocks, coarse_columns):
    blocks = coarse_blocks.reshape(coarse_blocks.shape[3:])
    columns = coarse_columns.reshape(coarse_columns.shape[3])
    count = blocks.shape[0]
    group = lax.axis_size(("ga", "gz"))
    selector = (columns[:, None] == jnp.arange(group, dtype=jnp.int32)[None, :]).astype(jnp.float32)
    shape = right_side.shape
    stacked = tuple((axis, dim + 1) for axis, dim in SIDES)
    wide_pair = padded_2(jnp.stack([diagonal, right_side]), stacked, RIM)
    wide_diagonal, wide_residual = wide_pair[0], wide_pair[1]
    inside = inside_grid(shape, RIM)
    table = padded_2(element_table(blocks, columns, shape), SIDES, 1)

    def precondition_rim(wide_field, field):
        local = schwarz_part(wide_field, basis_tables, eigenvalues)
        return padded_2(local, SIDES, RIM + 1), coarse_terms(field, blocks, selector)

    def coarse_on_rim(wholes):
        return spread_rim(coarse_rim(wholes, table, count, group), RIM + 1, shape)

    solution = jnp.zeros_like(right_side)
    for restart in range(CYCLES):
        residual = interior(wide_residual, RIM)
        wide_local, terms = precondition_rim(wide_residual, residual)
        wholes, (square,) = reduce_coarse(terms, [jnp.sum(residual * residual)])
        initial_norm = jnp.sqrt(square)
        first_vector = residual / initial_norm
        wide_zed = (wide_local + coarse_on_rim(wholes)) / initial_norm
        first_zed = interior(wide_zed, RIM + 1)
        wide_first = operate_rim(wide_zed, wide_diagonal, inside)
        first_image = interior(wide_first, RIM)
        wide_local, terms = precondition_rim(wide_first, first_image)
        wholes, (first_proj, image_square) = reduce_coarse(
            terms, [jnp.sum(first_vector * first_image), jnp.sum(first_image * first_image)]
        )
        first_len = jnp.sqrt(image_square - first_proj * first_proj)
        second_vector = (first_image - first_proj * first_vector) / first_len
        wide_second_zed = (wide_local + coarse_on_rim(wholes) - first_proj * wide_zed) / first_len
        second_zed = interior(wide_second_zed, RIM + 1)
        wide_second = operate_rim(wide_second_zed, wide_diagonal, inside)
        second_image = interior(wide_second, RIM)
        upper_proj, lower_proj, second_square = reduce_scalars(
            [
                jnp.sum(first_vector * second_image),
                jnp.sum(second_vector * second_image),
                jnp.sum(second_image * second_image),
            ]
        )
        second_len = jnp.sqrt(second_square - upper_proj * upper_proj - lower_proj * lower_proj)
        gram_first = first_proj * first_proj + first_len * first_len
        gram_cross = first_proj * upper_proj + first_len * lower_proj
        gram_second = upper_proj * upper_proj + lower_proj * lower_proj + second_len * second_len
        target_first = initial_norm * first_proj
        target_second = initial_norm * upper_proj
        determinant = gram_first * gram_second - gram_cross * gram_cross
        weight_first = (gram_second * target_first - gram_cross * target_second) / determinant
        weight_second = (gram_first * target_second - gram_cross * target_first) / determinant
        solution = solution + weight_first * first_zed + weight_second * second_zed
        wide_residual = wide_residual - weight_first * wide_first - weight_second * wide_second
    return (solution, interior(wide_residual, RIM))


def solution(mesh):
    in_specs = (
        P("gx", "ga", "gz"),
        P("gx", "ga", "gz"),
        P(),
        P(),
        P("gx", "ga", "gz", None, None, None),
        P("gx", "ga", "gz", None),
    )
    out_specs = (P("gx", "ga", "gz"), P("gx", "ga", "gz"))
    return jax.shard_map(body, mesh=mesh, in_specs=in_specs, out_specs=out_specs, check_vma=False)
```

```python
import functools

import jax
import jax.numpy as jnp
from jax import lax
from jax.sharding import PartitionSpec as P

PTS = 8
RIM = 2
WIDE = 12
CYCLES = 2


PRECISE = lax.Precision.HIGHEST


def pad_side(value, axis, dim, width):
    size, length = (lax.axis_size(axis), value.shape[dim])
    last = lax.slice_in_dim(value, length - width, length, axis=dim)
    leading = lax.slice_in_dim(value, 0, width, axis=dim)
    if size == 2:
        first = lax.axis_index(axis) == 0
        got = lax.ppermute(jnp.where(first, last, leading), axis, [(0, 1), (1, 0)])
        zero = jnp.zeros_like(got)
        before = jnp.where(first, zero, got)
        after = jnp.where(first, got, zero)
    else:
        up = [(i, (i + 1) % size) for i in range(size - 1)]
        down = [(j, i) for i, j in up]
        before = lax.ppermute(last, axis, up)
        after = lax.ppermute(leading, axis, down)
    return jnp.concatenate([before, value, after], axis=dim)


def padded_2(value, sides, width):
    for axis, dim in sides:
        value = pad_side(value, axis, dim, width)
    return value


SIDES = (("gx", 0), ("ga", 1), ("gz", 2))


def operate_rim(zed, diagonal, inside):
    centre = zed[1:-1, 1:-1, 1:-1]
    beside = zed[2:, 1:-1, 1:-1] + zed[:-2, 1:-1, 1:-1]
    beside = beside + zed[1:-1, 2:, 1:-1] + zed[1:-1, :-2, 1:-1]
    beside = beside + zed[1:-1, 1:-1, 2:] + zed[1:-1, 1:-1, :-2]
    return ((6.0 + diagonal) * centre - beside) * inside


def inside_grid(shape, width):
    result = None
    for axis, dim in SIDES:
        length = shape[dim]
        place = lax.axis_index(axis) * length - width + jnp.arange(length + 2 * width, dtype=jnp.int32)
        line = ((place >= 0) & (place < lax.axis_size(axis) * length)).astype(jnp.float32)
        view = [1, 1, 1]
        view[dim] = length + 2 * width
        line = line.reshape(view)
        result = line if result is None else result * line
    return result


def interior(value, width):
    return value[width:-width, width:-width, width:-width]


def forward_table(count, basis):
    row_index = jnp.arange(PTS * count + 2 * RIM, dtype=jnp.int32)
    element = jnp.arange(count, dtype=jnp.int32)
    offset = jnp.arange(WIDE, dtype=jnp.int32)
    select = (
        row_index[:, None, None] == PTS * element[None, :, None] + offset[None, None, :]
    ).astype(jnp.float32)
    table = jnp.einsum("rcj,jm->rcm", select, basis, precision=PRECISE)
    return table.reshape(PTS * count + 2 * RIM, count * WIDE)


def backward_table(count, basis):
    same = jnp.eye(count, dtype=jnp.float32)
    table = jnp.einsum("cd,im->cmdi", same, basis[RIM : RIM + PTS], precision=PRECISE)
    return table.reshape(count * WIDE, count * PTS)


def schwarz_part(padded, basis_tables, eigenvalues):
    count_x = (padded.shape[0] - 2 * RIM) // PTS
    count_y = (padded.shape[1] - 2 * RIM) // PTS
    count_z = (padded.shape[2] - 2 * RIM) // PTS
    spectral = jnp.einsum(
        "pqr,rc->pqc", padded, forward_table(count_z, basis_tables[2]), precision=PRECISE
    )
    spectral = jnp.einsum(
        "pqc,pa->aqc", spectral, forward_table(count_x, basis_tables[0]), precision=PRECISE
    )
    spectral = jnp.einsum(
        "aqc,qb->abc", spectral, forward_table(count_y, basis_tables[1]), precision=PRECISE
    )
    denominator = (
        jnp.tile(eigenvalues[0], count_x)[:, None, None]
        + jnp.tile(eigenvalues[1], count_y)[None, :, None]
    )
    denominator = denominator + jnp.tile(eigenvalues[2], count_z)[None, None, :]
    spectral = spectral / denominator
    local_part = jnp.einsum(
        "abc,cr->abr", spectral, backward_table(count_z, basis_tables[2]), precision=PRECISE
    )
    local_part = jnp.einsum(
        "abr,ap->pbr", local_part, backward_table(count_x, basis_tables[0]), precision=PRECISE
    )
    local_part = jnp.einsum(
        "pbr,bq->pqr", local_part, backward_table(count_y, basis_tables[1]), precision=PRECISE
    )
    return local_part


def coarse_terms(field, blocks, selector):
    count_x = field.shape[0] // PTS
    count_y = field.shape[1] // PTS
    count_z = field.shape[2] // PTS
    cells = count_x * count_y * count_z
    point = jnp.arange(field.shape[2], dtype=jnp.int32)
    along = (point[:, None] // PTS == jnp.arange(count_z, dtype=jnp.int32)[None, :]).astype(jnp.float32)
    sums = jnp.einsum("pqr,rc->pqc", field, along, precision=PRECISE)
    sums = jnp.sum(sums.reshape(count_x, PTS, count_y, PTS, count_z), axis=(1, 3))
    restricted = sums.reshape(cells) * (1.0 / PTS**3)
    terms = jnp.einsum("kpq,p->kq", blocks, restricted, precision=PRECISE)
    return jnp.einsum("kj,kq->jq", selector, terms, precision=PRECISE)


def element_table(blocks, columns, shape):
    count = blocks.shape[0]
    grid = (shape[0] // PTS, shape[1] // PTS, shape[2] // PTS)
    rows = jnp.transpose(blocks, (1, 0, 2)).reshape(grid + (count * blocks.shape[2],))
    cols = jnp.broadcast_to(columns.astype(jnp.float32), grid + (count,))
    return jnp.concatenate([rows, cols], axis=-1)


def coarse_rim(wholes, table, count, group):
    lo, whole, hi = wholes
    grid = table.shape[:3]
    width = (table.shape[3] - count) // count
    rows = table[..., : count * width].reshape(grid + (count, width))
    cols = table[..., count * width :]
    onehot = (cols[..., None] == jnp.arange(group, dtype=jnp.float32)).astype(jnp.float32)
    stacked = jnp.stack([lo] + [whole] * (grid[0] - 2) + [hi])
    picked = jnp.einsum("abckg,agq->abckq", onehot, stacked, precision=PRECISE)
    return jnp.sum(rows * picked, axis=(3, 4))


def spread_rim(values, width, shape):
    def table(length, count):
        point = jnp.arange(length + 2 * width, dtype=jnp.int32) - width + PTS
        element = jnp.arange(count, dtype=jnp.int32)
        return (point[:, None] // PTS == element[None, :]).astype(jnp.float32)

    grid = values.shape
    out = jnp.einsum("abc,rc->abr", values, table(shape[2], grid[2]), precision=PRECISE)
    out = jnp.einsum("abr,pa->pbr", out, table(shape[0], grid[0]), precision=PRECISE)
    return jnp.einsum("pbr,qb->pqr", out, table(shape[1], grid[1]), precision=PRECISE)


ALL = ("gx", "ga", "gz")


def butterfly_stages(axes):
    stages = []
    for axis in axes:
        size = lax.axis_size(axis)
        if size & (size - 1):
            stages.append(lambda value, axis=axis: lax.psum(value, axis))
            continue
        step = 1
        while step < size:
            pairs = [(i, i ^ step) for i in range(size)]
            stages.append(lambda value, axis=axis, pairs=pairs: value + lax.ppermute(value, axis, pairs))
            step *= 2
    return stages


def butterfly(value, axes):
    for stage in butterfly_stages(axes):
        value = stage(value)
    return value


def reduce_scalars(scalars):
    total = butterfly(lax.optimization_barrier(jnp.stack(scalars)), ALL)
    return [total[i] for i in range(len(scalars))]


HALO_ORDER = (("ga", 1), ("gz", 2), ("gx", 0))


def reduce_coarse(local, buffer, scalars):
    count = len(scalars)
    payload = jnp.concatenate([buffer.reshape(-1), jnp.stack(scalars)])
    halo = [functools.partial(pad_side, axis=axis, dim=dim, width=RIM + 1) for axis, dim in HALO_ORDER]
    sums = butterfly_stages(("ga", "gz"))
    local, payload = lax.optimization_barrier((local, payload))
    for index in range(max(len(halo), len(sums))):
        if index < len(halo):
            local = halo[index](local)
        if index < len(sums):
            payload = sums[index](payload)
        local, payload = lax.optimization_barrier((local, payload))
    size = payload.shape[0] - count
    whole = payload[:size].reshape(buffer.shape)
    if lax.axis_size("gx") == 2:
        got = lax.ppermute(payload, "gx", [(0, 1), (1, 0)])
        total = payload[size:] + got[size:]
        other = got[:size].reshape(buffer.shape)
        first = lax.axis_index("gx") == 0
        zero = jnp.zeros_like(other)
        lo, hi = jnp.where(first, zero, other), jnp.where(first, other, zero)
    else:
        total = butterfly(payload[size:], ("gx",))
        gx = lax.axis_size("gx")
        up = [(i, i + 1) for i in range(gx - 1)]
        lo = lax.ppermute(whole, "gx", up)
        hi = lax.ppermute(whole, "gx", [(j, i) for i, j in up])
    return local, (lo, whole, hi), [total[i] for i in range(count)]


def body(right_side, diagonal, basis_tables, eigenvalues, coarse_blocks, coarse_columns):
    blocks = coarse_blocks.reshape(coarse_blocks.shape[3:])
    columns = coarse_columns.reshape(coarse_columns.shape[3])
    count = blocks.shape[0]
    group = lax.axis_size(("ga", "gz"))
    selector = (columns[:, None] == jnp.arange(group, dtype=jnp.int32)[None, :]).astype(jnp.float32)
    shape = right_side.shape
    stacked = tuple((axis, dim + 1) for axis, dim in SIDES)
    wide_pair = padded_2(jnp.stack([diagonal, right_side]), stacked, RIM)
    wide_diagonal, wide_residual = wide_pair[0], wide_pair[1]
    inside = inside_grid(shape, RIM)
    table = padded_2(element_table(blocks, columns, shape), SIDES, 1)

    def precondition_rim(wide_field, field):
        local = schwarz_part(wide_field, basis_tables, eigenvalues)
        return local, coarse_terms(field, blocks, selector)

    def coarse_on_rim(wholes):
        return spread_rim(coarse_rim(wholes, table, count, group), RIM + 1, shape)

    solution = jnp.zeros_like(right_side)
    for restart in range(CYCLES):
        residual = interior(wide_residual, RIM)
        wide_local, terms = precondition_rim(wide_residual, residual)
        wide_local, wholes, (square,) = reduce_coarse(wide_local, terms, [jnp.sum(residual * residual)])
        initial_norm = jnp.sqrt(square)
        first_vector = residual / initial_norm
        wide_zed = (wide_local + coarse_on_rim(wholes)) / initial_norm
        first_zed = interior(wide_zed, RIM + 1)
        wide_first = operate_rim(wide_zed, wide_diagonal, inside)
        first_image = interior(wide_first, RIM)
        wide_local, terms = precondition_rim(wide_first, first_image)
        wide_local, wholes, (first_proj, image_square) = reduce_coarse(
            wide_local, terms, [jnp.sum(first_vector * first_image), jnp.sum(first_image * first_image)]
        )
        first_len = jnp.sqrt(image_square - first_proj * first_proj)
        second_vector = (first_image - first_proj * first_vector) / first_len
        wide_second_zed = (wide_local + coarse_on_rim(wholes) - first_proj * wide_zed) / first_len
        second_zed = interior(wide_second_zed, RIM + 1)
        wide_second = operate_rim(wide_second_zed, wide_diagonal, inside)
        second_image = interior(wide_second, RIM)
        upper_proj, lower_proj, second_square = reduce_scalars(
            [
                jnp.sum(first_vector * second_image),
                jnp.sum(second_vector * second_image),
                jnp.sum(second_image * second_image),
            ]
        )
        second_len = jnp.sqrt(second_square - upper_proj * upper_proj - lower_proj * lower_proj)
        gram_first = first_proj * first_proj + first_len * first_len
        gram_cross = first_proj * upper_proj + first_len * lower_proj
        gram_second = upper_proj * upper_proj + lower_proj * lower_proj + second_len * second_len
        target_first = initial_norm * first_proj
        target_second = initial_norm * upper_proj
        determinant = gram_first * gram_second - gram_cross * gram_cross
        weight_first = (gram_second * target_first - gram_cross * target_second) / determinant
        weight_second = (gram_first * target_second - gram_cross * target_first) / determinant
        solution = solution + weight_first * first_zed + weight_second * second_zed
        wide_residual = wide_residual - weight_first * wide_first - weight_second * wide_second
    return (solution, interior(wide_residual, RIM))


def solution(mesh):
    in_specs = (
        P("gx", "ga", "gz"),
        P("gx", "ga", "gz"),
        P(),
        P(),
        P("gx", "ga", "gz", None, None, None),
        P("gx", "ga", "gz", None),
    )
    out_specs = (P("gx", "ga", "gz"), P("gx", "ga", "gz"))
    return jax.shard_map(body, mesh=mesh, in_specs=in_specs, out_specs=out_specs, check_vma=False)
```

```python
import functools

import jax
import jax.numpy as jnp
from jax import lax
from jax.sharding import PartitionSpec as P

PTS = 8
RIM = 2
WIDE = 12
CYCLES = 2


PRECISE = lax.Precision.HIGHEST


def pad_side(value, axis, dim, width):
    size, length = (lax.axis_size(axis), value.shape[dim])
    last = lax.slice_in_dim(value, length - width, length, axis=dim)
    leading = lax.slice_in_dim(value, 0, width, axis=dim)
    if size == 2:
        first = lax.axis_index(axis) == 0
        got = lax.ppermute(jnp.where(first, last, leading), axis, [(0, 1), (1, 0)])
        zero = jnp.zeros_like(got)
        before = jnp.where(first, zero, got)
        after = jnp.where(first, got, zero)
    else:
        up = [(i, (i + 1) % size) for i in range(size - 1)]
        down = [(j, i) for i, j in up]
        before = lax.ppermute(last, axis, up)
        after = lax.ppermute(leading, axis, down)
    return jnp.concatenate([before, value, after], axis=dim)


def padded_2(value, sides, width):
    for axis, dim in sides:
        value = pad_side(value, axis, dim, width)
    return value


SIDES = (("gx", 0), ("ga", 1), ("gz", 2))


def operate_rim(zed, diagonal, inside):
    centre = zed[1:-1, 1:-1, 1:-1]
    beside = zed[2:, 1:-1, 1:-1] + zed[:-2, 1:-1, 1:-1]
    beside = beside + zed[1:-1, 2:, 1:-1] + zed[1:-1, :-2, 1:-1]
    beside = beside + zed[1:-1, 1:-1, 2:] + zed[1:-1, 1:-1, :-2]
    return ((6.0 + diagonal) * centre - beside) * inside


def inside_grid(shape, width):
    result = None
    for axis, dim in SIDES:
        length = shape[dim]
        place = lax.axis_index(axis) * length - width + jnp.arange(length + 2 * width, dtype=jnp.int32)
        line = ((place >= 0) & (place < lax.axis_size(axis) * length)).astype(jnp.float32)
        view = [1, 1, 1]
        view[dim] = length + 2 * width
        line = line.reshape(view)
        result = line if result is None else result * line
    return result


def interior(value, width):
    return value[width:-width, width:-width, width:-width]


def forward_table(count, basis):
    row_index = jnp.arange(PTS * count + 2 * RIM, dtype=jnp.int32)
    element = jnp.arange(count, dtype=jnp.int32)
    offset = jnp.arange(WIDE, dtype=jnp.int32)
    select = (
        row_index[:, None, None] == PTS * element[None, :, None] + offset[None, None, :]
    ).astype(jnp.float32)
    table = jnp.einsum("rcj,jm->rcm", select, basis, precision=PRECISE)
    return table.reshape(PTS * count + 2 * RIM, count * WIDE)


def backward_table(count, basis):
    same = jnp.eye(count, dtype=jnp.float32)
    table = jnp.einsum("cd,im->cmdi", same, basis[RIM : RIM + PTS], precision=PRECISE)
    return table.reshape(count * WIDE, count * PTS)


def schwarz_part(padded, basis_tables, eigenvalues):
    count_x = (padded.shape[0] - 2 * RIM) // PTS
    count_y = (padded.shape[1] - 2 * RIM) // PTS
    count_z = (padded.shape[2] - 2 * RIM) // PTS
    spectral = jnp.einsum(
        "pqr,rc->pqc", padded, forward_table(count_z, basis_tables[2]), precision=PRECISE
    )
    spectral = jnp.einsum(
        "pqc,pa->aqc", spectral, forward_table(count_x, basis_tables[0]), precision=PRECISE
    )
    spectral = jnp.einsum(
        "aqc,qb->abc", spectral, forward_table(count_y, basis_tables[1]), precision=PRECISE
    )
    denominator = (
        jnp.tile(eigenvalues[0], count_x)[:, None, None]
        + jnp.tile(eigenvalues[1], count_y)[None, :, None]
    )
    denominator = denominator + jnp.tile(eigenvalues[2], count_z)[None, None, :]
    spectral = spectral / denominator
    local_part = jnp.einsum(
        "abc,cr->abr", spectral, backward_table(count_z, basis_tables[2]), precision=PRECISE
    )
    local_part = jnp.einsum(
        "abr,ap->pbr", local_part, backward_table(count_x, basis_tables[0]), precision=PRECISE
    )
    local_part = jnp.einsum(
        "pbr,bq->pqr", local_part, backward_table(count_y, basis_tables[1]), precision=PRECISE
    )
    return local_part


def coarse_terms(field, blocks, selector):
    count_x = field.shape[0] // PTS
    count_y = field.shape[1] // PTS
    count_z = field.shape[2] // PTS
    cells = count_x * count_y * count_z
    point = jnp.arange(field.shape[2], dtype=jnp.int32)
    along = (point[:, None] // PTS == jnp.arange(count_z, dtype=jnp.int32)[None, :]).astype(jnp.float32)
    sums = jnp.einsum("pqr,rc->pqc", field, along, precision=PRECISE)
    sums = jnp.sum(sums.reshape(count_x, PTS, count_y, PTS, count_z), axis=(1, 3))
    restricted = sums.reshape(cells) * (1.0 / PTS**3)
    terms = jnp.einsum("kpq,p->kq", blocks, restricted, precision=PRECISE)
    return jnp.einsum("kj,kq->jq", selector, terms, precision=PRECISE)


def element_table(blocks, columns, shape):
    count = blocks.shape[0]
    grid = (shape[0] // PTS, shape[1] // PTS, shape[2] // PTS)
    rows = jnp.transpose(blocks, (1, 0, 2)).reshape(grid + (count * blocks.shape[2],))
    cols = jnp.broadcast_to(columns.astype(jnp.float32), grid + (count,))
    return jnp.concatenate([rows, cols], axis=-1)


def coarse_rim(wholes, table, count, group):
    lo, whole, hi = wholes
    grid = table.shape[:3]
    width = (table.shape[3] - count) // count
    rows = table[..., : count * width].reshape(grid + (count, width))
    cols = table[..., count * width :]
    onehot = (cols[..., None] == jnp.arange(group, dtype=jnp.float32)).astype(jnp.float32)
    stacked = jnp.stack([lo] + [whole] * (grid[0] - 2) + [hi])
    picked = jnp.einsum("abckg,agq->abckq", onehot, stacked, precision=PRECISE)
    return jnp.sum(rows * picked, axis=(3, 4))


def spread_rim(values, width, shape):
    def table(length, count):
        point = jnp.arange(length + 2 * width, dtype=jnp.int32) - width + PTS
        element = jnp.arange(count, dtype=jnp.int32)
        return (point[:, None] // PTS == element[None, :]).astype(jnp.float32)

    grid = values.shape
    out = jnp.einsum("abc,rc->abr", values, table(shape[2], grid[2]), precision=PRECISE)
    out = jnp.einsum("abr,pa->pbr", out, table(shape[0], grid[0]), precision=PRECISE)
    return jnp.einsum("pbr,qb->pqr", out, table(shape[1], grid[1]), precision=PRECISE)


ALL = ("gx", "ga", "gz")


def butterfly_stages(axes):
    stages = []
    for axis in axes:
        size = lax.axis_size(axis)
        if size & (size - 1):
            stages.append(lambda value, axis=axis: lax.psum(value, axis))
            continue
        if size == 4:
            stages.append(functools.partial(sum_of_four, axis=axis))
            continue
        step = 1
        while step < size:
            pairs = [(i, i ^ step) for i in range(size)]
            stages.append(lambda value, axis=axis, pairs=pairs: value + lax.ppermute(value, axis, pairs))
            step *= 2
    return stages


def sum_of_four(value, axis):
    got = [value] + [lax.ppermute(value, axis, [(i, i ^ s) for i in range(4)]) for s in (1, 2, 3)]
    return (got[0] + got[1]) + (got[2] + got[3])


def butterfly(value, axes):
    for stage in butterfly_stages(axes):
        value = stage(value)
    return value


def reduce_scalars(scalars):
    total = butterfly(lax.optimization_barrier(jnp.stack(scalars)), ALL)
    return [total[i] for i in range(len(scalars))]


HALO_ORDER = (("ga", 1), ("gz", 2), ("gx", 0))


def reduce_coarse(local, buffer, scalars):
    count = len(scalars)
    payload = jnp.concatenate([buffer.reshape(-1), jnp.stack(scalars)])
    halo = [functools.partial(pad_side, axis=axis, dim=dim, width=RIM + 1) for axis, dim in HALO_ORDER]
    sums = butterfly_stages(("ga", "gz"))
    local, payload = lax.optimization_barrier((local, payload))
    for index in range(max(len(halo), len(sums))):
        if index < len(halo):
            local = halo[index](local)
        if index < len(sums):
            payload = sums[index](payload)
        local, payload = lax.optimization_barrier((local, payload))
    size = payload.shape[0] - count
    whole = payload[:size].reshape(buffer.shape)
    if lax.axis_size("gx") == 2:
        got = lax.ppermute(payload, "gx", [(0, 1), (1, 0)])
        total = payload[size:] + got[size:]
        other = got[:size].reshape(buffer.shape)
        first = lax.axis_index("gx") == 0
        zero = jnp.zeros_like(other)
        lo, hi = jnp.where(first, zero, other), jnp.where(first, other, zero)
    else:
        total = butterfly(payload[size:], ("gx",))
        gx = lax.axis_size("gx")
        up = [(i, i + 1) for i in range(gx - 1)]
        lo = lax.ppermute(whole, "gx", up)
        hi = lax.ppermute(whole, "gx", [(j, i) for i, j in up])
    return local, (lo, whole, hi), [total[i] for i in range(count)]


def body(right_side, diagonal, basis_tables, eigenvalues, coarse_blocks, coarse_columns):
    blocks = coarse_blocks.reshape(coarse_blocks.shape[3:])
    columns = coarse_columns.reshape(coarse_columns.shape[3])
    count = blocks.shape[0]
    group = lax.axis_size(("ga", "gz"))
    selector = (columns[:, None] == jnp.arange(group, dtype=jnp.int32)[None, :]).astype(jnp.float32)
    shape = right_side.shape
    stacked = tuple((axis, dim + 1) for axis, dim in SIDES)
    wide_pair = padded_2(jnp.stack([diagonal, right_side]), stacked, RIM)
    wide_diagonal, wide_residual = wide_pair[0], wide_pair[1]
    inside = inside_grid(shape, RIM)
    table = padded_2(element_table(blocks, columns, shape), SIDES, 1)

    def precondition_rim(wide_field, field):
        local = schwarz_part(wide_field, basis_tables, eigenvalues)
        return local, coarse_terms(field, blocks, selector)

    def coarse_on_rim(wholes):
        return spread_rim(coarse_rim(wholes, table, count, group), RIM + 1, shape)

    solution = jnp.zeros_like(right_side)
    for restart in range(CYCLES):
        residual = interior(wide_residual, RIM)
        wide_local, terms = precondition_rim(wide_residual, residual)
        wide_local, wholes, (square,) = reduce_coarse(wide_local, terms, [jnp.sum(residual * residual)])
        initial_norm = jnp.sqrt(square)
        first_vector = residual / initial_norm
        wide_zed = (wide_local + coarse_on_rim(wholes)) / initial_norm
        first_zed = interior(wide_zed, RIM + 1)
        wide_first = operate_rim(wide_zed, wide_diagonal, inside)
        first_image = interior(wide_first, RIM)
        wide_local, terms = precondition_rim(wide_first, first_image)
        wide_local, wholes, (first_proj, image_square) = reduce_coarse(
            wide_local, terms, [jnp.sum(first_vector * first_image), jnp.sum(first_image * first_image)]
        )
        first_len = jnp.sqrt(image_square - first_proj * first_proj)
        second_vector = (first_image - first_proj * first_vector) / first_len
        wide_second_zed = (wide_local + coarse_on_rim(wholes) - first_proj * wide_zed) / first_len
        second_zed = interior(wide_second_zed, RIM + 1)
        wide_second = operate_rim(wide_second_zed, wide_diagonal, inside)
        second_image = interior(wide_second, RIM)
        upper_proj, lower_proj, second_square = reduce_scalars(
            [
                jnp.sum(first_vector * second_image),
                jnp.sum(second_vector * second_image),
                jnp.sum(second_image * second_image),
            ]
        )
        second_len = jnp.sqrt(second_square - upper_proj * upper_proj - lower_proj * lower_proj)
        gram_first = first_proj * first_proj + first_len * first_len
        gram_cross = first_proj * upper_proj + first_len * lower_proj
        gram_second = upper_proj * upper_proj + lower_proj * lower_proj + second_len * second_len
        target_first = initial_norm * first_proj
        target_second = initial_norm * upper_proj
        determinant = gram_first * gram_second - gram_cross * gram_cross
        weight_first = (gram_second * target_first - gram_cross * target_second) / determinant
        weight_second = (gram_first * target_second - gram_cross * target_first) / determinant
        solution = solution + weight_first * first_zed + weight_second * second_zed
        wide_residual = wide_residual - weight_first * wide_first - weight_second * wide_second
    return (solution, interior(wide_residual, RIM))


def solution(mesh):
    in_specs = (
        P("gx", "ga", "gz"),
        P("gx", "ga", "gz"),
        P(),
        P(),
        P("gx", "ga", "gz", None, None, None),
        P("gx", "ga", "gz", None),
    )
    out_specs = (P("gx", "ga", "gz"), P("gx", "ga", "gz"))
    return jax.shard_map(body, mesh=mesh, in_specs=in_specs, out_specs=out_specs, check_vma=False)
```

```python
import functools

import jax
import jax.numpy as jnp
from jax import lax
from jax.sharding import PartitionSpec as P

PTS = 8
RIM = 2
WIDE = 12
CYCLES = 2


PRECISE = lax.Precision.HIGHEST


def pad_side(value, axis, dim, width):
    size, length = (lax.axis_size(axis), value.shape[dim])
    last = lax.slice_in_dim(value, length - width, length, axis=dim)
    leading = lax.slice_in_dim(value, 0, width, axis=dim)
    if size == 2:
        first = lax.axis_index(axis) == 0
        got = lax.ppermute(jnp.where(first, last, leading), axis, [(0, 1), (1, 0)])
        zero = jnp.zeros_like(got)
        before = jnp.where(first, zero, got)
        after = jnp.where(first, got, zero)
    else:
        up = [(i, (i + 1) % size) for i in range(size - 1)]
        down = [(j, i) for i, j in up]
        before = lax.ppermute(last, axis, up)
        after = lax.ppermute(leading, axis, down)
    return jnp.concatenate([before, value, after], axis=dim)


def padded_2(value, sides, width):
    for axis, dim in sides:
        value = pad_side(value, axis, dim, width)
    return value


SIDES = (("gx", 0), ("ga", 1), ("gz", 2))


def operate_rim(zed, diagonal, inside):
    centre = zed[1:-1, 1:-1, 1:-1]
    beside = zed[2:, 1:-1, 1:-1] + zed[:-2, 1:-1, 1:-1]
    beside = beside + zed[1:-1, 2:, 1:-1] + zed[1:-1, :-2, 1:-1]
    beside = beside + zed[1:-1, 1:-1, 2:] + zed[1:-1, 1:-1, :-2]
    return ((6.0 + diagonal) * centre - beside) * inside


def inside_grid(shape, width):
    result = None
    for axis, dim in SIDES:
        length = shape[dim]
        place = lax.axis_index(axis) * length - width + jnp.arange(length + 2 * width, dtype=jnp.int32)
        line = ((place >= 0) & (place < lax.axis_size(axis) * length)).astype(jnp.float32)
        view = [1, 1, 1]
        view[dim] = length + 2 * width
        line = line.reshape(view)
        result = line if result is None else result * line
    return result


def interior(value, width):
    return value[width:-width, width:-width, width:-width]


def forward_table(count, basis):
    row_index = jnp.arange(PTS * count + 2 * RIM, dtype=jnp.int32)
    element = jnp.arange(count, dtype=jnp.int32)
    offset = jnp.arange(WIDE, dtype=jnp.int32)
    select = (
        row_index[:, None, None] == PTS * element[None, :, None] + offset[None, None, :]
    ).astype(jnp.float32)
    table = jnp.einsum("rcj,jm->rcm", select, basis, precision=PRECISE)
    return table.reshape(PTS * count + 2 * RIM, count * WIDE)


def backward_table(count, basis):
    same = jnp.eye(count, dtype=jnp.float32)
    table = jnp.einsum("cd,im->cmdi", same, basis[RIM : RIM + PTS], precision=PRECISE)
    return table.reshape(count * WIDE, count * PTS)


def schwarz_part(padded, basis_tables, eigenvalues):
    count_x = (padded.shape[0] - 2 * RIM) // PTS
    count_y = (padded.shape[1] - 2 * RIM) // PTS
    count_z = (padded.shape[2] - 2 * RIM) // PTS
    spectral = jnp.einsum(
        "pqr,rc->pqc", padded, forward_table(count_z, basis_tables[2]), precision=PRECISE
    )
    spectral = jnp.einsum(
        "pqc,pa->aqc", spectral, forward_table(count_x, basis_tables[0]), precision=PRECISE
    )
    spectral = jnp.einsum(
        "aqc,qb->abc", spectral, forward_table(count_y, basis_tables[1]), precision=PRECISE
    )
    denominator = (
        jnp.tile(eigenvalues[0], count_x)[:, None, None]
        + jnp.tile(eigenvalues[1], count_y)[None, :, None]
    )
    denominator = denominator + jnp.tile(eigenvalues[2], count_z)[None, None, :]
    spectral = spectral / denominator
    local_part = jnp.einsum(
        "abc,cr->abr", spectral, backward_table(count_z, basis_tables[2]), precision=PRECISE
    )
    local_part = jnp.einsum(
        "abr,ap->pbr", local_part, backward_table(count_x, basis_tables[0]), precision=PRECISE
    )
    local_part = jnp.einsum(
        "pbr,bq->pqr", local_part, backward_table(count_y, basis_tables[1]), precision=PRECISE
    )
    return local_part


def coarse_terms(field, blocks, selector):
    count_x = field.shape[0] // PTS
    count_y = field.shape[1] // PTS
    count_z = field.shape[2] // PTS
    cells = count_x * count_y * count_z
    point = jnp.arange(field.shape[2], dtype=jnp.int32)
    along = (point[:, None] // PTS == jnp.arange(count_z, dtype=jnp.int32)[None, :]).astype(jnp.float32)
    sums = jnp.einsum("pqr,rc->pqc", field, along, precision=PRECISE)
    sums = jnp.sum(sums.reshape(count_x, PTS, count_y, PTS, count_z), axis=(1, 3))
    restricted = sums.reshape(cells) * (1.0 / PTS**3)
    terms = jnp.einsum("kpq,p->kq", blocks, restricted, precision=PRECISE)
    return jnp.einsum("kj,kq->jq", selector, terms, precision=PRECISE)


def element_table(blocks, columns, shape):
    count = blocks.shape[0]
    grid = (shape[0] // PTS, shape[1] // PTS, shape[2] // PTS)
    rows = jnp.transpose(blocks, (1, 0, 2)).reshape(grid + (count * blocks.shape[2],))
    cols = jnp.broadcast_to(columns.astype(jnp.float32), grid + (count,))
    return jnp.concatenate([rows, cols], axis=-1)


def coarse_rim(wholes, table, count, group):
    lo, whole, hi = wholes
    grid = table.shape[:3]
    width = (table.shape[3] - count) // count
    rows = table[..., : count * width].reshape(grid + (count, width))
    cols = table[..., count * width :]
    onehot = (cols[..., None] == jnp.arange(group, dtype=jnp.float32)).astype(jnp.float32)
    stacked = jnp.stack([lo] + [whole] * (grid[0] - 2) + [hi])
    picked = jnp.einsum("abckg,agq->abckq", onehot, stacked, precision=PRECISE)
    return jnp.sum(rows * picked, axis=(3, 4))


def spread_rim(values, width, shape):
    def table(length, count):
        point = jnp.arange(length + 2 * width, dtype=jnp.int32) - width + PTS
        element = jnp.arange(count, dtype=jnp.int32)
        return (point[:, None] // PTS == element[None, :]).astype(jnp.float32)

    grid = values.shape
    out = jnp.einsum("abc,rc->abr", values, table(shape[2], grid[2]), precision=PRECISE)
    out = jnp.einsum("abr,pa->pbr", out, table(shape[0], grid[0]), precision=PRECISE)
    return jnp.einsum("pbr,qb->pqr", out, table(shape[1], grid[1]), precision=PRECISE)


ALL = ("gx", "ga", "gz")


def butterfly_stages(axes):
    stages = []
    for axis in axes:
        size = lax.axis_size(axis)
        if size & (size - 1):
            stages.append(lambda value, axis=axis: lax.psum(value, axis))
            continue
        if size == 4:
            stages.append(functools.partial(sum_of_four, axis=axis))
            continue
        step = 1
        while step < size:
            pairs = [(i, i ^ step) for i in range(size)]
            stages.append(lambda value, axis=axis, pairs=pairs: value + lax.ppermute(value, axis, pairs))
            step *= 2
    return stages


def sum_of_four(value, axis):
    got = [value] + [lax.ppermute(value, axis, [(i, i ^ s) for i in range(4)]) for s in (1, 2, 3)]
    return (got[0] + got[1]) + (got[2] + got[3])


def butterfly(value, axes):
    for stage in butterfly_stages(axes):
        value = stage(value)
    return value


def reduce_scalars(scalars):
    total = butterfly(lax.optimization_barrier(jnp.stack(scalars)), ALL)
    return [total[i] for i in range(len(scalars))]


def fold_four(payload, local, axis, dim, width):
    me = lax.axis_index(axis)
    length = local.shape[dim]
    last = lax.slice_in_dim(local, length - width, length, axis=dim)
    leading = lax.slice_in_dim(local, 0, width, axis=dim)
    even = me % 2 == 0
    count = payload.shape[0]

    def send(slab, step):
        message = jnp.concatenate([payload, slab.reshape(-1)])
        return lax.ppermute(message, axis, [(i, i ^ step) for i in range(4)])

    got_one = send(jnp.where(even, last, leading), 1)
    got_two = lax.ppermute(payload, axis, [(i, i ^ 2) for i in range(4)])
    got_three = send(jnp.where(me == 1, last, leading), 3)
    total = (payload + got_one[:count]) + (got_two + got_three[:count])
    from_one = got_one[count:].reshape(last.shape)
    from_three = got_three[count:].reshape(last.shape)
    zero = jnp.zeros_like(from_one)
    before = jnp.where(even, jnp.where(me == 2, from_three, zero), from_one)
    after = jnp.where(even, from_one, jnp.where(me == 1, from_three, zero))
    return total, jnp.concatenate([before, local, after], axis=dim)


def reduce_coarse(local, buffer, scalars):
    count = len(scalars)
    width = RIM + 1
    payload = jnp.concatenate([buffer.reshape(-1), jnp.stack(scalars)])
    local, payload = lax.optimization_barrier((local, payload))
    for axis, dim in (("ga", 1), ("gz", 2)):
        if lax.axis_size(axis) == 4:
            payload, local = fold_four(payload, local, axis, dim, width)
        else:
            payload = butterfly(payload, (axis,))
            local = pad_side(local, axis, dim, width)
        local, payload = lax.optimization_barrier((local, payload))
    size = payload.shape[0] - count
    whole = payload[:size].reshape(buffer.shape)
    if lax.axis_size("gx") == 2:
        first = lax.axis_index("gx") == 0
        length = local.shape[0]
        slab = jnp.where(first, local[length - width :], local[:width])
        message = jnp.concatenate([payload, slab.reshape(-1)])
        got = lax.ppermute(message, "gx", [(0, 1), (1, 0)])
        total = payload[size:] + got[size : size + count]
        other = got[:size].reshape(buffer.shape)
        beside = got[size + count :].reshape(slab.shape)
        zero = jnp.zeros_like(other)
        lo, hi = jnp.where(first, zero, other), jnp.where(first, other, zero)
        flat = jnp.zeros_like(beside)
        local = jnp.concatenate(
            [jnp.where(first, flat, beside), local, jnp.where(first, beside, flat)], axis=0
        )
    else:
        total = butterfly(payload[size:], ("gx",))
        gx = lax.axis_size("gx")
        up = [(i, i + 1) for i in range(gx - 1)]
        lo = lax.ppermute(whole, "gx", up)
        hi = lax.ppermute(whole, "gx", [(j, i) for i, j in up])
        local = pad_side(local, "gx", 0, width)
    return local, (lo, whole, hi), [total[i] for i in range(count)]


def body(right_side, diagonal, basis_tables, eigenvalues, coarse_blocks, coarse_columns):
    blocks = coarse_blocks.reshape(coarse_blocks.shape[3:])
    columns = coarse_columns.reshape(coarse_columns.shape[3])
    count = blocks.shape[0]
    group = lax.axis_size(("ga", "gz"))
    selector = (columns[:, None] == jnp.arange(group, dtype=jnp.int32)[None, :]).astype(jnp.float32)
    shape = right_side.shape
    stacked = tuple((axis, dim + 1) for axis, dim in SIDES)
    wide_pair = padded_2(jnp.stack([diagonal, right_side]), stacked, RIM)
    wide_diagonal, wide_residual = wide_pair[0], wide_pair[1]
    inside = inside_grid(shape, RIM)
    table = padded_2(element_table(blocks, columns, shape), SIDES, 1)

    def precondition_rim(wide_field, field):
        local = schwarz_part(wide_field, basis_tables, eigenvalues)
        return local, coarse_terms(field, blocks, selector)

    def coarse_on_rim(wholes):
        return spread_rim(coarse_rim(wholes, table, count, group), RIM + 1, shape)

    solution = jnp.zeros_like(right_side)
    for restart in range(CYCLES):
        residual = interior(wide_residual, RIM)
        wide_local, terms = precondition_rim(wide_residual, residual)
        wide_local, wholes, (square,) = reduce_coarse(wide_local, terms, [jnp.sum(residual * residual)])
        initial_norm = jnp.sqrt(square)
        first_vector = residual / initial_norm
        wide_zed = (wide_local + coarse_on_rim(wholes)) / initial_norm
        first_zed = interior(wide_zed, RIM + 1)
        wide_first = operate_rim(wide_zed, wide_diagonal, inside)
        first_image = interior(wide_first, RIM)
        wide_local, terms = precondition_rim(wide_first, first_image)
        wide_local, wholes, (first_proj, image_square) = reduce_coarse(
            wide_local, terms, [jnp.sum(first_vector * first_image), jnp.sum(first_image * first_image)]
        )
        first_len = jnp.sqrt(image_square - first_proj * first_proj)
        second_vector = (first_image - first_proj * first_vector) / first_len
        wide_second_zed = (wide_local + coarse_on_rim(wholes) - first_proj * wide_zed) / first_len
        second_zed = interior(wide_second_zed, RIM + 1)
        wide_second = operate_rim(wide_second_zed, wide_diagonal, inside)
        second_image = interior(wide_second, RIM)
        upper_proj, lower_proj, second_square = reduce_scalars(
            [
                jnp.sum(first_vector * second_image),
                jnp.sum(second_vector * second_image),
                jnp.sum(second_image * second_image),
            ]
        )
        second_len = jnp.sqrt(second_square - upper_proj * upper_proj - lower_proj * lower_proj)
        gram_first = first_proj * first_proj + first_len * first_len
        gram_cross = first_proj * upper_proj + first_len * lower_proj
        gram_second = upper_proj * upper_proj + lower_proj * lower_proj + second_len * second_len
        target_first = initial_norm * first_proj
        target_second = initial_norm * upper_proj
        determinant = gram_first * gram_second - gram_cross * gram_cross
        weight_first = (gram_second * target_first - gram_cross * target_second) / determinant
        weight_second = (gram_first * target_second - gram_cross * target_first) / determinant
        solution = solution + weight_first * first_zed + weight_second * second_zed
        wide_residual = wide_residual - weight_first * wide_first - weight_second * wide_second
    return (solution, interior(wide_residual, RIM))


def solution(mesh):
    in_specs = (
        P("gx", "ga", "gz"),
        P("gx", "ga", "gz"),
        P(),
        P(),
        P("gx", "ga", "gz", None, None, None),
        P("gx", "ga", "gz", None),
    )
    out_specs = (P("gx", "ga", "gz"), P("gx", "ga", "gz"))
    return jax.shard_map(body, mesh=mesh, in_specs=in_specs, out_specs=out_specs, check_vma=False)
```

```python
import functools

import jax
import jax.numpy as jnp
from jax import lax
from jax.sharding import PartitionSpec as P

PTS = 8
RIM = 2
WIDE = 12
CYCLES = 2


PRECISE = lax.Precision.HIGHEST


def pad_side(value, axis, dim, width):
    size, length = (lax.axis_size(axis), value.shape[dim])
    last = lax.slice_in_dim(value, length - width, length, axis=dim)
    leading = lax.slice_in_dim(value, 0, width, axis=dim)
    if size == 2:
        first = lax.axis_index(axis) == 0
        got = lax.ppermute(jnp.where(first, last, leading), axis, [(0, 1), (1, 0)])
        zero = jnp.zeros_like(got)
        before = jnp.where(first, zero, got)
        after = jnp.where(first, got, zero)
    else:
        up = [(i, (i + 1) % size) for i in range(size - 1)]
        down = [(j, i) for i, j in up]
        before = lax.ppermute(last, axis, up)
        after = lax.ppermute(leading, axis, down)
    return jnp.concatenate([before, value, after], axis=dim)


def padded_2(value, sides, width):
    for axis, dim in sides:
        value = pad_side(value, axis, dim, width)
    return value


def pad_together(values, axis, dims, widths):
    lasts, leads = [], []
    for value, dim, width in zip(values, dims, widths):
        length = value.shape[dim]
        lasts.append(lax.slice_in_dim(value, length - width, length, axis=dim))
        leads.append(lax.slice_in_dim(value, 0, width, axis=dim))

    def pack(slabs):
        return jnp.concatenate([slab.reshape(-1) for slab in slabs])

    def unpack(flat):
        pieces, at = [], 0
        for slab in lasts:
            pieces.append(flat[at : at + slab.size].reshape(slab.shape))
            at += slab.size
        return pieces

    size = lax.axis_size(axis)
    if size == 2:
        first = lax.axis_index(axis) == 0
        got = unpack(lax.ppermute(jnp.where(first, pack(lasts), pack(leads)), axis, [(0, 1), (1, 0)]))
        befores = [jnp.where(first, jnp.zeros_like(g), g) for g in got]
        afters = [jnp.where(first, g, jnp.zeros_like(g)) for g in got]
    else:
        up = [(i, (i + 1) % size) for i in range(size - 1)]
        befores = unpack(lax.ppermute(pack(lasts), axis, up))
        afters = unpack(lax.ppermute(pack(leads), axis, [(j, i) for i, j in up]))
    return [
        jnp.concatenate([before, value, after], axis=dim)
        for before, value, after, dim in zip(befores, values, afters, dims)
    ]


SIDES = (("gx", 0), ("ga", 1), ("gz", 2))


def operate_rim(zed, diagonal, inside):
    centre = zed[1:-1, 1:-1, 1:-1]
    beside = zed[2:, 1:-1, 1:-1] + zed[:-2, 1:-1, 1:-1]
    beside = beside + zed[1:-1, 2:, 1:-1] + zed[1:-1, :-2, 1:-1]
    beside = beside + zed[1:-1, 1:-1, 2:] + zed[1:-1, 1:-1, :-2]
    return ((6.0 + diagonal) * centre - beside) * inside


def inside_grid(shape, width):
    result = None
    for axis, dim in SIDES:
        length = shape[dim]
        place = lax.axis_index(axis) * length - width + jnp.arange(length + 2 * width, dtype=jnp.int32)
        line = ((place >= 0) & (place < lax.axis_size(axis) * length)).astype(jnp.float32)
        view = [1, 1, 1]
        view[dim] = length + 2 * width
        line = line.reshape(view)
        result = line if result is None else result * line
    return result


def interior(value, width):
    return value[width:-width, width:-width, width:-width]


def forward_table(count, basis):
    row_index = jnp.arange(PTS * count + 2 * RIM, dtype=jnp.int32)
    element = jnp.arange(count, dtype=jnp.int32)
    offset = jnp.arange(WIDE, dtype=jnp.int32)
    select = (
        row_index[:, None, None] == PTS * element[None, :, None] + offset[None, None, :]
    ).astype(jnp.float32)
    table = jnp.einsum("rcj,jm->rcm", select, basis, precision=PRECISE)
    return table.reshape(PTS * count + 2 * RIM, count * WIDE)


def backward_table(count, basis):
    same = jnp.eye(count, dtype=jnp.float32)
    table = jnp.einsum("cd,im->cmdi", same, basis[RIM : RIM + PTS], precision=PRECISE)
    return table.reshape(count * WIDE, count * PTS)


def schwarz_part(padded, basis_tables, eigenvalues):
    count_x = (padded.shape[0] - 2 * RIM) // PTS
    count_y = (padded.shape[1] - 2 * RIM) // PTS
    count_z = (padded.shape[2] - 2 * RIM) // PTS
    spectral = jnp.einsum(
        "pqr,rc->pqc", padded, forward_table(count_z, basis_tables[2]), precision=PRECISE
    )
    spectral = jnp.einsum(
        "pqc,pa->aqc", spectral, forward_table(count_x, basis_tables[0]), precision=PRECISE
    )
    spectral = jnp.einsum(
        "aqc,qb->abc", spectral, forward_table(count_y, basis_tables[1]), precision=PRECISE
    )
    denominator = (
        jnp.tile(eigenvalues[0], count_x)[:, None, None]
        + jnp.tile(eigenvalues[1], count_y)[None, :, None]
    )
    denominator = denominator + jnp.tile(eigenvalues[2], count_z)[None, None, :]
    spectral = spectral / denominator
    local_part = jnp.einsum(
        "abc,cr->abr", spectral, backward_table(count_z, basis_tables[2]), precision=PRECISE
    )
    local_part = jnp.einsum(
        "abr,ap->pbr", local_part, backward_table(count_x, basis_tables[0]), precision=PRECISE
    )
    local_part = jnp.einsum(
        "pbr,bq->pqr", local_part, backward_table(count_y, basis_tables[1]), precision=PRECISE
    )
    return local_part


def coarse_terms(field, blocks, selector):
    count_x = field.shape[0] // PTS
    count_y = field.shape[1] // PTS
    count_z = field.shape[2] // PTS
    cells = count_x * count_y * count_z
    point = jnp.arange(field.shape[2], dtype=jnp.int32)
    along = (point[:, None] // PTS == jnp.arange(count_z, dtype=jnp.int32)[None, :]).astype(jnp.float32)
    sums = jnp.einsum("pqr,rc->pqc", field, along, precision=PRECISE)
    sums = jnp.sum(sums.reshape(count_x, PTS, count_y, PTS, count_z), axis=(1, 3))
    restricted = sums.reshape(cells) * (1.0 / PTS**3)
    terms = jnp.einsum("kpq,p->kq", blocks, restricted, precision=PRECISE)
    return jnp.einsum("kj,kq->jq", selector, terms, precision=PRECISE)


def element_table(blocks, columns, shape):
    count = blocks.shape[0]
    grid = (shape[0] // PTS, shape[1] // PTS, shape[2] // PTS)
    rows = jnp.transpose(blocks, (1, 0, 2)).reshape(grid + (count * blocks.shape[2],))
    cols = jnp.broadcast_to(columns.astype(jnp.float32), grid + (count,))
    return jnp.concatenate([rows, cols], axis=-1)


def coarse_rim(wholes, table, count, group):
    lo, whole, hi = wholes
    grid = table.shape[:3]
    width = (table.shape[3] - count) // count
    rows = table[..., : count * width].reshape(grid + (count, width))
    cols = table[..., count * width :]
    onehot = (cols[..., None] == jnp.arange(group, dtype=jnp.float32)).astype(jnp.float32)
    stacked = jnp.stack([lo] + [whole] * (grid[0] - 2) + [hi])
    picked = jnp.einsum("abckg,agq->abckq", onehot, stacked, precision=PRECISE)
    return jnp.sum(rows * picked, axis=(3, 4))


def spread_rim(values, width, shape):
    def table(length, count):
        point = jnp.arange(length + 2 * width, dtype=jnp.int32) - width + PTS
        element = jnp.arange(count, dtype=jnp.int32)
        return (point[:, None] // PTS == element[None, :]).astype(jnp.float32)

    grid = values.shape
    out = jnp.einsum("abc,rc->abr", values, table(shape[2], grid[2]), precision=PRECISE)
    out = jnp.einsum("abr,pa->pbr", out, table(shape[0], grid[0]), precision=PRECISE)
    return jnp.einsum("pbr,qb->pqr", out, table(shape[1], grid[1]), precision=PRECISE)


ALL = ("gx", "ga", "gz")


def butterfly_stages(axes):
    stages = []
    for axis in axes:
        size = lax.axis_size(axis)
        if size & (size - 1):
            stages.append(lambda value, axis=axis: lax.psum(value, axis))
            continue
        if size == 4:
            stages.append(functools.partial(sum_of_four, axis=axis))
            continue
        step = 1
        while step < size:
            pairs = [(i, i ^ step) for i in range(size)]
            stages.append(lambda value, axis=axis, pairs=pairs: value + lax.ppermute(value, axis, pairs))
            step *= 2
    return stages


def sum_of_four(value, axis):
    got = [value] + [lax.ppermute(value, axis, [(i, i ^ s) for i in range(4)]) for s in (1, 2, 3)]
    return (got[0] + got[1]) + (got[2] + got[3])


def butterfly(value, axes):
    for stage in butterfly_stages(axes):
        value = stage(value)
    return value


def reduce_scalars(scalars):
    total = butterfly(lax.optimization_barrier(jnp.stack(scalars)), ALL)
    return [total[i] for i in range(len(scalars))]


def fold_four(payload, local, axis, dim, width):
    me = lax.axis_index(axis)
    length = local.shape[dim]
    last = lax.slice_in_dim(local, length - width, length, axis=dim)
    leading = lax.slice_in_dim(local, 0, width, axis=dim)
    even = me % 2 == 0
    count = payload.shape[0]

    def send(slab, step):
        message = jnp.concatenate([payload, slab.reshape(-1)])
        return lax.ppermute(message, axis, [(i, i ^ step) for i in range(4)])

    got_one = send(jnp.where(even, last, leading), 1)
    got_two = lax.ppermute(payload, axis, [(i, i ^ 2) for i in range(4)])
    got_three = send(jnp.where(me == 1, last, leading), 3)
    total = (payload + got_one[:count]) + (got_two + got_three[:count])
    from_one = got_one[count:].reshape(last.shape)
    from_three = got_three[count:].reshape(last.shape)
    zero = jnp.zeros_like(from_one)
    before = jnp.where(even, jnp.where(me == 2, from_three, zero), from_one)
    after = jnp.where(even, from_one, jnp.where(me == 1, from_three, zero))
    return total, jnp.concatenate([before, local, after], axis=dim)


def reduce_coarse(local, buffer, scalars):
    count = len(scalars)
    width = RIM + 1
    payload = jnp.concatenate([buffer.reshape(-1), jnp.stack(scalars)])
    local, payload = lax.optimization_barrier((local, payload))
    for axis, dim in (("ga", 1), ("gz", 2)):
        if lax.axis_size(axis) == 4:
            payload, local = fold_four(payload, local, axis, dim, width)
        else:
            payload = butterfly(payload, (axis,))
            local = pad_side(local, axis, dim, width)
        local, payload = lax.optimization_barrier((local, payload))
    size = payload.shape[0] - count
    whole = payload[:size].reshape(buffer.shape)
    if lax.axis_size("gx") == 2:
        first = lax.axis_index("gx") == 0
        length = local.shape[0]
        slab = jnp.where(first, local[length - width :], local[:width])
        message = jnp.concatenate([payload, slab.reshape(-1)])
        got = lax.ppermute(message, "gx", [(0, 1), (1, 0)])
        total = payload[size:] + got[size : size + count]
        other = got[:size].reshape(buffer.shape)
        beside = got[size + count :].reshape(slab.shape)
        zero = jnp.zeros_like(other)
        lo, hi = jnp.where(first, zero, other), jnp.where(first, other, zero)
        flat = jnp.zeros_like(beside)
        local = jnp.concatenate(
            [jnp.where(first, flat, beside), local, jnp.where(first, beside, flat)], axis=0
        )
    else:
        total = butterfly(payload[size:], ("gx",))
        gx = lax.axis_size("gx")
        up = [(i, i + 1) for i in range(gx - 1)]
        lo = lax.ppermute(whole, "gx", up)
        hi = lax.ppermute(whole, "gx", [(j, i) for i, j in up])
        local = pad_side(local, "gx", 0, width)
    return local, (lo, whole, hi), [total[i] for i in range(count)]


def body(right_side, diagonal, basis_tables, eigenvalues, coarse_blocks, coarse_columns):
    blocks = coarse_blocks.reshape(coarse_blocks.shape[3:])
    columns = coarse_columns.reshape(coarse_columns.shape[3])
    count = blocks.shape[0]
    group = lax.axis_size(("ga", "gz"))
    selector = (columns[:, None] == jnp.arange(group, dtype=jnp.int32)[None, :]).astype(jnp.float32)
    shape = right_side.shape
    wide_pair = jnp.stack([diagonal, right_side])
    table = element_table(blocks, columns, shape)
    for axis, dim in SIDES:
        wide_pair, table = pad_together([wide_pair, table], axis, (dim + 1, dim), (RIM, 1))
    wide_diagonal, wide_residual = wide_pair[0], wide_pair[1]
    inside = inside_grid(shape, RIM)

    def precondition_rim(wide_field, field):
        local = schwarz_part(wide_field, basis_tables, eigenvalues)
        return local, coarse_terms(field, blocks, selector)

    def coarse_on_rim(wholes):
        return spread_rim(coarse_rim(wholes, table, count, group), RIM + 1, shape)

    solution = jnp.zeros_like(right_side)
    for restart in range(CYCLES):
        residual = interior(wide_residual, RIM)
        wide_local, terms = precondition_rim(wide_residual, residual)
        wide_local, wholes, (square,) = reduce_coarse(wide_local, terms, [jnp.sum(residual * residual)])
        initial_norm = jnp.sqrt(square)
        first_vector = residual / initial_norm
        wide_zed = (wide_local + coarse_on_rim(wholes)) / initial_norm
        first_zed = interior(wide_zed, RIM + 1)
        wide_first = operate_rim(wide_zed, wide_diagonal, inside)
        first_image = interior(wide_first, RIM)
        wide_local, terms = precondition_rim(wide_first, first_image)
        wide_local, wholes, (first_proj, image_square) = reduce_coarse(
            wide_local, terms, [jnp.sum(first_vector * first_image), jnp.sum(first_image * first_image)]
        )
        first_len = jnp.sqrt(image_square - first_proj * first_proj)
        second_vector = (first_image - first_proj * first_vector) / first_len
        wide_second_zed = (wide_local + coarse_on_rim(wholes) - first_proj * wide_zed) / first_len
        second_zed = interior(wide_second_zed, RIM + 1)
        wide_second = operate_rim(wide_second_zed, wide_diagonal, inside)
        second_image = interior(wide_second, RIM)
        upper_proj, lower_proj, second_square = reduce_scalars(
            [
                jnp.sum(first_vector * second_image),
                jnp.sum(second_vector * second_image),
                jnp.sum(second_image * second_image),
            ]
        )
        second_len = jnp.sqrt(second_square - upper_proj * upper_proj - lower_proj * lower_proj)
        gram_first = first_proj * first_proj + first_len * first_len
        gram_cross = first_proj * upper_proj + first_len * lower_proj
        gram_second = upper_proj * upper_proj + lower_proj * lower_proj + second_len * second_len
        target_first = initial_norm * first_proj
        target_second = initial_norm * upper_proj
        determinant = gram_first * gram_second - gram_cross * gram_cross
        weight_first = (gram_second * target_first - gram_cross * target_second) / determinant
        weight_second = (gram_first * target_second - gram_cross * target_first) / determinant
        solution = solution + weight_first * first_zed + weight_second * second_zed
        wide_residual = wide_residual - weight_first * wide_first - weight_second * wide_second
    return (solution, interior(wide_residual, RIM))


def solution(mesh):
    in_specs = (
        P("gx", "ga", "gz"),
        P("gx", "ga", "gz"),
        P(),
        P(),
        P("gx", "ga", "gz", None, None, None),
        P("gx", "ga", "gz", None),
    )
    out_specs = (P("gx", "ga", "gz"), P("gx", "ga", "gz"))
    return jax.shard_map(body, mesh=mesh, in_specs=in_specs, out_specs=out_specs, check_vma=False)
```

```python
import functools

import jax
import jax.numpy as jnp
from jax import lax
from jax.sharding import PartitionSpec as P

PTS = 8
RIM = 2
WIDE = 12
CYCLES = 2


PRECISE = lax.Precision.HIGHEST


def pad_side(value, axis, dim, width):
    size, length = (lax.axis_size(axis), value.shape[dim])
    last = lax.slice_in_dim(value, length - width, length, axis=dim)
    leading = lax.slice_in_dim(value, 0, width, axis=dim)
    if size == 2:
        first = lax.axis_index(axis) == 0
        got = lax.ppermute(jnp.where(first, last, leading), axis, [(0, 1), (1, 0)])
        zero = jnp.zeros_like(got)
        before = jnp.where(first, zero, got)
        after = jnp.where(first, got, zero)
    else:
        up = [(i, (i + 1) % size) for i in range(size - 1)]
        down = [(j, i) for i, j in up]
        before = lax.ppermute(last, axis, up)
        after = lax.ppermute(leading, axis, down)
    return jnp.concatenate([before, value, after], axis=dim)


def padded_2(value, sides, width):
    for axis, dim in sides:
        value = pad_side(value, axis, dim, width)
    return value


def pad_together(values, axis, dims, widths):
    lasts, leads = [], []
    for value, dim, width in zip(values, dims, widths):
        length = value.shape[dim]
        lasts.append(lax.slice_in_dim(value, length - width, length, axis=dim))
        leads.append(lax.slice_in_dim(value, 0, width, axis=dim))

    def pack(slabs):
        return jnp.concatenate([slab.reshape(-1) for slab in slabs])

    def unpack(flat):
        pieces, at = [], 0
        for slab in lasts:
            pieces.append(flat[at : at + slab.size].reshape(slab.shape))
            at += slab.size
        return pieces

    size = lax.axis_size(axis)
    if size == 2:
        first = lax.axis_index(axis) == 0
        got = unpack(lax.ppermute(jnp.where(first, pack(lasts), pack(leads)), axis, [(0, 1), (1, 0)]))
        befores = [jnp.where(first, jnp.zeros_like(g), g) for g in got]
        afters = [jnp.where(first, g, jnp.zeros_like(g)) for g in got]
    else:
        up = [(i, (i + 1) % size) for i in range(size - 1)]
        befores = unpack(lax.ppermute(pack(lasts), axis, up))
        afters = unpack(lax.ppermute(pack(leads), axis, [(j, i) for i, j in up]))
    return [
        jnp.concatenate([before, value, after], axis=dim)
        for before, value, after, dim in zip(befores, values, afters, dims)
    ]


SIDES = (("gx", 0), ("ga", 1), ("gz", 2))


def operate_rim(zed, diagonal, inside):
    centre = zed[1:-1, 1:-1, 1:-1]
    beside = zed[2:, 1:-1, 1:-1] + zed[:-2, 1:-1, 1:-1]
    beside = beside + zed[1:-1, 2:, 1:-1] + zed[1:-1, :-2, 1:-1]
    beside = beside + zed[1:-1, 1:-1, 2:] + zed[1:-1, 1:-1, :-2]
    return ((6.0 + diagonal) * centre - beside) * inside


def inside_grid(shape, width):
    result = None
    for axis, dim in SIDES:
        length = shape[dim]
        place = lax.axis_index(axis) * length - width + jnp.arange(length + 2 * width, dtype=jnp.int32)
        line = ((place >= 0) & (place < lax.axis_size(axis) * length)).astype(jnp.float32)
        view = [1, 1, 1]
        view[dim] = length + 2 * width
        line = line.reshape(view)
        result = line if result is None else result * line
    return result


def interior(value, width):
    return value[width:-width, width:-width, width:-width]


def forward_table(count, basis):
    row_index = jnp.arange(PTS * count + 2 * RIM, dtype=jnp.int32)
    element = jnp.arange(count, dtype=jnp.int32)
    offset = jnp.arange(WIDE, dtype=jnp.int32)
    select = (
        row_index[:, None, None] == PTS * element[None, :, None] + offset[None, None, :]
    ).astype(jnp.float32)
    table = jnp.einsum("rcj,jm->rcm", select, basis, precision=PRECISE)
    return table.reshape(PTS * count + 2 * RIM, count * WIDE)


def backward_table(count, basis):
    same = jnp.eye(count, dtype=jnp.float32)
    table = jnp.einsum("cd,im->cmdi", same, basis[RIM : RIM + PTS], precision=PRECISE)
    return table.reshape(count * WIDE, count * PTS)


def schwarz_part(padded, basis_tables, eigenvalues):
    count_x = (padded.shape[0] - 2 * RIM) // PTS
    count_y = (padded.shape[1] - 2 * RIM) // PTS
    count_z = (padded.shape[2] - 2 * RIM) // PTS
    spectral = jnp.einsum(
        "pqr,rc->pqc", padded, forward_table(count_z, basis_tables[2]), precision=PRECISE
    )
    spectral = jnp.einsum(
        "pqc,pa->aqc", spectral, forward_table(count_x, basis_tables[0]), precision=PRECISE
    )
    spectral = jnp.einsum(
        "aqc,qb->abc", spectral, forward_table(count_y, basis_tables[1]), precision=PRECISE
    )
    denominator = (
        jnp.tile(eigenvalues[0], count_x)[:, None, None]
        + jnp.tile(eigenvalues[1], count_y)[None, :, None]
    )
    denominator = denominator + jnp.tile(eigenvalues[2], count_z)[None, None, :]
    spectral = spectral / denominator
    local_part = jnp.einsum(
        "abc,cr->abr", spectral, backward_table(count_z, basis_tables[2]), precision=PRECISE
    )
    local_part = jnp.einsum(
        "abr,ap->pbr", local_part, backward_table(count_x, basis_tables[0]), precision=PRECISE
    )
    local_part = jnp.einsum(
        "pbr,bq->pqr", local_part, backward_table(count_y, basis_tables[1]), precision=PRECISE
    )
    return local_part


def coarse_terms(field, blocks, selector):
    count_x = field.shape[0] // PTS
    count_y = field.shape[1] // PTS
    count_z = field.shape[2] // PTS
    cells = count_x * count_y * count_z
    point = jnp.arange(field.shape[2], dtype=jnp.int32)
    along = (point[:, None] // PTS == jnp.arange(count_z, dtype=jnp.int32)[None, :]).astype(jnp.float32)
    sums = jnp.einsum("pqr,rc->pqc", field, along, precision=PRECISE)
    sums = jnp.sum(sums.reshape(count_x, PTS, count_y, PTS, count_z), axis=(1, 3))
    restricted = sums.reshape(cells) * (1.0 / PTS**3)
    terms = jnp.einsum("kpq,p->kq", blocks, restricted, precision=PRECISE)
    return jnp.einsum("kj,kq->jq", selector, terms, precision=PRECISE)


def element_table(blocks, columns, shape):
    count = blocks.shape[0]
    grid = (shape[0] // PTS, shape[1] // PTS, shape[2] // PTS)
    rows = jnp.transpose(blocks, (1, 0, 2)).reshape(grid + (count * blocks.shape[2],))
    cols = jnp.broadcast_to(columns.astype(jnp.float32), grid + (count,))
    return jnp.concatenate([rows, cols], axis=-1)


def coarse_rim(wholes, table, count, group):
    lo, whole, hi = wholes
    grid = table.shape[:3]
    width = (table.shape[3] - count) // count
    rows = table[..., : count * width].reshape(grid + (count, width))
    cols = table[..., count * width :]
    onehot = (cols[..., None] == jnp.arange(group, dtype=jnp.float32)).astype(jnp.float32)
    stacked = jnp.stack([lo] + [whole] * (grid[0] - 2) + [hi])
    picked = jnp.einsum("abckg,agq->abckq", onehot, stacked, precision=PRECISE)
    return jnp.sum(rows * picked, axis=(3, 4))


def spread_rim(values, width, shape):
    def table(length, count):
        point = jnp.arange(length + 2 * width, dtype=jnp.int32) - width + PTS
        element = jnp.arange(count, dtype=jnp.int32)
        return (point[:, None] // PTS == element[None, :]).astype(jnp.float32)

    grid = values.shape
    out = jnp.einsum("abc,rc->abr", values, table(shape[2], grid[2]), precision=PRECISE)
    out = jnp.einsum("abr,pa->pbr", out, table(shape[0], grid[0]), precision=PRECISE)
    return jnp.einsum("pbr,qb->pqr", out, table(shape[1], grid[1]), precision=PRECISE)


ALL = ("gx", "ga", "gz")


def butterfly_stages(axes):
    stages = []
    for axis in axes:
        size = lax.axis_size(axis)
        if size & (size - 1):
            stages.append(lambda value, axis=axis: lax.psum(value, axis))
            continue
        if size == 4:
            stages.append(functools.partial(sum_of_four, axis=axis))
            continue
        step = 1
        while step < size:
            pairs = [(i, i ^ step) for i in range(size)]
            stages.append(lambda value, axis=axis, pairs=pairs: value + lax.ppermute(value, axis, pairs))
            step *= 2
    return stages


def sum_of_four(value, axis):
    got = [value] + [lax.ppermute(value, axis, [(i, i ^ s) for i in range(4)]) for s in (1, 2, 3)]
    return (got[0] + got[1]) + (got[2] + got[3])


def butterfly(value, axes):
    for stage in butterfly_stages(axes):
        value = stage(value)
    return value


def reduce_scalars(scalars):
    total = butterfly(lax.optimization_barrier(jnp.stack(scalars)), ALL)
    return [total[i] for i in range(len(scalars))]


def fold_four(payload, local, axis, dim, width):
    me = lax.axis_index(axis)
    length = local.shape[dim]
    last = lax.slice_in_dim(local, length - width, length, axis=dim)
    leading = lax.slice_in_dim(local, 0, width, axis=dim)
    even = me % 2 == 0
    count = payload.shape[0]

    def send(slab, step):
        message = jnp.concatenate([payload, slab.reshape(-1)])
        return lax.ppermute(message, axis, [(i, i ^ step) for i in range(4)])

    got_one = send(jnp.where(even, last, leading), 1)
    got_two = lax.ppermute(payload, axis, [(i, i ^ 2) for i in range(4)])
    got_three = send(jnp.where(me == 1, last, leading), 3)
    total = (payload + got_one[:count]) + (got_two + got_three[:count])
    from_one = got_one[count:].reshape(last.shape)
    from_three = got_three[count:].reshape(last.shape)
    zero = jnp.zeros_like(from_one)
    before = jnp.where(even, jnp.where(me == 2, from_three, zero), from_one)
    after = jnp.where(even, from_one, jnp.where(me == 1, from_three, zero))
    return total, jnp.concatenate([before, local, after], axis=dim)


def reduce_coarse(local, buffer, scalars):
    count = len(scalars)
    width = RIM + 1
    payload = jnp.concatenate([buffer.reshape(-1), jnp.stack(scalars)])
    local, payload = lax.optimization_barrier((local, payload))
    for axis, dim in (("ga", 1), ("gz", 2)):
        if lax.axis_size(axis) == 4:
            payload, local = fold_four(payload, local, axis, dim, width)
        else:
            payload = butterfly(payload, (axis,))
            local = pad_side(local, axis, dim, width)
        local, payload = lax.optimization_barrier((local, payload))
    size = payload.shape[0] - count
    whole = payload[:size].reshape(buffer.shape)
    if lax.axis_size("gx") == 2:
        first = lax.axis_index("gx") == 0
        length = local.shape[0]
        slab = jnp.where(first, local[length - width :], local[:width])
        message = jnp.concatenate([payload, slab.reshape(-1)])
        got = lax.ppermute(message, "gx", [(0, 1), (1, 0)])
        total = payload[size:] + got[size : size + count]
        other = got[:size].reshape(buffer.shape)
        beside = got[size + count :].reshape(slab.shape)
        zero = jnp.zeros_like(other)
        lo, hi = jnp.where(first, zero, other), jnp.where(first, other, zero)
        flat = jnp.zeros_like(beside)
        local = jnp.concatenate(
            [jnp.where(first, flat, beside), local, jnp.where(first, beside, flat)], axis=0
        )
    else:
        total = butterfly(payload[size:], ("gx",))
        gx = lax.axis_size("gx")
        up = [(i, i + 1) for i in range(gx - 1)]
        lo = lax.ppermute(whole, "gx", up)
        hi = lax.ppermute(whole, "gx", [(j, i) for i, j in up])
        local = pad_side(local, "gx", 0, width)
    return local, (lo, whole, hi), [total[i] for i in range(count)]


def body(right_side, diagonal, basis_tables, eigenvalues, coarse_blocks, coarse_columns):
    blocks = coarse_blocks.reshape(coarse_blocks.shape[3:])
    columns = coarse_columns.reshape(coarse_columns.shape[3])
    count = blocks.shape[0]
    group = lax.axis_size(("ga", "gz"))
    selector = (columns[:, None] == jnp.arange(group, dtype=jnp.int32)[None, :]).astype(jnp.float32)
    shape = right_side.shape
    wide_pair = jnp.stack([diagonal, right_side])
    table = element_table(blocks, columns, shape)
    for axis, dim in SIDES:
        wide_pair, table = pad_together([wide_pair, table], axis, (dim + 1, dim), (RIM, 1))
    wide_diagonal, wide_residual = wide_pair[0], wide_pair[1]
    inside = inside_grid(shape, RIM)

    def precondition_rim(wide_field, field):
        local = schwarz_part(wide_field, basis_tables, eigenvalues)
        return local, coarse_terms(field, blocks, selector)

    def coarse_on_rim(wholes):
        return spread_rim(coarse_rim(wholes, table, count, group), RIM + 1, shape)

    solution = jnp.zeros_like(right_side)
    residual = interior(wide_residual, RIM)
    wide_local, terms = precondition_rim(wide_residual, residual)
    wide_local, wholes, (square,) = reduce_coarse(wide_local, terms, [jnp.sum(residual * residual)])
    for restart in range(CYCLES):
        residual = interior(wide_residual, RIM)
        initial_norm = jnp.sqrt(square)
        first_vector = residual / initial_norm
        wide_local_r, wholes_r = wide_local, wholes
        wide_zed = (wide_local_r + coarse_on_rim(wholes_r)) / initial_norm
        first_zed = interior(wide_zed, RIM + 1)
        wide_first = operate_rim(wide_zed, wide_diagonal, inside)
        first_image = interior(wide_first, RIM)
        wide_local, terms = precondition_rim(wide_first, first_image)
        wide_local_w, wholes_w, (first_proj, image_square) = reduce_coarse(
            wide_local, terms, [jnp.sum(first_vector * first_image), jnp.sum(first_image * first_image)]
        )
        first_len = jnp.sqrt(image_square - first_proj * first_proj)
        second_vector = (first_image - first_proj * first_vector) / first_len
        wide_second_zed = (wide_local_w + coarse_on_rim(wholes_w) - first_proj * wide_zed) / first_len
        second_zed = interior(wide_second_zed, RIM + 1)
        wide_second = operate_rim(wide_second_zed, wide_diagonal, inside)
        second_image = interior(wide_second, RIM)
        products = [
            jnp.sum(first_vector * second_image),
            jnp.sum(second_vector * second_image),
            jnp.sum(second_image * second_image),
        ]
        last = restart == CYCLES - 1
        if last:
            upper_proj, lower_proj, second_square = reduce_scalars(products)
        else:
            wide_local, terms = precondition_rim(wide_second, second_image)
            wide_local_s, wholes_s, (upper_proj, lower_proj, second_square, cross) = reduce_coarse(
                wide_local, terms, products + [jnp.sum(first_image * second_image)]
            )
        second_len = jnp.sqrt(second_square - upper_proj * upper_proj - lower_proj * lower_proj)
        gram_first = first_proj * first_proj + first_len * first_len
        gram_cross = first_proj * upper_proj + first_len * lower_proj
        gram_second = upper_proj * upper_proj + lower_proj * lower_proj + second_len * second_len
        target_first = initial_norm * first_proj
        target_second = initial_norm * upper_proj
        determinant = gram_first * gram_second - gram_cross * gram_cross
        weight_first = (gram_second * target_first - gram_cross * target_second) / determinant
        weight_second = (gram_first * target_second - gram_cross * target_first) / determinant
        solution = solution + weight_first * first_zed + weight_second * second_zed
        wide_residual = wide_residual - weight_first * wide_first - weight_second * wide_second
        if not last:
            wide_local = wide_local_r - weight_first * wide_local_w - weight_second * wide_local_s
            wholes = tuple(
                r - weight_first * w - weight_second * s for r, w, s in zip(wholes_r, wholes_w, wholes_s)
            )
            square = (
                square
                - 2.0 * weight_first * target_first
                - 2.0 * weight_second * target_second
                + weight_first * weight_first * image_square
                + 2.0 * weight_first * weight_second * cross
                + weight_second * weight_second * second_square
            )
    return (solution, interior(wide_residual, RIM))


def solution(mesh):
    in_specs = (
        P("gx", "ga", "gz"),
        P("gx", "ga", "gz"),
        P(),
        P(),
        P("gx", "ga", "gz", None, None, None),
        P("gx", "ga", "gz", None),
    )
    out_specs = (P("gx", "ga", "gz"), P("gx", "ga", "gz"))
    return jax.shard_map(body, mesh=mesh, in_specs=in_specs, out_specs=out_specs, check_vma=False)
```

```python
import functools

import jax
import jax.numpy as jnp
from jax import lax
from jax.sharding import PartitionSpec as P

PTS = 8
RIM = 2
WIDE = 12
CYCLES = 2


PRECISE = lax.Precision.HIGHEST
TRANSFORM = lax.Precision.HIGH


def pad_side(value, axis, dim, width):
    size, length = (lax.axis_size(axis), value.shape[dim])
    last = lax.slice_in_dim(value, length - width, length, axis=dim)
    leading = lax.slice_in_dim(value, 0, width, axis=dim)
    if size == 2:
        first = lax.axis_index(axis) == 0
        got = lax.ppermute(jnp.where(first, last, leading), axis, [(0, 1), (1, 0)])
        zero = jnp.zeros_like(got)
        before = jnp.where(first, zero, got)
        after = jnp.where(first, got, zero)
    else:
        up = [(i, (i + 1) % size) for i in range(size - 1)]
        down = [(j, i) for i, j in up]
        before = lax.ppermute(last, axis, up)
        after = lax.ppermute(leading, axis, down)
    return jnp.concatenate([before, value, after], axis=dim)


def padded_2(value, sides, width):
    for axis, dim in sides:
        value = pad_side(value, axis, dim, width)
    return value


def pad_together(values, axis, dims, widths):
    lasts, leads = [], []
    for value, dim, width in zip(values, dims, widths):
        length = value.shape[dim]
        lasts.append(lax.slice_in_dim(value, length - width, length, axis=dim))
        leads.append(lax.slice_in_dim(value, 0, width, axis=dim))

    def pack(slabs):
        return jnp.concatenate([slab.reshape(-1) for slab in slabs])

    def unpack(flat):
        pieces, at = [], 0
        for slab in lasts:
            pieces.append(flat[at : at + slab.size].reshape(slab.shape))
            at += slab.size
        return pieces

    size = lax.axis_size(axis)
    if size == 2:
        first = lax.axis_index(axis) == 0
        got = unpack(lax.ppermute(jnp.where(first, pack(lasts), pack(leads)), axis, [(0, 1), (1, 0)]))
        befores = [jnp.where(first, jnp.zeros_like(g), g) for g in got]
        afters = [jnp.where(first, g, jnp.zeros_like(g)) for g in got]
    else:
        up = [(i, (i + 1) % size) for i in range(size - 1)]
        befores = unpack(lax.ppermute(pack(lasts), axis, up))
        afters = unpack(lax.ppermute(pack(leads), axis, [(j, i) for i, j in up]))
    return [
        jnp.concatenate([before, value, after], axis=dim)
        for before, value, after, dim in zip(befores, values, afters, dims)
    ]


SIDES = (("gx", 0), ("ga", 1), ("gz", 2))


def operate_rim(zed, diagonal, inside):
    centre = zed[1:-1, 1:-1, 1:-1]
    beside = zed[2:, 1:-1, 1:-1] + zed[:-2, 1:-1, 1:-1]
    beside = beside + zed[1:-1, 2:, 1:-1] + zed[1:-1, :-2, 1:-1]
    beside = beside + zed[1:-1, 1:-1, 2:] + zed[1:-1, 1:-1, :-2]
    return ((6.0 + diagonal) * centre - beside) * inside


def inside_grid(shape, width):
    result = None
    for axis, dim in SIDES:
        length = shape[dim]
        place = lax.axis_index(axis) * length - width + jnp.arange(length + 2 * width, dtype=jnp.int32)
        line = ((place >= 0) & (place < lax.axis_size(axis) * length)).astype(jnp.float32)
        view = [1, 1, 1]
        view[dim] = length + 2 * width
        line = line.reshape(view)
        result = line if result is None else result * line
    return result


def interior(value, width):
    return value[width:-width, width:-width, width:-width]


def forward_table(count, basis):
    row_index = jnp.arange(PTS * count + 2 * RIM, dtype=jnp.int32)
    element = jnp.arange(count, dtype=jnp.int32)
    offset = jnp.arange(WIDE, dtype=jnp.int32)
    select = (
        row_index[:, None, None] == PTS * element[None, :, None] + offset[None, None, :]
    ).astype(jnp.float32)
    table = jnp.einsum("rcj,jm->rcm", select, basis, precision=PRECISE)
    return table.reshape(PTS * count + 2 * RIM, count * WIDE)


def backward_table(count, basis):
    same = jnp.eye(count, dtype=jnp.float32)
    table = jnp.einsum("cd,im->cmdi", same, basis[RIM : RIM + PTS], precision=PRECISE)
    return table.reshape(count * WIDE, count * PTS)


def schwarz_part(padded, basis_tables, eigenvalues):
    count_x = (padded.shape[0] - 2 * RIM) // PTS
    count_y = (padded.shape[1] - 2 * RIM) // PTS
    count_z = (padded.shape[2] - 2 * RIM) // PTS
    spectral = jnp.einsum(
        "pqr,rc->pqc", padded, forward_table(count_z, basis_tables[2]), precision=TRANSFORM
    )
    spectral = jnp.einsum(
        "pqc,pa->aqc", spectral, forward_table(count_x, basis_tables[0]), precision=TRANSFORM
    )
    spectral = jnp.einsum(
        "aqc,qb->abc", spectral, forward_table(count_y, basis_tables[1]), precision=TRANSFORM
    )
    denominator = (
        jnp.tile(eigenvalues[0], count_x)[:, None, None]
        + jnp.tile(eigenvalues[1], count_y)[None, :, None]
    )
    denominator = denominator + jnp.tile(eigenvalues[2], count_z)[None, None, :]
    spectral = spectral / denominator
    local_part = jnp.einsum(
        "abc,cr->abr", spectral, backward_table(count_z, basis_tables[2]), precision=TRANSFORM
    )
    local_part = jnp.einsum(
        "abr,ap->pbr", local_part, backward_table(count_x, basis_tables[0]), precision=TRANSFORM
    )
    local_part = jnp.einsum(
        "pbr,bq->pqr", local_part, backward_table(count_y, basis_tables[1]), precision=TRANSFORM
    )
    return local_part


def coarse_terms(field, blocks, selector):
    count_x = field.shape[0] // PTS
    count_y = field.shape[1] // PTS
    count_z = field.shape[2] // PTS
    cells = count_x * count_y * count_z
    point = jnp.arange(field.shape[2], dtype=jnp.int32)
    along = (point[:, None] // PTS == jnp.arange(count_z, dtype=jnp.int32)[None, :]).astype(jnp.float32)
    sums = jnp.einsum("pqr,rc->pqc", field, along, precision=PRECISE)
    sums = jnp.sum(sums.reshape(count_x, PTS, count_y, PTS, count_z), axis=(1, 3))
    restricted = sums.reshape(cells) * (1.0 / PTS**3)
    terms = jnp.einsum("kpq,p->kq", blocks, restricted, precision=PRECISE)
    return jnp.einsum("kj,kq->jq", selector, terms, precision=PRECISE)


def element_table(blocks, columns, shape):
    count = blocks.shape[0]
    grid = (shape[0] // PTS, shape[1] // PTS, shape[2] // PTS)
    rows = jnp.transpose(blocks, (1, 0, 2)).reshape(grid + (count * blocks.shape[2],))
    cols = jnp.broadcast_to(columns.astype(jnp.float32), grid + (count,))
    return jnp.concatenate([rows, cols], axis=-1)


def coarse_rim(wholes, table, count, group):
    lo, whole, hi = wholes
    grid = table.shape[:3]
    width = (table.shape[3] - count) // count
    rows = table[..., : count * width].reshape(grid + (count, width))
    cols = table[..., count * width :]
    onehot = (cols[..., None] == jnp.arange(group, dtype=jnp.float32)).astype(jnp.float32)
    stacked = jnp.stack([lo] + [whole] * (grid[0] - 2) + [hi])
    picked = jnp.einsum("abckg,agq->abckq", onehot, stacked, precision=PRECISE)
    return jnp.sum(rows * picked, axis=(3, 4))


def spread_rim(values, width, shape):
    def table(length, count):
        point = jnp.arange(length + 2 * width, dtype=jnp.int32) - width + PTS
        element = jnp.arange(count, dtype=jnp.int32)
        return (point[:, None] // PTS == element[None, :]).astype(jnp.float32)

    grid = values.shape
    out = jnp.einsum("abc,rc->abr", values, table(shape[2], grid[2]), precision=PRECISE)
    out = jnp.einsum("abr,pa->pbr", out, table(shape[0], grid[0]), precision=PRECISE)
    return jnp.einsum("pbr,qb->pqr", out, table(shape[1], grid[1]), precision=PRECISE)


ALL = ("gx", "ga", "gz")


def butterfly_stages(axes):
    stages = []
    for axis in axes:
        size = lax.axis_size(axis)
        if size & (size - 1):
            stages.append(lambda value, axis=axis: lax.psum(value, axis))
            continue
        if size == 4:
            stages.append(functools.partial(sum_of_four, axis=axis))
            continue
        step = 1
        while step < size:
            pairs = [(i, i ^ step) for i in range(size)]
            stages.append(lambda value, axis=axis, pairs=pairs: value + lax.ppermute(value, axis, pairs))
            step *= 2
    return stages


def sum_of_four(value, axis):
    got = [value] + [lax.ppermute(value, axis, [(i, i ^ s) for i in range(4)]) for s in (1, 2, 3)]
    return (got[0] + got[1]) + (got[2] + got[3])


def butterfly(value, axes):
    for stage in butterfly_stages(axes):
        value = stage(value)
    return value


def reduce_scalars(scalars):
    total = butterfly(lax.optimization_barrier(jnp.stack(scalars)), ALL)
    return [total[i] for i in range(len(scalars))]


def fold_four(payload, local, axis, dim, width):
    me = lax.axis_index(axis)
    length = local.shape[dim]
    last = lax.slice_in_dim(local, length - width, length, axis=dim)
    leading = lax.slice_in_dim(local, 0, width, axis=dim)
    even = me % 2 == 0
    count = payload.shape[0]

    def send(slab, step):
        message = jnp.concatenate([payload, slab.reshape(-1)])
        return lax.ppermute(message, axis, [(i, i ^ step) for i in range(4)])

    got_one = send(jnp.where(even, last, leading), 1)
    got_two = lax.ppermute(payload, axis, [(i, i ^ 2) for i in range(4)])
    got_three = send(jnp.where(me == 1, last, leading), 3)
    total = (payload + got_one[:count]) + (got_two + got_three[:count])
    from_one = got_one[count:].reshape(last.shape)
    from_three = got_three[count:].reshape(last.shape)
    zero = jnp.zeros_like(from_one)
    before = jnp.where(even, jnp.where(me == 2, from_three, zero), from_one)
    after = jnp.where(even, from_one, jnp.where(me == 1, from_three, zero))
    return total, jnp.concatenate([before, local, after], axis=dim)


def reduce_coarse(local, buffer, scalars):
    count = len(scalars)
    width = RIM + 1
    payload = jnp.concatenate([buffer.reshape(-1), jnp.stack(scalars)])
    local, payload = lax.optimization_barrier((local, payload))
    for axis, dim in (("ga", 1), ("gz", 2)):
        if lax.axis_size(axis) == 4:
            payload, local = fold_four(payload, local, axis, dim, width)
        else:
            payload = butterfly(payload, (axis,))
            local = pad_side(local, axis, dim, width)
        local, payload = lax.optimization_barrier((local, payload))
    size = payload.shape[0] - count
    whole = payload[:size].reshape(buffer.shape)
    if lax.axis_size("gx") == 2:
        first = lax.axis_index("gx") == 0
        length = local.shape[0]
        slab = jnp.where(first, local[length - width :], local[:width])
        message = jnp.concatenate([payload, slab.reshape(-1)])
        got = lax.ppermute(message, "gx", [(0, 1), (1, 0)])
        total = payload[size:] + got[size : size + count]
        other = got[:size].reshape(buffer.shape)
        beside = got[size + count :].reshape(slab.shape)
        zero = jnp.zeros_like(other)
        lo, hi = jnp.where(first, zero, other), jnp.where(first, other, zero)
        flat = jnp.zeros_like(beside)
        local = jnp.concatenate(
            [jnp.where(first, flat, beside), local, jnp.where(first, beside, flat)], axis=0
        )
    else:
        total = butterfly(payload[size:], ("gx",))
        gx = lax.axis_size("gx")
        up = [(i, i + 1) for i in range(gx - 1)]
        lo = lax.ppermute(whole, "gx", up)
        hi = lax.ppermute(whole, "gx", [(j, i) for i, j in up])
        local = pad_side(local, "gx", 0, width)
    return local, (lo, whole, hi), [total[i] for i in range(count)]


def body(right_side, diagonal, basis_tables, eigenvalues, coarse_blocks, coarse_columns):
    blocks = coarse_blocks.reshape(coarse_blocks.shape[3:])
    columns = coarse_columns.reshape(coarse_columns.shape[3])
    count = blocks.shape[0]
    group = lax.axis_size(("ga", "gz"))
    selector = (columns[:, None] == jnp.arange(group, dtype=jnp.int32)[None, :]).astype(jnp.float32)
    shape = right_side.shape
    wide_pair = jnp.stack([diagonal, right_side])
    table = element_table(blocks, columns, shape)
    for axis, dim in SIDES:
        wide_pair, table = pad_together([wide_pair, table], axis, (dim + 1, dim), (RIM, 1))
    wide_diagonal, wide_residual = wide_pair[0], wide_pair[1]
    inside = inside_grid(shape, RIM)

    def precondition_rim(wide_field, field):
        local = schwarz_part(wide_field, basis_tables, eigenvalues)
        return local, coarse_terms(field, blocks, selector)

    def coarse_on_rim(wholes):
        return spread_rim(coarse_rim(wholes, table, count, group), RIM + 1, shape)

    solution = jnp.zeros_like(right_side)
    residual = interior(wide_residual, RIM)
    wide_local, terms = precondition_rim(wide_residual, residual)
    wide_local, wholes, (square,) = reduce_coarse(wide_local, terms, [jnp.sum(residual * residual)])
    for restart in range(CYCLES):
        residual = interior(wide_residual, RIM)
        initial_norm = jnp.sqrt(square)
        first_vector = residual / initial_norm
        wide_local_r, wholes_r = wide_local, wholes
        wide_zed = (wide_local_r + coarse_on_rim(wholes_r)) / initial_norm
        first_zed = interior(wide_zed, RIM + 1)
        wide_first = operate_rim(wide_zed, wide_diagonal, inside)
        first_image = interior(wide_first, RIM)
        wide_local, terms = precondition_rim(wide_first, first_image)
        wide_local_w, wholes_w, (first_proj, image_square) = reduce_coarse(
            wide_local, terms, [jnp.sum(first_vector * first_image), jnp.sum(first_image * first_image)]
        )
        first_len = jnp.sqrt(image_square - first_proj * first_proj)
        second_vector = (first_image - first_proj * first_vector) / first_len
        wide_second_zed = (wide_local_w + coarse_on_rim(wholes_w) - first_proj * wide_zed) / first_len
        second_zed = interior(wide_second_zed, RIM + 1)
        wide_second = operate_rim(wide_second_zed, wide_diagonal, inside)
        second_image = interior(wide_second, RIM)
        products = [
            jnp.sum(first_vector * second_image),
            jnp.sum(second_vector * second_image),
            jnp.sum(second_image * second_image),
        ]
        last = restart == CYCLES - 1
        if last:
            upper_proj, lower_proj, second_square = reduce_scalars(products)
        else:
            wide_local, terms = precondition_rim(wide_second, second_image)
            wide_local_s, wholes_s, (upper_proj, lower_proj, second_square, cross) = reduce_coarse(
                wide_local, terms, products + [jnp.sum(first_image * second_image)]
            )
        second_len = jnp.sqrt(second_square - upper_proj * upper_proj - lower_proj * lower_proj)
        gram_first = first_proj * first_proj + first_len * first_len
        gram_cross = first_proj * upper_proj + first_len * lower_proj
        gram_second = upper_proj * upper_proj + lower_proj * lower_proj + second_len * second_len
        target_first = initial_norm * first_proj
        target_second = initial_norm * upper_proj
        determinant = gram_first * gram_second - gram_cross * gram_cross
        weight_first = (gram_second * target_first - gram_cross * target_second) / determinant
        weight_second = (gram_first * target_second - gram_cross * target_first) / determinant
        solution = solution + weight_first * first_zed + weight_second * second_zed
        wide_residual = wide_residual - weight_first * wide_first - weight_second * wide_second
        if not last:
            wide_local = wide_local_r - weight_first * wide_local_w - weight_second * wide_local_s
            wholes = tuple(
                r - weight_first * w - weight_second * s for r, w, s in zip(wholes_r, wholes_w, wholes_s)
            )
            square = (
                square
                - 2.0 * weight_first * target_first
                - 2.0 * weight_second * target_second
                + weight_first * weight_first * image_square
                + 2.0 * weight_first * weight_second * cross
                + weight_second * weight_second * second_square
            )
    return (solution, interior(wide_residual, RIM))


def solution(mesh):
    in_specs = (
        P("gx", "ga", "gz"),
        P("gx", "ga", "gz"),
        P(),
        P(),
        P("gx", "ga", "gz", None, None, None),
        P("gx", "ga", "gz", None),
    )
    out_specs = (P("gx", "ga", "gz"), P("gx", "ga", "gz"))
    return jax.shard_map(body, mesh=mesh, in_specs=in_specs, out_specs=out_specs, check_vma=False)
```

```python
import functools

import jax
import jax.numpy as jnp
from jax import lax
from jax.sharding import PartitionSpec as P

PTS = 8
RIM = 2
WIDE = 12
CYCLES = 2


PRECISE = lax.Precision.HIGHEST
TRANSFORM = lax.Precision.HIGH


def pad_side(value, axis, dim, width):
    size, length = (lax.axis_size(axis), value.shape[dim])
    last = lax.slice_in_dim(value, length - width, length, axis=dim)
    leading = lax.slice_in_dim(value, 0, width, axis=dim)
    if size == 2:
        first = lax.axis_index(axis) == 0
        got = lax.ppermute(jnp.where(first, last, leading), axis, [(0, 1), (1, 0)])
        zero = jnp.zeros_like(got)
        before = jnp.where(first, zero, got)
        after = jnp.where(first, got, zero)
    else:
        up = [(i, (i + 1) % size) for i in range(size - 1)]
        down = [(j, i) for i, j in up]
        before = lax.ppermute(last, axis, up)
        after = lax.ppermute(leading, axis, down)
    return jnp.concatenate([before, value, after], axis=dim)


def padded_2(value, sides, width):
    for axis, dim in sides:
        value = pad_side(value, axis, dim, width)
    return value


def pad_together(values, axis, dims, widths):
    lasts, leads = [], []
    for value, dim, width in zip(values, dims, widths):
        length = value.shape[dim]
        lasts.append(lax.slice_in_dim(value, length - width, length, axis=dim))
        leads.append(lax.slice_in_dim(value, 0, width, axis=dim))

    def pack(slabs):
        return jnp.concatenate([slab.reshape(-1) for slab in slabs])

    def unpack(flat):
        pieces, at = [], 0
        for slab in lasts:
            pieces.append(flat[at : at + slab.size].reshape(slab.shape))
            at += slab.size
        return pieces

    size = lax.axis_size(axis)
    if size == 2:
        first = lax.axis_index(axis) == 0
        got = unpack(lax.ppermute(jnp.where(first, pack(lasts), pack(leads)), axis, [(0, 1), (1, 0)]))
        befores = [jnp.where(first, jnp.zeros_like(g), g) for g in got]
        afters = [jnp.where(first, g, jnp.zeros_like(g)) for g in got]
    else:
        up = [(i, (i + 1) % size) for i in range(size - 1)]
        befores = unpack(lax.ppermute(pack(lasts), axis, up))
        afters = unpack(lax.ppermute(pack(leads), axis, [(j, i) for i, j in up]))
    return [
        jnp.concatenate([before, value, after], axis=dim)
        for before, value, after, dim in zip(befores, values, afters, dims)
    ]


SIDES = (("gx", 0), ("ga", 1), ("gz", 2))


def operate_rim(zed, diagonal, inside):
    centre = zed[1:-1, 1:-1, 1:-1]
    beside = zed[2:, 1:-1, 1:-1] + zed[:-2, 1:-1, 1:-1]
    beside = beside + zed[1:-1, 2:, 1:-1] + zed[1:-1, :-2, 1:-1]
    beside = beside + zed[1:-1, 1:-1, 2:] + zed[1:-1, 1:-1, :-2]
    return ((6.0 + diagonal) * centre - beside) * inside


def inside_grid(shape, width):
    result = None
    for axis, dim in SIDES:
        length = shape[dim]
        place = lax.axis_index(axis) * length - width + jnp.arange(length + 2 * width, dtype=jnp.int32)
        line = ((place >= 0) & (place < lax.axis_size(axis) * length)).astype(jnp.float32)
        view = [1, 1, 1]
        view[dim] = length + 2 * width
        line = line.reshape(view)
        result = line if result is None else result * line
    return result


def interior(value, width):
    return value[width:-width, width:-width, width:-width]


def forward_table(count, basis):
    row_index = jnp.arange(PTS * count + 2 * RIM, dtype=jnp.int32)
    element = jnp.arange(count, dtype=jnp.int32)
    offset = jnp.arange(WIDE, dtype=jnp.int32)
    select = (
        row_index[:, None, None] == PTS * element[None, :, None] + offset[None, None, :]
    ).astype(jnp.float32)
    table = jnp.einsum("rcj,jm->rcm", select, basis, precision=PRECISE)
    return table.reshape(PTS * count + 2 * RIM, count * WIDE)


def backward_table(count, basis):
    same = jnp.eye(count, dtype=jnp.float32)
    table = jnp.einsum("cd,im->cmdi", same, basis[RIM : RIM + PTS], precision=PRECISE)
    return table.reshape(count * WIDE, count * PTS)


def schwarz_part(padded, basis_tables, eigenvalues):
    count_x = (padded.shape[0] - 2 * RIM) // PTS
    count_y = (padded.shape[1] - 2 * RIM) // PTS
    count_z = (padded.shape[2] - 2 * RIM) // PTS
    spectral = jnp.einsum(
        "pqr,rc->pqc", padded, forward_table(count_z, basis_tables[2]), precision=TRANSFORM
    )
    spectral = jnp.einsum(
        "pqc,pa->aqc", spectral, forward_table(count_x, basis_tables[0]), precision=TRANSFORM
    )
    spectral = jnp.einsum(
        "aqc,qb->abc", spectral, forward_table(count_y, basis_tables[1]), precision=TRANSFORM
    )
    denominator = (
        jnp.tile(eigenvalues[0], count_x)[:, None, None]
        + jnp.tile(eigenvalues[1], count_y)[None, :, None]
    )
    denominator = denominator + jnp.tile(eigenvalues[2], count_z)[None, None, :]
    spectral = spectral / denominator
    local_part = jnp.einsum(
        "abc,cr->abr", spectral, backward_table(count_z, basis_tables[2]), precision=TRANSFORM
    )
    local_part = jnp.einsum(
        "abr,ap->pbr", local_part, backward_table(count_x, basis_tables[0]), precision=TRANSFORM
    )
    local_part = jnp.einsum(
        "pbr,bq->pqr", local_part, backward_table(count_y, basis_tables[1]), precision=TRANSFORM
    )
    return local_part


def coarse_terms(field, blocks, selector):
    count_x = field.shape[0] // PTS
    count_y = field.shape[1] // PTS
    count_z = field.shape[2] // PTS
    cells = count_x * count_y * count_z
    point = jnp.arange(field.shape[2], dtype=jnp.int32)
    along = (point[:, None] // PTS == jnp.arange(count_z, dtype=jnp.int32)[None, :]).astype(jnp.float32)
    sums = jnp.einsum("pqr,rc->pqc", field, along, precision=PRECISE)
    sums = jnp.sum(sums.reshape(count_x, PTS, count_y, PTS, count_z), axis=(1, 3))
    restricted = sums.reshape(cells) * (1.0 / PTS**3)
    terms = jnp.einsum("kpq,p->kq", blocks, restricted, precision=PRECISE)
    return jnp.einsum("kj,kq->jq", selector, terms, precision=PRECISE)


def element_table(blocks, columns, shape):
    count = blocks.shape[0]
    grid = (shape[0] // PTS, shape[1] // PTS, shape[2] // PTS)
    rows = jnp.transpose(blocks, (1, 0, 2)).reshape(grid + (count * blocks.shape[2],))
    cols = jnp.broadcast_to(columns.astype(jnp.float32), grid + (count,))
    return jnp.concatenate([rows, cols], axis=-1)


def coarse_rim(wholes, table, count, group):
    lo, whole, hi = wholes
    grid = table.shape[:3]
    width = (table.shape[3] - count) // count
    rows = table[..., : count * width].reshape(grid + (count, width))
    cols = table[..., count * width :]
    onehot = (cols[..., None] == jnp.arange(group, dtype=jnp.float32)).astype(jnp.float32)
    stacked = jnp.stack([lo] + [whole] * (grid[0] - 2) + [hi])
    picked = jnp.einsum("abckg,agq->abckq", onehot, stacked, precision=PRECISE)
    return jnp.sum(rows * picked, axis=(3, 4))


def spread_rim(values, width, shape):
    def table(length, count):
        point = jnp.arange(length + 2 * width, dtype=jnp.int32) - width + PTS
        element = jnp.arange(count, dtype=jnp.int32)
        return (point[:, None] // PTS == element[None, :]).astype(jnp.float32)

    grid = values.shape
    out = jnp.einsum("abc,rc->abr", values, table(shape[2], grid[2]), precision=PRECISE)
    out = jnp.einsum("abr,pa->pbr", out, table(shape[0], grid[0]), precision=PRECISE)
    return jnp.einsum("pbr,qb->pqr", out, table(shape[1], grid[1]), precision=PRECISE)


ALL = ("gx", "ga", "gz")


def butterfly_stages(axes):
    stages = []
    for axis in axes:
        size = lax.axis_size(axis)
        if size & (size - 1):
            stages.append(lambda value, axis=axis: lax.psum(value, axis))
            continue
        if size == 4:
            stages.append(functools.partial(sum_of_four, axis=axis))
            continue
        step = 1
        while step < size:
            pairs = [(i, i ^ step) for i in range(size)]
            stages.append(lambda value, axis=axis, pairs=pairs: value + lax.ppermute(value, axis, pairs))
            step *= 2
    return stages


def sum_of_four(value, axis):
    got = [value] + [lax.ppermute(value, axis, [(i, i ^ s) for i in range(4)]) for s in (1, 2, 3)]
    return (got[0] + got[1]) + (got[2] + got[3])


def butterfly(value, axes):
    for stage in butterfly_stages(axes):
        value = stage(value)
    return value


def lane_sums(a, b):
    return jnp.sum((a * b).reshape(-1, a.shape[-1]), axis=0)


def finish(total, count):
    return [jnp.sum(part) for part in jnp.split(total, count)]


def reduce_scalars(scalars):
    total = butterfly(lax.optimization_barrier(jnp.concatenate(scalars)), ALL)
    return finish(total, len(scalars))


def fold_four(payload, local, axis, dim, width):
    me = lax.axis_index(axis)
    length = local.shape[dim]
    last = lax.slice_in_dim(local, length - width, length, axis=dim)
    leading = lax.slice_in_dim(local, 0, width, axis=dim)
    even = me % 2 == 0
    count = payload.shape[0]

    def send(slab, step):
        message = jnp.concatenate([payload, slab.reshape(-1)])
        return lax.ppermute(message, axis, [(i, i ^ step) for i in range(4)])

    got_one = send(jnp.where(even, last, leading), 1)
    got_two = lax.ppermute(payload, axis, [(i, i ^ 2) for i in range(4)])
    got_three = send(jnp.where(me == 1, last, leading), 3)
    total = (payload + got_one[:count]) + (got_two + got_three[:count])
    from_one = got_one[count:].reshape(last.shape)
    from_three = got_three[count:].reshape(last.shape)
    zero = jnp.zeros_like(from_one)
    before = jnp.where(even, jnp.where(me == 2, from_three, zero), from_one)
    after = jnp.where(even, from_one, jnp.where(me == 1, from_three, zero))
    return total, jnp.concatenate([before, local, after], axis=dim)


def reduce_coarse(local, buffer, scalars):
    count = sum(part.shape[0] for part in scalars)
    width = RIM + 1
    payload = jnp.concatenate([buffer.reshape(-1)] + list(scalars))
    local, payload = lax.optimization_barrier((local, payload))
    for axis, dim in (("ga", 1), ("gz", 2)):
        if lax.axis_size(axis) == 4:
            payload, local = fold_four(payload, local, axis, dim, width)
        else:
            payload = butterfly(payload, (axis,))
            local = pad_side(local, axis, dim, width)
        local, payload = lax.optimization_barrier((local, payload))
    size = payload.shape[0] - count
    whole = payload[:size].reshape(buffer.shape)
    if lax.axis_size("gx") == 2:
        first = lax.axis_index("gx") == 0
        length = local.shape[0]
        slab = jnp.where(first, local[length - width :], local[:width])
        message = jnp.concatenate([payload, slab.reshape(-1)])
        got = lax.ppermute(message, "gx", [(0, 1), (1, 0)])
        total = payload[size:] + got[size : size + count]
        other = got[:size].reshape(buffer.shape)
        beside = got[size + count :].reshape(slab.shape)
        zero = jnp.zeros_like(other)
        lo, hi = jnp.where(first, zero, other), jnp.where(first, other, zero)
        flat = jnp.zeros_like(beside)
        local = jnp.concatenate(
            [jnp.where(first, flat, beside), local, jnp.where(first, beside, flat)], axis=0
        )
    else:
        total = butterfly(payload[size:], ("gx",))
        gx = lax.axis_size("gx")
        up = [(i, i + 1) for i in range(gx - 1)]
        lo = lax.ppermute(whole, "gx", up)
        hi = lax.ppermute(whole, "gx", [(j, i) for i, j in up])
        local = pad_side(local, "gx", 0, width)
    return local, (lo, whole, hi), finish(total, len(scalars))


def body(right_side, diagonal, basis_tables, eigenvalues, coarse_blocks, coarse_columns):
    blocks = coarse_blocks.reshape(coarse_blocks.shape[3:])
    columns = coarse_columns.reshape(coarse_columns.shape[3])
    count = blocks.shape[0]
    group = lax.axis_size(("ga", "gz"))
    selector = (columns[:, None] == jnp.arange(group, dtype=jnp.int32)[None, :]).astype(jnp.float32)
    shape = right_side.shape
    wide_pair = jnp.stack([diagonal, right_side])
    table = element_table(blocks, columns, shape)
    for axis, dim in SIDES:
        wide_pair, table = pad_together([wide_pair, table], axis, (dim + 1, dim), (RIM, 1))
    wide_diagonal, wide_residual = wide_pair[0], wide_pair[1]
    inside = inside_grid(shape, RIM)

    def precondition_rim(wide_field, field):
        local = schwarz_part(wide_field, basis_tables, eigenvalues)
        return local, coarse_terms(field, blocks, selector)

    def coarse_on_rim(wholes):
        return spread_rim(coarse_rim(wholes, table, count, group), RIM + 1, shape)

    solution = jnp.zeros_like(right_side)
    residual = interior(wide_residual, RIM)
    wide_local, terms = precondition_rim(wide_residual, residual)
    wide_local, wholes, (square,) = reduce_coarse(wide_local, terms, [lane_sums(residual, residual)])
    for restart in range(CYCLES):
        residual = interior(wide_residual, RIM)
        initial_norm = jnp.sqrt(square)
        first_vector = residual / initial_norm
        wide_local_r, wholes_r = wide_local, wholes
        wide_zed = (wide_local_r + coarse_on_rim(wholes_r)) / initial_norm
        first_zed = interior(wide_zed, RIM + 1)
        wide_first = operate_rim(wide_zed, wide_diagonal, inside)
        first_image = interior(wide_first, RIM)
        wide_local, terms = precondition_rim(wide_first, first_image)
        wide_local_w, wholes_w, (first_proj, image_square) = reduce_coarse(
            wide_local, terms, [lane_sums(first_vector, first_image), lane_sums(first_image, first_image)]
        )
        first_len = jnp.sqrt(image_square - first_proj * first_proj)
        second_vector = (first_image - first_proj * first_vector) / first_len
        wide_second_zed = (wide_local_w + coarse_on_rim(wholes_w) - first_proj * wide_zed) / first_len
        second_zed = interior(wide_second_zed, RIM + 1)
        wide_second = operate_rim(wide_second_zed, wide_diagonal, inside)
        second_image = interior(wide_second, RIM)
        products = [
            lane_sums(first_vector, second_image),
            lane_sums(second_vector, second_image),
            lane_sums(second_image, second_image),
        ]
        last = restart == CYCLES - 1
        if last:
            upper_proj, lower_proj, second_square = reduce_scalars(products)
        else:
            wide_local, terms = precondition_rim(wide_second, second_image)
            wide_local_s, wholes_s, (upper_proj, lower_proj, second_square, cross) = reduce_coarse(
                wide_local, terms, products + [lane_sums(first_image, second_image)]
            )
        second_len = jnp.sqrt(second_square - upper_proj * upper_proj - lower_proj * lower_proj)
        gram_first = first_proj * first_proj + first_len * first_len
        gram_cross = first_proj * upper_proj + first_len * lower_proj
        gram_second = upper_proj * upper_proj + lower_proj * lower_proj + second_len * second_len
        target_first = initial_norm * first_proj
        target_second = initial_norm * upper_proj
        determinant = gram_first * gram_second - gram_cross * gram_cross
        weight_first = (gram_second * target_first - gram_cross * target_second) / determinant
        weight_second = (gram_first * target_second - gram_cross * target_first) / determinant
        solution = solution + weight_first * first_zed + weight_second * second_zed
        wide_residual = wide_residual - weight_first * wide_first - weight_second * wide_second
        if not last:
            wide_local = wide_local_r - weight_first * wide_local_w - weight_second * wide_local_s
            wholes = tuple(
                r - weight_first * w - weight_second * s for r, w, s in zip(wholes_r, wholes_w, wholes_s)
            )
            square = (
                square
                - 2.0 * weight_first * target_first
                - 2.0 * weight_second * target_second
                + weight_first * weight_first * image_square
                + 2.0 * weight_first * weight_second * cross
                + weight_second * weight_second * second_square
            )
    return (solution, interior(wide_residual, RIM))


def solution(mesh):
    in_specs = (
        P("gx", "ga", "gz"),
        P("gx", "ga", "gz"),
        P(),
        P(),
        P("gx", "ga", "gz", None, None, None),
        P("gx", "ga", "gz", None),
    )
    out_specs = (P("gx", "ga", "gz"), P("gx", "ga", "gz"))
    return jax.shard_map(body, mesh=mesh, in_specs=in_specs, out_specs=out_specs, check_vma=False)
```

```python
import functools

import jax
import jax.numpy as jnp
from jax import lax
from jax.sharding import PartitionSpec as P

PTS = 8
RIM = 2
WIDE = 12
CYCLES = 2


PRECISE = lax.Precision.HIGHEST
TRANSFORM = lax.Precision.HIGH


def pad_side(value, axis, dim, width):
    size, length = (lax.axis_size(axis), value.shape[dim])
    last = lax.slice_in_dim(value, length - width, length, axis=dim)
    leading = lax.slice_in_dim(value, 0, width, axis=dim)
    if size == 2:
        first = lax.axis_index(axis) == 0
        got = lax.ppermute(jnp.where(first, last, leading), axis, [(0, 1), (1, 0)])
        zero = jnp.zeros_like(got)
        before = jnp.where(first, zero, got)
        after = jnp.where(first, got, zero)
    else:
        up = [(i, (i + 1) % size) for i in range(size - 1)]
        down = [(j, i) for i, j in up]
        before = lax.ppermute(last, axis, up)
        after = lax.ppermute(leading, axis, down)
    return jnp.concatenate([before, value, after], axis=dim)


def padded_2(value, sides, width):
    for axis, dim in sides:
        value = pad_side(value, axis, dim, width)
    return value


def pad_together(values, axis, dims, widths):
    lasts, leads = [], []
    for value, dim, width in zip(values, dims, widths):
        length = value.shape[dim]
        lasts.append(lax.slice_in_dim(value, length - width, length, axis=dim))
        leads.append(lax.slice_in_dim(value, 0, width, axis=dim))

    def pack(slabs):
        return jnp.concatenate([slab.reshape(-1) for slab in slabs])

    def unpack(flat):
        pieces, at = [], 0
        for slab in lasts:
            pieces.append(flat[at : at + slab.size].reshape(slab.shape))
            at += slab.size
        return pieces

    size = lax.axis_size(axis)
    if size == 2:
        first = lax.axis_index(axis) == 0
        got = unpack(lax.ppermute(jnp.where(first, pack(lasts), pack(leads)), axis, [(0, 1), (1, 0)]))
        befores = [jnp.where(first, jnp.zeros_like(g), g) for g in got]
        afters = [jnp.where(first, g, jnp.zeros_like(g)) for g in got]
    elif size == 4:
        me = lax.axis_index(axis)
        even = me % 2 == 0
        to_one = jnp.where(even, pack(lasts), pack(leads))
        to_three = jnp.where(me == 1, pack(lasts), pack(leads))
        from_one = unpack(lax.ppermute(to_one, axis, [(i, i ^ 1) for i in range(4)]))
        from_three = unpack(lax.ppermute(to_three, axis, [(i, i ^ 3) for i in range(4)]))
        befores = [
            jnp.where(even, jnp.where(me == 2, t, jnp.zeros_like(t)), o)
            for o, t in zip(from_one, from_three)
        ]
        afters = [
            jnp.where(even, o, jnp.where(me == 1, t, jnp.zeros_like(t)))
            for o, t in zip(from_one, from_three)
        ]
    else:
        up = [(i, (i + 1) % size) for i in range(size - 1)]
        befores = unpack(lax.ppermute(pack(lasts), axis, up))
        afters = unpack(lax.ppermute(pack(leads), axis, [(j, i) for i, j in up]))
    return [
        jnp.concatenate([before, value, after], axis=dim)
        for before, value, after, dim in zip(befores, values, afters, dims)
    ]


SIDES = (("gx", 0), ("ga", 1), ("gz", 2))


def operate_rim(zed, diagonal, inside):
    centre = zed[1:-1, 1:-1, 1:-1]
    beside = zed[2:, 1:-1, 1:-1] + zed[:-2, 1:-1, 1:-1]
    beside = beside + zed[1:-1, 2:, 1:-1] + zed[1:-1, :-2, 1:-1]
    beside = beside + zed[1:-1, 1:-1, 2:] + zed[1:-1, 1:-1, :-2]
    return ((6.0 + diagonal) * centre - beside) * inside


def inside_grid(shape, width):
    result = None
    for axis, dim in SIDES:
        length = shape[dim]
        place = lax.axis_index(axis) * length - width + jnp.arange(length + 2 * width, dtype=jnp.int32)
        line = ((place >= 0) & (place < lax.axis_size(axis) * length)).astype(jnp.float32)
        view = [1, 1, 1]
        view[dim] = length + 2 * width
        line = line.reshape(view)
        result = line if result is None else result * line
    return result


def interior(value, width):
    return value[width:-width, width:-width, width:-width]


def forward_table(count, basis):
    row_index = jnp.arange(PTS * count + 2 * RIM, dtype=jnp.int32)
    element = jnp.arange(count, dtype=jnp.int32)
    offset = jnp.arange(WIDE, dtype=jnp.int32)
    select = (
        row_index[:, None, None] == PTS * element[None, :, None] + offset[None, None, :]
    ).astype(jnp.float32)
    table = jnp.einsum("rcj,jm->rcm", select, basis, precision=PRECISE)
    return table.reshape(PTS * count + 2 * RIM, count * WIDE)


def backward_table(count, basis):
    same = jnp.eye(count, dtype=jnp.float32)
    table = jnp.einsum("cd,im->cmdi", same, basis[RIM : RIM + PTS], precision=PRECISE)
    return table.reshape(count * WIDE, count * PTS)


def schwarz_part(padded, basis_tables, eigenvalues):
    count_x = (padded.shape[0] - 2 * RIM) // PTS
    count_y = (padded.shape[1] - 2 * RIM) // PTS
    count_z = (padded.shape[2] - 2 * RIM) // PTS
    spectral = jnp.einsum(
        "pqr,rc->pqc", padded, forward_table(count_z, basis_tables[2]), precision=TRANSFORM
    )
    spectral = jnp.einsum(
        "pqc,pa->aqc", spectral, forward_table(count_x, basis_tables[0]), precision=TRANSFORM
    )
    spectral = jnp.einsum(
        "aqc,qb->abc", spectral, forward_table(count_y, basis_tables[1]), precision=TRANSFORM
    )
    denominator = (
        jnp.tile(eigenvalues[0], count_x)[:, None, None]
        + jnp.tile(eigenvalues[1], count_y)[None, :, None]
    )
    denominator = denominator + jnp.tile(eigenvalues[2], count_z)[None, None, :]
    spectral = spectral / denominator
    local_part = jnp.einsum(
        "abc,cr->abr", spectral, backward_table(count_z, basis_tables[2]), precision=TRANSFORM
    )
    local_part = jnp.einsum(
        "abr,ap->pbr", local_part, backward_table(count_x, basis_tables[0]), precision=TRANSFORM
    )
    local_part = jnp.einsum(
        "pbr,bq->pqr", local_part, backward_table(count_y, basis_tables[1]), precision=TRANSFORM
    )
    return local_part


def coarse_terms(field, blocks, selector):
    count_x = field.shape[0] // PTS
    count_y = field.shape[1] // PTS
    count_z = field.shape[2] // PTS
    cells = count_x * count_y * count_z
    point = jnp.arange(field.shape[2], dtype=jnp.int32)
    along = (point[:, None] // PTS == jnp.arange(count_z, dtype=jnp.int32)[None, :]).astype(jnp.float32)
    sums = jnp.einsum("pqr,rc->pqc", field, along, precision=PRECISE)
    sums = jnp.sum(sums.reshape(count_x, PTS, count_y, PTS, count_z), axis=(1, 3))
    restricted = sums.reshape(cells) * (1.0 / PTS**3)
    terms = jnp.einsum("kpq,p->kq", blocks, restricted, precision=PRECISE)
    return jnp.einsum("kj,kq->jq", selector, terms, precision=PRECISE)


def element_table(blocks, columns, shape):
    count = blocks.shape[0]
    grid = (shape[0] // PTS, shape[1] // PTS, shape[2] // PTS)
    rows = jnp.transpose(blocks, (1, 0, 2)).reshape(grid + (count * blocks.shape[2],))
    cols = jnp.broadcast_to(columns.astype(jnp.float32), grid + (count,))
    return jnp.concatenate([rows, cols], axis=-1)


def coarse_rim(wholes, table, count, group):
    lo, whole, hi = wholes
    grid = table.shape[:3]
    width = (table.shape[3] - count) // count
    rows = table[..., : count * width].reshape(grid + (count, width))
    cols = table[..., count * width :]
    onehot = (cols[..., None] == jnp.arange(group, dtype=jnp.float32)).astype(jnp.float32)
    stacked = jnp.stack([lo] + [whole] * (grid[0] - 2) + [hi])
    picked = jnp.einsum("abckg,agq->abckq", onehot, stacked, precision=PRECISE)
    return jnp.sum(rows * picked, axis=(3, 4))


def spread_rim(values, width, shape):
    def table(length, count):
        point = jnp.arange(length + 2 * width, dtype=jnp.int32) - width + PTS
        element = jnp.arange(count, dtype=jnp.int32)
        return (point[:, None] // PTS == element[None, :]).astype(jnp.float32)

    grid = values.shape
    out = jnp.einsum("abc,rc->abr", values, table(shape[2], grid[2]), precision=PRECISE)
    out = jnp.einsum("abr,pa->pbr", out, table(shape[0], grid[0]), precision=PRECISE)
    return jnp.einsum("pbr,qb->pqr", out, table(shape[1], grid[1]), precision=PRECISE)


ALL = ("gx", "ga", "gz")


def butterfly_stages(axes):
    stages = []
    for axis in axes:
        size = lax.axis_size(axis)
        if size & (size - 1):
            stages.append(lambda value, axis=axis: lax.psum(value, axis))
            continue
        if size == 4:
            stages.append(functools.partial(sum_of_four, axis=axis))
            continue
        step = 1
        while step < size:
            pairs = [(i, i ^ step) for i in range(size)]
            stages.append(lambda value, axis=axis, pairs=pairs: value + lax.ppermute(value, axis, pairs))
            step *= 2
    return stages


def sum_of_four(value, axis):
    got = [value] + [lax.ppermute(value, axis, [(i, i ^ s) for i in range(4)]) for s in (1, 2, 3)]
    return (got[0] + got[1]) + (got[2] + got[3])


def butterfly(value, axes):
    for stage in butterfly_stages(axes):
        value = stage(value)
    return value


def lane_sums(a, b):
    return jnp.sum((a * b).reshape(-1, a.shape[-1]), axis=0)


def finish(total, count):
    return [jnp.sum(part) for part in jnp.split(total, count)]


def reduce_scalars(scalars):
    total = butterfly(lax.optimization_barrier(jnp.concatenate(scalars)), ALL)
    return finish(total, len(scalars))


def fold_four(payload, local, axis, dim, width):
    me = lax.axis_index(axis)
    length = local.shape[dim]
    last = lax.slice_in_dim(local, length - width, length, axis=dim)
    leading = lax.slice_in_dim(local, 0, width, axis=dim)
    even = me % 2 == 0
    count = payload.shape[0]

    def send(slab, step):
        message = jnp.concatenate([payload, slab.reshape(-1)])
        return lax.ppermute(message, axis, [(i, i ^ step) for i in range(4)])

    got_one = send(jnp.where(even, last, leading), 1)
    got_two = lax.ppermute(payload, axis, [(i, i ^ 2) for i in range(4)])
    got_three = send(jnp.where(me == 1, last, leading), 3)
    total = (payload + got_one[:count]) + (got_two + got_three[:count])
    from_one = got_one[count:].reshape(last.shape)
    from_three = got_three[count:].reshape(last.shape)
    zero = jnp.zeros_like(from_one)
    before = jnp.where(even, jnp.where(me == 2, from_three, zero), from_one)
    after = jnp.where(even, from_one, jnp.where(me == 1, from_three, zero))
    return total, jnp.concatenate([before, local, after], axis=dim)


def reduce_coarse(local, buffer, scalars):
    count = sum(part.shape[0] for part in scalars)
    width = RIM + 1
    payload = jnp.concatenate([buffer.reshape(-1)] + list(scalars))
    local, payload = lax.optimization_barrier((local, payload))
    for axis, dim in (("ga", 1), ("gz", 2)):
        if lax.axis_size(axis) == 4:
            payload, local = fold_four(payload, local, axis, dim, width)
        else:
            payload = butterfly(payload, (axis,))
            local = pad_side(local, axis, dim, width)
        local, payload = lax.optimization_barrier((local, payload))
    size = payload.shape[0] - count
    whole = payload[:size].reshape(buffer.shape)
    if lax.axis_size("gx") == 2:
        first = lax.axis_index("gx") == 0
        length = local.shape[0]
        slab = jnp.where(first, local[length - width :], local[:width])
        message = jnp.concatenate([payload, slab.reshape(-1)])
        got = lax.ppermute(message, "gx", [(0, 1), (1, 0)])
        total = payload[size:] + got[size : size + count]
        other = got[:size].reshape(buffer.shape)
        beside = got[size + count :].reshape(slab.shape)
        zero = jnp.zeros_like(other)
        lo, hi = jnp.where(first, zero, other), jnp.where(first, other, zero)
        flat = jnp.zeros_like(beside)
        local = jnp.concatenate(
            [jnp.where(first, flat, beside), local, jnp.where(first, beside, flat)], axis=0
        )
    else:
        total = butterfly(payload[size:], ("gx",))
        gx = lax.axis_size("gx")
        up = [(i, i + 1) for i in range(gx - 1)]
        lo = lax.ppermute(whole, "gx", up)
        hi = lax.ppermute(whole, "gx", [(j, i) for i, j in up])
        local = pad_side(local, "gx", 0, width)
    return local, (lo, whole, hi), finish(total, len(scalars))


def body(right_side, diagonal, basis_tables, eigenvalues, coarse_blocks, coarse_columns):
    blocks = coarse_blocks.reshape(coarse_blocks.shape[3:])
    columns = coarse_columns.reshape(coarse_columns.shape[3])
    count = blocks.shape[0]
    group = lax.axis_size(("ga", "gz"))
    selector = (columns[:, None] == jnp.arange(group, dtype=jnp.int32)[None, :]).astype(jnp.float32)
    shape = right_side.shape
    wide_pair = jnp.stack([diagonal, right_side])
    table = element_table(blocks, columns, shape)
    for axis, dim in SIDES:
        wide_pair, table = pad_together([wide_pair, table], axis, (dim + 1, dim), (RIM, 1))
    wide_diagonal, wide_residual = wide_pair[0], wide_pair[1]
    inside = inside_grid(shape, RIM)

    def precondition_rim(wide_field, field):
        local = schwarz_part(wide_field, basis_tables, eigenvalues)
        return local, coarse_terms(field, blocks, selector)

    def coarse_on_rim(wholes):
        return spread_rim(coarse_rim(wholes, table, count, group), RIM + 1, shape)

    solution = jnp.zeros_like(right_side)
    residual = interior(wide_residual, RIM)
    wide_local, terms = precondition_rim(wide_residual, residual)
    wide_local, wholes, (square,) = reduce_coarse(wide_local, terms, [lane_sums(residual, residual)])
    for restart in range(CYCLES):
        residual = interior(wide_residual, RIM)
        initial_norm = jnp.sqrt(square)
        first_vector = residual / initial_norm
        wide_local_r, wholes_r = wide_local, wholes
        wide_zed = (wide_local_r + coarse_on_rim(wholes_r)) / initial_norm
        first_zed = interior(wide_zed, RIM + 1)
        wide_first = operate_rim(wide_zed, wide_diagonal, inside)
        first_image = interior(wide_first, RIM)
        wide_local, terms = precondition_rim(wide_first, first_image)
        wide_local_w, wholes_w, (first_proj, image_square) = reduce_coarse(
            wide_local, terms, [lane_sums(first_vector, first_image), lane_sums(first_image, first_image)]
        )
        first_len = jnp.sqrt(image_square - first_proj * first_proj)
        second_vector = (first_image - first_proj * first_vector) / first_len
        wide_second_zed = (wide_local_w + coarse_on_rim(wholes_w) - first_proj * wide_zed) / first_len
        second_zed = interior(wide_second_zed, RIM + 1)
        wide_second = operate_rim(wide_second_zed, wide_diagonal, inside)
        second_image = interior(wide_second, RIM)
        products = [
            lane_sums(first_vector, second_image),
            lane_sums(second_vector, second_image),
            lane_sums(second_image, second_image),
        ]
        last = restart == CYCLES - 1
        if last:
            upper_proj, lower_proj, second_square = reduce_scalars(products)
        else:
            wide_local, terms = precondition_rim(wide_second, second_image)
            wide_local_s, wholes_s, (upper_proj, lower_proj, second_square, cross) = reduce_coarse(
                wide_local, terms, products + [lane_sums(first_image, second_image)]
            )
        second_len = jnp.sqrt(second_square - upper_proj * upper_proj - lower_proj * lower_proj)
        gram_first = first_proj * first_proj + first_len * first_len
        gram_cross = first_proj * upper_proj + first_len * lower_proj
        gram_second = upper_proj * upper_proj + lower_proj * lower_proj + second_len * second_len
        target_first = initial_norm * first_proj
        target_second = initial_norm * upper_proj
        determinant = gram_first * gram_second - gram_cross * gram_cross
        weight_first = (gram_second * target_first - gram_cross * target_second) / determinant
        weight_second = (gram_first * target_second - gram_cross * target_first) / determinant
        solution = solution + weight_first * first_zed + weight_second * second_zed
        wide_residual = wide_residual - weight_first * wide_first - weight_second * wide_second
        if not last:
            wide_local = wide_local_r - weight_first * wide_local_w - weight_second * wide_local_s
            wholes = tuple(
                r - weight_first * w - weight_second * s for r, w, s in zip(wholes_r, wholes_w, wholes_s)
            )
            square = (
                square
                - 2.0 * weight_first * target_first
                - 2.0 * weight_second * target_second
                + weight_first * weight_first * image_square
                + 2.0 * weight_first * weight_second * cross
                + weight_second * weight_second * second_square
            )
    return (solution, interior(wide_residual, RIM))


def solution(mesh):
    in_specs = (
        P("gx", "ga", "gz"),
        P("gx", "ga", "gz"),
        P(),
        P(),
        P("gx", "ga", "gz", None, None, None),
        P("gx", "ga", "gz", None),
    )
    out_specs = (P("gx", "ga", "gz"), P("gx", "ga", "gz"))
    return jax.shard_map(body, mesh=mesh, in_specs=in_specs, out_specs=out_specs, check_vma=False)
```

```python
import functools

import jax
import jax.numpy as jnp
from jax import lax
from jax.sharding import PartitionSpec as P

PTS = 8
RIM = 2
WIDE = 12
CYCLES = 2


PRECISE = lax.Precision.HIGHEST
TRANSFORM = lax.Precision.HIGH


def pad_side(value, axis, dim, width):
    size, length = (lax.axis_size(axis), value.shape[dim])
    last = lax.slice_in_dim(value, length - width, length, axis=dim)
    leading = lax.slice_in_dim(value, 0, width, axis=dim)
    if size == 2:
        first = lax.axis_index(axis) == 0
        got = lax.ppermute(jnp.where(first, last, leading), axis, [(0, 1), (1, 0)])
        zero = jnp.zeros_like(got)
        before = jnp.where(first, zero, got)
        after = jnp.where(first, got, zero)
    else:
        up = [(i, (i + 1) % size) for i in range(size - 1)]
        down = [(j, i) for i, j in up]
        before = lax.ppermute(last, axis, up)
        after = lax.ppermute(leading, axis, down)
    return jnp.concatenate([before, value, after], axis=dim)


def padded_2(value, sides, width):
    for axis, dim in sides:
        value = pad_side(value, axis, dim, width)
    return value


def pad_together(values, axis, dims, widths):
    lasts, leads = [], []
    for value, dim, width in zip(values, dims, widths):
        length = value.shape[dim]
        lasts.append(lax.slice_in_dim(value, length - width, length, axis=dim))
        leads.append(lax.slice_in_dim(value, 0, width, axis=dim))

    def pack(slabs):
        return jnp.concatenate([slab.reshape(-1) for slab in slabs])

    def unpack(flat):
        pieces, at = [], 0
        for slab in lasts:
            pieces.append(flat[at : at + slab.size].reshape(slab.shape))
            at += slab.size
        return pieces

    size = lax.axis_size(axis)
    if size == 2:
        first = lax.axis_index(axis) == 0
        got = unpack(lax.ppermute(jnp.where(first, pack(lasts), pack(leads)), axis, [(0, 1), (1, 0)]))
        befores = [jnp.where(first, jnp.zeros_like(g), g) for g in got]
        afters = [jnp.where(first, g, jnp.zeros_like(g)) for g in got]
    elif size == 4:
        me = lax.axis_index(axis)
        even = me % 2 == 0
        to_one = jnp.where(even, pack(lasts), pack(leads))
        to_three = jnp.where(me == 1, pack(lasts), pack(leads))
        from_one = unpack(lax.ppermute(to_one, axis, [(i, i ^ 1) for i in range(4)]))
        from_three = unpack(lax.ppermute(to_three, axis, [(i, i ^ 3) for i in range(4)]))
        befores = [
            jnp.where(even, jnp.where(me == 2, t, jnp.zeros_like(t)), o)
            for o, t in zip(from_one, from_three)
        ]
        afters = [
            jnp.where(even, o, jnp.where(me == 1, t, jnp.zeros_like(t)))
            for o, t in zip(from_one, from_three)
        ]
    else:
        up = [(i, (i + 1) % size) for i in range(size - 1)]
        befores = unpack(lax.ppermute(pack(lasts), axis, up))
        afters = unpack(lax.ppermute(pack(leads), axis, [(j, i) for i, j in up]))
    return [
        jnp.concatenate([before, value, after], axis=dim)
        for before, value, after, dim in zip(befores, values, afters, dims)
    ]


SIDES = (("gx", 0), ("ga", 1), ("gz", 2))


def operate_rim(zed, diagonal, inside):
    centre = zed[1:-1, 1:-1, 1:-1]
    beside = zed[2:, 1:-1, 1:-1] + zed[:-2, 1:-1, 1:-1]
    beside = beside + zed[1:-1, 2:, 1:-1] + zed[1:-1, :-2, 1:-1]
    beside = beside + zed[1:-1, 1:-1, 2:] + zed[1:-1, 1:-1, :-2]
    return ((6.0 + diagonal) * centre - beside) * inside


def inside_grid(shape, width):
    result = None
    for axis, dim in SIDES:
        length = shape[dim]
        place = lax.axis_index(axis) * length - width + jnp.arange(length + 2 * width, dtype=jnp.int32)
        line = ((place >= 0) & (place < lax.axis_size(axis) * length)).astype(jnp.float32)
        view = [1, 1, 1]
        view[dim] = length + 2 * width
        line = line.reshape(view)
        result = line if result is None else result * line
    return result


def interior(value, width):
    return value[width:-width, width:-width, width:-width]


def forward_table(count, basis):
    row_index = jnp.arange(PTS * count + 2 * RIM, dtype=jnp.int32)
    element = jnp.arange(count, dtype=jnp.int32)
    offset = jnp.arange(WIDE, dtype=jnp.int32)
    select = (
        row_index[:, None, None] == PTS * element[None, :, None] + offset[None, None, :]
    ).astype(jnp.float32)
    table = jnp.einsum("rcj,jm->rcm", select, basis, precision=PRECISE)
    return table.reshape(PTS * count + 2 * RIM, count * WIDE)


def backward_table(count, basis):
    same = jnp.eye(count, dtype=jnp.float32)
    table = jnp.einsum("cd,im->cmdi", same, basis[RIM : RIM + PTS], precision=PRECISE)
    return table.reshape(count * WIDE, count * PTS)


def schwarz_part(padded, basis_tables, eigenvalues):
    count_x = (padded.shape[0] - 2 * RIM) // PTS
    count_y = (padded.shape[1] - 2 * RIM) // PTS
    count_z = (padded.shape[2] - 2 * RIM) // PTS
    spectral = jnp.einsum(
        "pqr,rc->pqc", padded, forward_table(count_z, basis_tables[2]), precision=TRANSFORM
    )
    spectral = jnp.einsum(
        "pqc,pa->aqc", spectral, forward_table(count_x, basis_tables[0]), precision=TRANSFORM
    )
    spectral = jnp.einsum(
        "aqc,qb->abc", spectral, forward_table(count_y, basis_tables[1]), precision=TRANSFORM
    )
    denominator = (
        jnp.tile(eigenvalues[0], count_x)[:, None, None]
        + jnp.tile(eigenvalues[1], count_y)[None, :, None]
    )
    denominator = denominator + jnp.tile(eigenvalues[2], count_z)[None, None, :]
    spectral = spectral / denominator
    local_part = jnp.einsum(
        "abc,cr->abr", spectral, backward_table(count_z, basis_tables[2]), precision=TRANSFORM
    )
    local_part = jnp.einsum(
        "abr,ap->pbr", local_part, backward_table(count_x, basis_tables[0]), precision=TRANSFORM
    )
    local_part = jnp.einsum(
        "pbr,bq->pqr", local_part, backward_table(count_y, basis_tables[1]), precision=TRANSFORM
    )
    return local_part


def coarse_terms(field, blocks, selector):
    count_x = field.shape[0] // PTS
    count_y = field.shape[1] // PTS
    count_z = field.shape[2] // PTS
    cells = count_x * count_y * count_z
    point = jnp.arange(field.shape[2], dtype=jnp.int32)
    along = (point[:, None] // PTS == jnp.arange(count_z, dtype=jnp.int32)[None, :]).astype(jnp.float32)
    sums = jnp.einsum("pqr,rc->pqc", field, along, precision=PRECISE)
    sums = jnp.sum(sums.reshape(count_x, PTS, count_y, PTS, count_z), axis=(1, 3))
    restricted = sums.reshape(cells) * (1.0 / PTS**3)
    terms = jnp.einsum("kpq,p->kq", blocks, restricted, precision=PRECISE)
    return jnp.einsum("kj,kq->jq", selector, terms, precision=PRECISE)


def element_table(blocks, columns, shape):
    count = blocks.shape[0]
    grid = (shape[0] // PTS, shape[1] // PTS, shape[2] // PTS)
    rows = jnp.transpose(blocks, (1, 0, 2)).reshape(grid + (count * blocks.shape[2],))
    cols = jnp.broadcast_to(columns.astype(jnp.float32), grid + (count,))
    return jnp.concatenate([rows, cols], axis=-1)


def coarse_rim(wholes, table, count, group):
    lo, whole, hi = wholes
    grid = table.shape[:3]
    width = (table.shape[3] - count) // count
    rows = table[..., : count * width].reshape(grid + (count, width))
    cols = table[..., count * width :]
    onehot = (cols[..., None] == jnp.arange(group, dtype=jnp.float32)).astype(jnp.float32)
    stacked = jnp.stack([lo] + [whole] * (grid[0] - 2) + [hi])
    picked = jnp.einsum("abckg,agq->abckq", onehot, stacked, precision=PRECISE)
    return jnp.sum(rows * picked, axis=(3, 4))


def spread_rim(values, width, shape):
    def table(length, count):
        point = jnp.arange(length + 2 * width, dtype=jnp.int32) - width + PTS
        element = jnp.arange(count, dtype=jnp.int32)
        return (point[:, None] // PTS == element[None, :]).astype(jnp.float32)

    grid = values.shape
    out = jnp.einsum("abc,rc->abr", values, table(shape[2], grid[2]), precision=PRECISE)
    out = jnp.repeat(out, PTS, axis=0)[PTS - width : PTS + shape[0] + width]
    return jnp.repeat(out, PTS, axis=1)[:, PTS - width : PTS + shape[1] + width]


ALL = ("gx", "ga", "gz")


def butterfly_stages(axes):
    stages = []
    for axis in axes:
        size = lax.axis_size(axis)
        if size & (size - 1):
            stages.append(lambda value, axis=axis: lax.psum(value, axis))
            continue
        if size == 4:
            stages.append(functools.partial(sum_of_four, axis=axis))
            continue
        step = 1
        while step < size:
            pairs = [(i, i ^ step) for i in range(size)]
            stages.append(lambda value, axis=axis, pairs=pairs: value + lax.ppermute(value, axis, pairs))
            step *= 2
    return stages


def sum_of_four(value, axis):
    got = [value] + [lax.ppermute(value, axis, [(i, i ^ s) for i in range(4)]) for s in (1, 2, 3)]
    return (got[0] + got[1]) + (got[2] + got[3])


def butterfly(value, axes):
    for stage in butterfly_stages(axes):
        value = stage(value)
    return value


def lane_sums(a, b):
    return jnp.sum((a * b).reshape(-1, a.shape[-1]), axis=0)


def finish(total, count):
    return [jnp.sum(part) for part in jnp.split(total, count)]


def reduce_scalars(scalars):
    total = butterfly(lax.optimization_barrier(jnp.concatenate(scalars)), ALL)
    return finish(total, len(scalars))


def fold_four(payload, local, axis, dim, width):
    me = lax.axis_index(axis)
    length = local.shape[dim]
    last = lax.slice_in_dim(local, length - width, length, axis=dim)
    leading = lax.slice_in_dim(local, 0, width, axis=dim)
    even = me % 2 == 0
    count = payload.shape[0]

    def send(slab, step):
        message = jnp.concatenate([payload, slab.reshape(-1)])
        return lax.ppermute(message, axis, [(i, i ^ step) for i in range(4)])

    got_one = send(jnp.where(even, last, leading), 1)
    got_two = lax.ppermute(payload, axis, [(i, i ^ 2) for i in range(4)])
    got_three = send(jnp.where(me == 1, last, leading), 3)
    total = (payload + got_one[:count]) + (got_two + got_three[:count])
    from_one = got_one[count:].reshape(last.shape)
    from_three = got_three[count:].reshape(last.shape)
    zero = jnp.zeros_like(from_one)
    before = jnp.where(even, jnp.where(me == 2, from_three, zero), from_one)
    after = jnp.where(even, from_one, jnp.where(me == 1, from_three, zero))
    return total, jnp.concatenate([before, local, after], axis=dim)


def reduce_coarse(local, buffer, scalars):
    count = sum(part.shape[0] for part in scalars)
    width = RIM + 1
    payload = jnp.concatenate([buffer.reshape(-1)] + list(scalars))
    local, payload = lax.optimization_barrier((local, payload))
    for axis, dim in (("ga", 1), ("gz", 2)):
        if lax.axis_size(axis) == 4:
            payload, local = fold_four(payload, local, axis, dim, width)
        else:
            payload = butterfly(payload, (axis,))
            local = pad_side(local, axis, dim, width)
        local, payload = lax.optimization_barrier((local, payload))
    size = payload.shape[0] - count
    whole = payload[:size].reshape(buffer.shape)
    if lax.axis_size("gx") == 2:
        first = lax.axis_index("gx") == 0
        length = local.shape[0]
        slab = jnp.where(first, local[length - width :], local[:width])
        message = jnp.concatenate([payload, slab.reshape(-1)])
        got = lax.ppermute(message, "gx", [(0, 1), (1, 0)])
        total = payload[size:] + got[size : size + count]
        other = got[:size].reshape(buffer.shape)
        beside = got[size + count :].reshape(slab.shape)
        zero = jnp.zeros_like(other)
        lo, hi = jnp.where(first, zero, other), jnp.where(first, other, zero)
        flat = jnp.zeros_like(beside)
        local = jnp.concatenate(
            [jnp.where(first, flat, beside), local, jnp.where(first, beside, flat)], axis=0
        )
    else:
        total = butterfly(payload[size:], ("gx",))
        gx = lax.axis_size("gx")
        up = [(i, i + 1) for i in range(gx - 1)]
        lo = lax.ppermute(whole, "gx", up)
        hi = lax.ppermute(whole, "gx", [(j, i) for i, j in up])
        local = pad_side(local, "gx", 0, width)
    return local, (lo, whole, hi), finish(total, len(scalars))


def body(right_side, diagonal, basis_tables, eigenvalues, coarse_blocks, coarse_columns):
    blocks = coarse_blocks.reshape(coarse_blocks.shape[3:])
    columns = coarse_columns.reshape(coarse_columns.shape[3])
    count = blocks.shape[0]
    group = lax.axis_size(("ga", "gz"))
    selector = (columns[:, None] == jnp.arange(group, dtype=jnp.int32)[None, :]).astype(jnp.float32)
    shape = right_side.shape
    wide_pair = jnp.stack([diagonal, right_side])
    table = element_table(blocks, columns, shape)
    for axis, dim in SIDES:
        wide_pair, table = pad_together([wide_pair, table], axis, (dim + 1, dim), (RIM, 1))
    wide_diagonal, wide_residual = wide_pair[0], wide_pair[1]
    inside = inside_grid(shape, RIM)

    def precondition_rim(wide_field, field):
        local = schwarz_part(wide_field, basis_tables, eigenvalues)
        return local, coarse_terms(field, blocks, selector)

    def coarse_on_rim(wholes):
        return spread_rim(coarse_rim(wholes, table, count, group), RIM + 1, shape)

    solution = jnp.zeros_like(right_side)
    residual = interior(wide_residual, RIM)
    wide_local, terms = precondition_rim(wide_residual, residual)
    wide_local, wholes, (square,) = reduce_coarse(wide_local, terms, [lane_sums(residual, residual)])
    for restart in range(CYCLES):
        residual = interior(wide_residual, RIM)
        initial_norm = jnp.sqrt(square)
        first_vector = residual / initial_norm
        wide_local_r, wholes_r = wide_local, wholes
        wide_zed = (wide_local_r + coarse_on_rim(wholes_r)) / initial_norm
        first_zed = interior(wide_zed, RIM + 1)
        wide_first = operate_rim(wide_zed, wide_diagonal, inside)
        first_image = interior(wide_first, RIM)
        wide_local, terms = precondition_rim(wide_first, first_image)
        wide_local_w, wholes_w, (first_proj, image_square) = reduce_coarse(
            wide_local, terms, [lane_sums(first_vector, first_image), lane_sums(first_image, first_image)]
        )
        first_len = jnp.sqrt(image_square - first_proj * first_proj)
        second_vector = (first_image - first_proj * first_vector) / first_len
        wide_second_zed = (wide_local_w + coarse_on_rim(wholes_w) - first_proj * wide_zed) / first_len
        second_zed = interior(wide_second_zed, RIM + 1)
        wide_second = operate_rim(wide_second_zed, wide_diagonal, inside)
        second_image = interior(wide_second, RIM)
        products = [
            lane_sums(first_vector, second_image),
            lane_sums(second_vector, second_image),
            lane_sums(second_image, second_image),
        ]
        last = restart == CYCLES - 1
        if last:
            upper_proj, lower_proj, second_square = reduce_scalars(products)
        else:
            wide_local, terms = precondition_rim(wide_second, second_image)
            wide_local_s, wholes_s, (upper_proj, lower_proj, second_square, cross) = reduce_coarse(
                wide_local, terms, products + [lane_sums(first_image, second_image)]
            )
        second_len = jnp.sqrt(second_square - upper_proj * upper_proj - lower_proj * lower_proj)
        gram_first = first_proj * first_proj + first_len * first_len
        gram_cross = first_proj * upper_proj + first_len * lower_proj
        gram_second = upper_proj * upper_proj + lower_proj * lower_proj + second_len * second_len
        target_first = initial_norm * first_proj
        target_second = initial_norm * upper_proj
        determinant = gram_first * gram_second - gram_cross * gram_cross
        weight_first = (gram_second * target_first - gram_cross * target_second) / determinant
        weight_second = (gram_first * target_second - gram_cross * target_first) / determinant
        solution = solution + weight_first * first_zed + weight_second * second_zed
        wide_residual = wide_residual - weight_first * wide_first - weight_second * wide_second
        if not last:
            wide_local = wide_local_r - weight_first * wide_local_w - weight_second * wide_local_s
            wholes = tuple(
                r - weight_first * w - weight_second * s for r, w, s in zip(wholes_r, wholes_w, wholes_s)
            )
            square = (
                square
                - 2.0 * weight_first * target_first
                - 2.0 * weight_second * target_second
                + weight_first * weight_first * image_square
                + 2.0 * weight_first * weight_second * cross
                + weight_second * weight_second * second_square
            )
    return (solution, interior(wide_residual, RIM))


def solution(mesh):
    in_specs = (
        P("gx", "ga", "gz"),
        P("gx", "ga", "gz"),
        P(),
        P(),
        P("gx", "ga", "gz", None, None, None),
        P("gx", "ga", "gz", None),
    )
    out_specs = (P("gx", "ga", "gz"), P("gx", "ga", "gz"))
    return jax.shard_map(body, mesh=mesh, in_specs=in_specs, out_specs=out_specs, check_vma=False)
```

```python
import functools

import jax
import jax.numpy as jnp
from jax import lax
from jax.sharding import PartitionSpec as P

PTS = 8
RIM = 2
WIDE = 12
CYCLES = 2


PRECISE = lax.Precision.HIGHEST
TRANSFORM = lax.Precision.HIGH


def pick(flag, when, otherwise):
    weight = flag.astype(when.dtype)
    return when * weight + otherwise * (1.0 - weight)


def pad_side(value, axis, dim, width):
    size, length = (lax.axis_size(axis), value.shape[dim])
    last = lax.slice_in_dim(value, length - width, length, axis=dim)
    leading = lax.slice_in_dim(value, 0, width, axis=dim)
    if size == 2:
        first = lax.axis_index(axis) == 0
        got = lax.ppermute(jnp.where(first, last, leading), axis, [(0, 1), (1, 0)])
        zero = jnp.zeros_like(got)
        before = jnp.where(first, zero, got)
        after = jnp.where(first, got, zero)
    else:
        up = [(i, (i + 1) % size) for i in range(size - 1)]
        down = [(j, i) for i, j in up]
        before = lax.ppermute(last, axis, up)
        after = lax.ppermute(leading, axis, down)
    return jnp.concatenate([before, value, after], axis=dim)


def padded_2(value, sides, width):
    for axis, dim in sides:
        value = pad_side(value, axis, dim, width)
    return value


def pad_together(values, axis, dims, widths):
    lasts, leads = [], []
    for value, dim, width in zip(values, dims, widths):
        length = value.shape[dim]
        lasts.append(lax.slice_in_dim(value, length - width, length, axis=dim))
        leads.append(lax.slice_in_dim(value, 0, width, axis=dim))

    def pack(slabs):
        return jnp.concatenate([slab.reshape(-1) for slab in slabs])

    def unpack(flat):
        pieces, at = [], 0
        for slab in lasts:
            pieces.append(flat[at : at + slab.size].reshape(slab.shape))
            at += slab.size
        return pieces

    size = lax.axis_size(axis)
    if size == 2:
        first = lax.axis_index(axis) == 0
        got = unpack(lax.ppermute(pick(first, pack(lasts), pack(leads)), axis, [(0, 1), (1, 0)]))
        befores = [g * (1.0 - first.astype(g.dtype)) for g in got]
        afters = [g * first.astype(g.dtype) for g in got]
    elif size == 4:
        me = lax.axis_index(axis)
        even = me % 2 == 0
        to_one = pick(even, pack(lasts), pack(leads))
        to_three = pick(me == 1, pack(lasts), pack(leads))
        from_one = unpack(lax.ppermute(to_one, axis, [(i, i ^ 1) for i in range(4)]))
        from_three = unpack(lax.ppermute(to_three, axis, [(i, i ^ 3) for i in range(4)]))
        odd = 1.0 - even.astype(jnp.float32)
        second, third = (me == 2).astype(jnp.float32), (me == 1).astype(jnp.float32)
        befores = [o * odd + t * second for o, t in zip(from_one, from_three)]
        afters = [o * (1.0 - odd) + t * third for o, t in zip(from_one, from_three)]
    else:
        up = [(i, (i + 1) % size) for i in range(size - 1)]
        befores = unpack(lax.ppermute(pack(lasts), axis, up))
        afters = unpack(lax.ppermute(pack(leads), axis, [(j, i) for i, j in up]))
    return [
        jnp.concatenate([before, value, after], axis=dim)
        for before, value, after, dim in zip(befores, values, afters, dims)
    ]


SIDES = (("gx", 0), ("ga", 1), ("gz", 2))


def operate_rim(zed, diagonal, inside):
    centre = zed[1:-1, 1:-1, 1:-1]
    beside = zed[2:, 1:-1, 1:-1] + zed[:-2, 1:-1, 1:-1]
    beside = beside + zed[1:-1, 2:, 1:-1] + zed[1:-1, :-2, 1:-1]
    beside = beside + zed[1:-1, 1:-1, 2:] + zed[1:-1, 1:-1, :-2]
    return ((6.0 + diagonal) * centre - beside) * inside


def inside_grid(shape, width):
    result = None
    for axis, dim in SIDES:
        length = shape[dim]
        place = lax.axis_index(axis) * length - width + jnp.arange(length + 2 * width, dtype=jnp.int32)
        line = ((place >= 0) & (place < lax.axis_size(axis) * length)).astype(jnp.float32)
        view = [1, 1, 1]
        view[dim] = length + 2 * width
        line = line.reshape(view)
        result = line if result is None else result * line
    return result


def interior(value, width):
    return value[width:-width, width:-width, width:-width]


def forward_table(count, basis):
    row_index = jnp.arange(PTS * count + 2 * RIM, dtype=jnp.int32)
    element = jnp.arange(count, dtype=jnp.int32)
    offset = jnp.arange(WIDE, dtype=jnp.int32)
    select = (
        row_index[:, None, None] == PTS * element[None, :, None] + offset[None, None, :]
    ).astype(jnp.float32)
    table = jnp.einsum("rcj,jm->rcm", select, basis, precision=PRECISE)
    return table.reshape(PTS * count + 2 * RIM, count * WIDE)


def backward_table(count, basis):
    same = jnp.eye(count, dtype=jnp.float32)
    table = jnp.einsum("cd,im->cmdi", same, basis[RIM : RIM + PTS], precision=PRECISE)
    return table.reshape(count * WIDE, count * PTS)


def schwarz_part(padded, basis_tables, eigenvalues):
    count_x = (padded.shape[0] - 2 * RIM) // PTS
    count_y = (padded.shape[1] - 2 * RIM) // PTS
    count_z = (padded.shape[2] - 2 * RIM) // PTS
    spectral = jnp.einsum(
        "pqr,rc->pqc", padded, forward_table(count_z, basis_tables[2]), precision=TRANSFORM
    )
    spectral = jnp.einsum(
        "pqc,pa->aqc", spectral, forward_table(count_x, basis_tables[0]), precision=TRANSFORM
    )
    spectral = jnp.einsum(
        "aqc,qb->abc", spectral, forward_table(count_y, basis_tables[1]), precision=TRANSFORM
    )
    denominator = (
        jnp.tile(eigenvalues[0], count_x)[:, None, None]
        + jnp.tile(eigenvalues[1], count_y)[None, :, None]
    )
    denominator = denominator + jnp.tile(eigenvalues[2], count_z)[None, None, :]
    spectral = spectral / denominator
    local_part = jnp.einsum(
        "abc,cr->abr", spectral, backward_table(count_z, basis_tables[2]), precision=TRANSFORM
    )
    local_part = jnp.einsum(
        "abr,ap->pbr", local_part, backward_table(count_x, basis_tables[0]), precision=TRANSFORM
    )
    local_part = jnp.einsum(
        "pbr,bq->pqr", local_part, backward_table(count_y, basis_tables[1]), precision=TRANSFORM
    )
    return local_part


def coarse_terms(field, blocks, selector):
    count_x = field.shape[0] // PTS
    count_y = field.shape[1] // PTS
    count_z = field.shape[2] // PTS
    cells = count_x * count_y * count_z
    point = jnp.arange(field.shape[2], dtype=jnp.int32)
    along = (point[:, None] // PTS == jnp.arange(count_z, dtype=jnp.int32)[None, :]).astype(jnp.float32)
    sums = jnp.einsum("pqr,rc->pqc", field, along, precision=PRECISE)
    sums = jnp.sum(sums.reshape(count_x, PTS, count_y, PTS, count_z), axis=(1, 3))
    restricted = sums.reshape(cells) * (1.0 / PTS**3)
    terms = jnp.einsum("kpq,p->kq", blocks, restricted, precision=PRECISE)
    return jnp.einsum("kj,kq->jq", selector, terms, precision=PRECISE)


def element_table(blocks, columns, shape):
    count = blocks.shape[0]
    grid = (shape[0] // PTS, shape[1] // PTS, shape[2] // PTS)
    rows = jnp.transpose(blocks, (1, 0, 2)).reshape(grid + (count * blocks.shape[2],))
    cols = jnp.broadcast_to(columns.astype(jnp.float32), grid + (count,))
    return jnp.concatenate([rows, cols], axis=-1)


def coarse_rim(wholes, table, count, group):
    lo, whole, hi = wholes
    grid = table.shape[:3]
    width = (table.shape[3] - count) // count
    rows = table[..., : count * width].reshape(grid + (count, width))
    cols = table[..., count * width :]
    onehot = (cols[..., None] == jnp.arange(group, dtype=jnp.float32)).astype(jnp.float32)
    stacked = jnp.stack([lo] + [whole] * (grid[0] - 2) + [hi])
    picked = jnp.einsum("abckg,agq->abckq", onehot, stacked, precision=PRECISE)
    return jnp.sum(rows * picked, axis=(3, 4))


def spread_rim(values, width, shape):
    def table(length, count):
        point = jnp.arange(length + 2 * width, dtype=jnp.int32) - width + PTS
        element = jnp.arange(count, dtype=jnp.int32)
        return (point[:, None] // PTS == element[None, :]).astype(jnp.float32)

    grid = values.shape
    out = jnp.einsum("abc,rc->abr", values, table(shape[2], grid[2]), precision=PRECISE)
    out = jnp.einsum("abr,pa->pbr", out, table(shape[0], grid[0]), precision=PRECISE)
    return jnp.einsum("pbr,qb->pqr", out, table(shape[1], grid[1]), precision=PRECISE)


ALL = ("gx", "ga", "gz")


def butterfly_stages(axes):
    stages = []
    for axis in axes:
        size = lax.axis_size(axis)
        if size & (size - 1):
            stages.append(lambda value, axis=axis: lax.psum(value, axis))
            continue
        if size == 4:
            stages.append(functools.partial(sum_of_four, axis=axis))
            continue
        step = 1
        while step < size:
            pairs = [(i, i ^ step) for i in range(size)]
            stages.append(lambda value, axis=axis, pairs=pairs: value + lax.ppermute(value, axis, pairs))
            step *= 2
    return stages


def sum_of_four(value, axis):
    got = [value] + [lax.ppermute(value, axis, [(i, i ^ s) for i in range(4)]) for s in (1, 2, 3)]
    return (got[0] + got[1]) + (got[2] + got[3])


def butterfly(value, axes):
    for stage in butterfly_stages(axes):
        value = stage(value)
    return value


def lane_sums(a, b):
    return jnp.sum((a * b).reshape(-1, a.shape[-1]), axis=0)


def finish(total, count):
    return [jnp.sum(part) for part in jnp.split(total, count)]


def reduce_scalars(scalars):
    total = butterfly(lax.optimization_barrier(jnp.concatenate(scalars)), ALL)
    return finish(total, len(scalars))


def fold_four(payload, local, axis, dim, width):
    me = lax.axis_index(axis)
    length = local.shape[dim]
    last = lax.slice_in_dim(local, length - width, length, axis=dim)
    leading = lax.slice_in_dim(local, 0, width, axis=dim)
    even = me % 2 == 0
    count = payload.shape[0]

    def send(slab, step):
        message = jnp.concatenate([payload, slab.reshape(-1)])
        return lax.ppermute(message, axis, [(i, i ^ step) for i in range(4)])

    got_one = send(pick(even, last, leading), 1)
    got_two = lax.ppermute(payload, axis, [(i, i ^ 2) for i in range(4)])
    got_three = send(pick(me == 1, last, leading), 3)
    total = (payload + got_one[:count]) + (got_two + got_three[:count])
    from_one = got_one[count:].reshape(last.shape)
    from_three = got_three[count:].reshape(last.shape)
    odd = 1.0 - even.astype(jnp.float32)
    before = from_one * odd + from_three * (me == 2).astype(jnp.float32)
    after = from_one * (1.0 - odd) + from_three * (me == 1).astype(jnp.float32)
    return total, jnp.concatenate([before, local, after], axis=dim)


def reduce_coarse(local, buffer, scalars):
    count = sum(part.shape[0] for part in scalars)
    width = RIM + 1
    payload = jnp.concatenate([buffer.reshape(-1)] + list(scalars))
    local, payload = lax.optimization_barrier((local, payload))
    for axis, dim in (("ga", 1), ("gz", 2)):
        if lax.axis_size(axis) == 4:
            payload, local = fold_four(payload, local, axis, dim, width)
        else:
            payload = butterfly(payload, (axis,))
            local = pad_side(local, axis, dim, width)
        local, payload = lax.optimization_barrier((local, payload))
    size = payload.shape[0] - count
    whole = payload[:size].reshape(buffer.shape)
    if lax.axis_size("gx") == 2:
        first = lax.axis_index("gx") == 0
        length = local.shape[0]
        slab = pick(first, local[length - width :], local[:width])
        message = jnp.concatenate([payload, slab.reshape(-1)])
        got = lax.ppermute(message, "gx", [(0, 1), (1, 0)])
        total = payload[size:] + got[size : size + count]
        other = got[:size].reshape(buffer.shape)
        beside = got[size + count :].reshape(slab.shape)
        mine = first.astype(jnp.float32)
        lo, hi = other * (1.0 - mine), other * mine
        local = jnp.concatenate([beside * (1.0 - mine), local, beside * mine], axis=0)
    else:
        total = butterfly(payload[size:], ("gx",))
        gx = lax.axis_size("gx")
        up = [(i, i + 1) for i in range(gx - 1)]
        lo = lax.ppermute(whole, "gx", up)
        hi = lax.ppermute(whole, "gx", [(j, i) for i, j in up])
        local = pad_side(local, "gx", 0, width)
    return local, (lo, whole, hi), finish(total, len(scalars))


def body(right_side, diagonal, basis_tables, eigenvalues, coarse_blocks, coarse_columns):
    blocks = coarse_blocks.reshape(coarse_blocks.shape[3:])
    columns = coarse_columns.reshape(coarse_columns.shape[3])
    count = blocks.shape[0]
    group = lax.axis_size(("ga", "gz"))
    selector = (columns[:, None] == jnp.arange(group, dtype=jnp.int32)[None, :]).astype(jnp.float32)
    shape = right_side.shape
    wide_pair = jnp.stack([diagonal, right_side])
    table = element_table(blocks, columns, shape)
    for axis, dim in SIDES:
        wide_pair, table = pad_together([wide_pair, table], axis, (dim + 1, dim), (RIM, 1))
    wide_diagonal, wide_residual = wide_pair[0], wide_pair[1]
    inside = inside_grid(shape, RIM)

    def precondition_rim(wide_field, field):
        local = schwarz_part(wide_field, basis_tables, eigenvalues)
        return local, coarse_terms(field, blocks, selector)

    def coarse_on_rim(wholes):
        return spread_rim(coarse_rim(wholes, table, count, group), RIM + 1, shape)

    solution = jnp.zeros_like(right_side)
    residual = interior(wide_residual, RIM)
    wide_local, terms = precondition_rim(wide_residual, residual)
    wide_local, wholes, (square,) = reduce_coarse(wide_local, terms, [lane_sums(residual, residual)])
    for restart in range(CYCLES):
        residual = interior(wide_residual, RIM)
        initial_norm = jnp.sqrt(square)
        first_vector = residual / initial_norm
        wide_local_r, wholes_r = wide_local, wholes
        wide_zed = (wide_local_r + coarse_on_rim(wholes_r)) / initial_norm
        first_zed = interior(wide_zed, RIM + 1)
        wide_first = operate_rim(wide_zed, wide_diagonal, inside)
        first_image = interior(wide_first, RIM)
        wide_local, terms = precondition_rim(wide_first, first_image)
        wide_local_w, wholes_w, (first_proj, image_square) = reduce_coarse(
            wide_local, terms, [lane_sums(first_vector, first_image), lane_sums(first_image, first_image)]
        )
        first_len = jnp.sqrt(image_square - first_proj * first_proj)
        second_vector = (first_image - first_proj * first_vector) / first_len
        wide_second_zed = (wide_local_w + coarse_on_rim(wholes_w) - first_proj * wide_zed) / first_len
        second_zed = interior(wide_second_zed, RIM + 1)
        wide_second = operate_rim(wide_second_zed, wide_diagonal, inside)
        second_image = interior(wide_second, RIM)
        products = [
            lane_sums(first_vector, second_image),
            lane_sums(second_vector, second_image),
            lane_sums(second_image, second_image),
        ]
        last = restart == CYCLES - 1
        if last:
            upper_proj, lower_proj, second_square = reduce_scalars(products)
        else:
            wide_local, terms = precondition_rim(wide_second, second_image)
            wide_local_s, wholes_s, (upper_proj, lower_proj, second_square, cross) = reduce_coarse(
                wide_local, terms, products + [lane_sums(first_image, second_image)]
            )
        second_len = jnp.sqrt(second_square - upper_proj * upper_proj - lower_proj * lower_proj)
        gram_first = first_proj * first_proj + first_len * first_len
        gram_cross = first_proj * upper_proj + first_len * lower_proj
        gram_second = upper_proj * upper_proj + lower_proj * lower_proj + second_len * second_len
        target_first = initial_norm * first_proj
        target_second = initial_norm * upper_proj
        determinant = gram_first * gram_second - gram_cross * gram_cross
        weight_first = (gram_second * target_first - gram_cross * target_second) / determinant
        weight_second = (gram_first * target_second - gram_cross * target_first) / determinant
        solution = solution + weight_first * first_zed + weight_second * second_zed
        wide_residual = wide_residual - weight_first * wide_first - weight_second * wide_second
        if not last:
            wide_local = wide_local_r - weight_first * wide_local_w - weight_second * wide_local_s
            wholes = tuple(
                r - weight_first * w - weight_second * s for r, w, s in zip(wholes_r, wholes_w, wholes_s)
            )
            square = (
                square
                - 2.0 * weight_first * target_first
                - 2.0 * weight_second * target_second
                + weight_first * weight_first * image_square
                + 2.0 * weight_first * weight_second * cross
                + weight_second * weight_second * second_square
            )
    return (solution, interior(wide_residual, RIM))


def solution(mesh):
    in_specs = (
        P("gx", "ga", "gz"),
        P("gx", "ga", "gz"),
        P(),
        P(),
        P("gx", "ga", "gz", None, None, None),
        P("gx", "ga", "gz", None),
    )
    out_specs = (P("gx", "ga", "gz"), P("gx", "ga", "gz"))
    return jax.shard_map(body, mesh=mesh, in_specs=in_specs, out_specs=out_specs, check_vma=False)
```

```python
import functools

import jax
import jax.numpy as jnp
from jax import lax
from jax.sharding import PartitionSpec as P

PTS = 8
RIM = 2
WIDE = 12
CYCLES = 2


PRECISE = lax.Precision.HIGHEST
TRANSFORM = lax.Precision.HIGH


def pad_side(value, axis, dim, width):
    size, length = (lax.axis_size(axis), value.shape[dim])
    last = lax.slice_in_dim(value, length - width, length, axis=dim)
    leading = lax.slice_in_dim(value, 0, width, axis=dim)
    if size == 2:
        first = lax.axis_index(axis) == 0
        got = lax.ppermute(jnp.where(first, last, leading), axis, [(0, 1), (1, 0)])
        zero = jnp.zeros_like(got)
        before = jnp.where(first, zero, got)
        after = jnp.where(first, got, zero)
    else:
        up = [(i, (i + 1) % size) for i in range(size - 1)]
        down = [(j, i) for i, j in up]
        before = lax.ppermute(last, axis, up)
        after = lax.ppermute(leading, axis, down)
    return jnp.concatenate([before, value, after], axis=dim)


def padded_2(value, sides, width):
    for axis, dim in sides:
        value = pad_side(value, axis, dim, width)
    return value


def pad_together(values, axis, dims, widths):
    lasts, leads = [], []
    for value, dim, width in zip(values, dims, widths):
        length = value.shape[dim]
        lasts.append(lax.slice_in_dim(value, length - width, length, axis=dim))
        leads.append(lax.slice_in_dim(value, 0, width, axis=dim))

    def pack(slabs):
        return jnp.concatenate([slab.reshape(-1) for slab in slabs])

    def unpack(flat):
        pieces, at = [], 0
        for slab in lasts:
            pieces.append(flat[at : at + slab.size].reshape(slab.shape))
            at += slab.size
        return pieces

    size = lax.axis_size(axis)
    if size == 2:
        first = lax.axis_index(axis) == 0
        got = unpack(lax.ppermute(jnp.where(first, pack(lasts), pack(leads)), axis, [(0, 1), (1, 0)]))
        befores = [jnp.where(first, jnp.zeros_like(g), g) for g in got]
        afters = [jnp.where(first, g, jnp.zeros_like(g)) for g in got]
    elif size == 4:
        me = lax.axis_index(axis)
        even = me % 2 == 0
        to_one = jnp.where(even, pack(lasts), pack(leads))
        to_three = jnp.where(me == 1, pack(lasts), pack(leads))
        from_one = unpack(lax.ppermute(to_one, axis, [(i, i ^ 1) for i in range(4)]))
        from_three = unpack(lax.ppermute(to_three, axis, [(i, i ^ 3) for i in range(4)]))
        befores = [
            jnp.where(even, jnp.where(me == 2, t, jnp.zeros_like(t)), o)
            for o, t in zip(from_one, from_three)
        ]
        afters = [
            jnp.where(even, o, jnp.where(me == 1, t, jnp.zeros_like(t)))
            for o, t in zip(from_one, from_three)
        ]
    else:
        up = [(i, (i + 1) % size) for i in range(size - 1)]
        befores = unpack(lax.ppermute(pack(lasts), axis, up))
        afters = unpack(lax.ppermute(pack(leads), axis, [(j, i) for i, j in up]))
    return [
        jnp.concatenate([before, value, after], axis=dim)
        for before, value, after, dim in zip(befores, values, afters, dims)
    ]


SIDES = (("gx", 0), ("ga", 1), ("gz", 2))


def operate_rim(zed, diagonal, inside):
    centre = zed[1:-1, 1:-1, 1:-1]
    beside = zed[2:, 1:-1, 1:-1] + zed[:-2, 1:-1, 1:-1]
    beside = beside + zed[1:-1, 2:, 1:-1] + zed[1:-1, :-2, 1:-1]
    beside = beside + zed[1:-1, 1:-1, 2:] + zed[1:-1, 1:-1, :-2]
    return ((6.0 + diagonal) * centre - beside) * inside


def inside_grid(shape, width):
    result = None
    for axis, dim in SIDES:
        length = shape[dim]
        place = lax.axis_index(axis) * length - width + jnp.arange(length + 2 * width, dtype=jnp.int32)
        line = ((place >= 0) & (place < lax.axis_size(axis) * length)).astype(jnp.float32)
        view = [1, 1, 1]
        view[dim] = length + 2 * width
        line = line.reshape(view)
        result = line if result is None else result * line
    return result


def interior(value, width):
    return value[width:-width, width:-width, width:-width]


def forward_table(count, basis):
    row_index = jnp.arange(PTS * count + 2 * RIM, dtype=jnp.int32)
    element = jnp.arange(count, dtype=jnp.int32)
    offset = jnp.arange(WIDE, dtype=jnp.int32)
    select = (
        row_index[:, None, None] == PTS * element[None, :, None] + offset[None, None, :]
    ).astype(jnp.float32)
    table = jnp.einsum("rcj,jm->rcm", select, basis, precision=PRECISE)
    return table.reshape(PTS * count + 2 * RIM, count * WIDE)


def backward_table(count, basis):
    same = jnp.eye(count, dtype=jnp.float32)
    table = jnp.einsum("cd,im->cmdi", same, basis[RIM : RIM + PTS], precision=PRECISE)
    return table.reshape(count * WIDE, count * PTS)


def schwarz_part(padded, basis_tables, eigenvalues):
    count_x = (padded.shape[0] - 2 * RIM) // PTS
    count_y = (padded.shape[1] - 2 * RIM) // PTS
    count_z = (padded.shape[2] - 2 * RIM) // PTS
    spectral = jnp.einsum(
        "pqr,rc->pqc", padded, forward_table(count_z, basis_tables[2]), precision=TRANSFORM
    )
    spectral = jnp.einsum(
        "pqc,pa->aqc", spectral, forward_table(count_x, basis_tables[0]), precision=TRANSFORM
    )
    spectral = jnp.einsum(
        "aqc,qb->abc", spectral, forward_table(count_y, basis_tables[1]), precision=TRANSFORM
    )
    denominator = (
        jnp.tile(eigenvalues[0], count_x)[:, None, None]
        + jnp.tile(eigenvalues[1], count_y)[None, :, None]
    )
    denominator = denominator + jnp.tile(eigenvalues[2], count_z)[None, None, :]
    spectral = spectral / denominator
    local_part = jnp.einsum(
        "abc,cr->abr", spectral, backward_table(count_z, basis_tables[2]), precision=TRANSFORM
    )
    local_part = jnp.einsum(
        "abr,ap->pbr", local_part, backward_table(count_x, basis_tables[0]), precision=TRANSFORM
    )
    local_part = jnp.einsum(
        "pbr,bq->pqr", local_part, backward_table(count_y, basis_tables[1]), precision=TRANSFORM
    )
    return local_part


def coarse_terms(field, blocks, selector):
    count_x = field.shape[0] // PTS
    count_y = field.shape[1] // PTS
    count_z = field.shape[2] // PTS
    cells = count_x * count_y * count_z
    point = jnp.arange(field.shape[2], dtype=jnp.int32)
    along = (point[:, None] // PTS == jnp.arange(count_z, dtype=jnp.int32)[None, :]).astype(jnp.float32)
    sums = jnp.einsum("pqr,rc->pqc", field, along, precision=PRECISE)
    sums = jnp.sum(sums.reshape(count_x, PTS, count_y, PTS, count_z), axis=(1, 3))
    restricted = sums.reshape(cells) * (1.0 / PTS**3)
    terms = jnp.einsum("kpq,p->kq", blocks, restricted, precision=PRECISE)
    return jnp.einsum("kj,kq->jq", selector, terms, precision=PRECISE)


def element_table(blocks, columns, shape):
    count = blocks.shape[0]
    grid = (shape[0] // PTS, shape[1] // PTS, shape[2] // PTS)
    rows = jnp.transpose(blocks, (1, 0, 2)).reshape(grid + (count * blocks.shape[2],))
    cols = jnp.broadcast_to(columns.astype(jnp.float32), grid + (count,))
    return jnp.concatenate([rows, cols], axis=-1)


def coarse_rim(wholes, table, count, group):
    lo, whole, hi = wholes
    grid = table.shape[:3]
    width = (table.shape[3] - count) // count
    rows = table[..., : count * width].reshape(grid + (count, width))
    cols = table[..., count * width :]
    onehot = (cols[..., None] == jnp.arange(group, dtype=jnp.float32)).astype(jnp.float32)
    stacked = jnp.stack([lo] + [whole] * (grid[0] - 2) + [hi])
    picked = jnp.einsum("abckg,agq->abckq", onehot, stacked, precision=PRECISE)
    return jnp.sum(rows * picked, axis=(3, 4))


def spread_rim(values, width, shape):
    def table(length, count):
        point = jnp.arange(length + 2 * width, dtype=jnp.int32) - width + PTS
        element = jnp.arange(count, dtype=jnp.int32)
        return (point[:, None] // PTS == element[None, :]).astype(jnp.float32)

    grid = values.shape
    out = jnp.einsum("abc,rc->abr", values, table(shape[2], grid[2]), precision=PRECISE)
    out = jnp.einsum("abr,pa->pbr", out, table(shape[0], grid[0]), precision=PRECISE)
    return jnp.einsum("pbr,qb->pqr", out, table(shape[1], grid[1]), precision=PRECISE)


ALL = ("gx", "ga", "gz")


def butterfly_stages(axes):
    stages = []
    for axis in axes:
        size = lax.axis_size(axis)
        if size & (size - 1):
            stages.append(lambda value, axis=axis: lax.psum(value, axis))
            continue
        if size == 4:
            stages.append(functools.partial(sum_of_four, axis=axis))
            continue
        step = 1
        while step < size:
            pairs = [(i, i ^ step) for i in range(size)]
            stages.append(lambda value, axis=axis, pairs=pairs: value + lax.ppermute(value, axis, pairs))
            step *= 2
    return stages


def sum_of_four(value, axis):
    got = [value] + [lax.ppermute(value, axis, [(i, i ^ s) for i in range(4)]) for s in (1, 2, 3)]
    return (got[0] + got[1]) + (got[2] + got[3])


def butterfly(value, axes):
    for stage in butterfly_stages(axes):
        value = stage(value)
    return value


def lane_sums(a, b):
    return jnp.sum((a * b).reshape(-1, a.shape[-1]), axis=0)


def finish(total, count):
    return [jnp.sum(part) for part in jnp.split(total, count)]


def reduce_scalars(scalars):
    total = butterfly(lax.optimization_barrier(jnp.concatenate(scalars)), ALL)
    return finish(total, len(scalars))


def fold_four(payload, local, axis, dim, width):
    me = lax.axis_index(axis)
    length = local.shape[dim]
    last = lax.slice_in_dim(local, length - width, length, axis=dim)
    leading = lax.slice_in_dim(local, 0, width, axis=dim)
    even = me % 2 == 0
    count = payload.shape[0]

    def send(slab, step):
        message = jnp.concatenate([payload, slab.reshape(-1)])
        return lax.ppermute(message, axis, [(i, i ^ step) for i in range(4)])

    got_one = send(jnp.where(even, last, leading), 1)
    got_two = lax.ppermute(payload, axis, [(i, i ^ 2) for i in range(4)])
    got_three = send(jnp.where(me == 1, last, leading), 3)
    total = (payload + got_one[:count]) + (got_two + got_three[:count])
    from_one = got_one[count:].reshape(last.shape)
    from_three = got_three[count:].reshape(last.shape)
    zero = jnp.zeros_like(from_one)
    before = jnp.where(even, jnp.where(me == 2, from_three, zero), from_one)
    after = jnp.where(even, from_one, jnp.where(me == 1, from_three, zero))
    return total, jnp.concatenate([before, local, after], axis=dim)


def reduce_coarse(local, buffer, scalars):
    count = sum(part.shape[0] for part in scalars)
    width = RIM + 1
    payload = jnp.concatenate([buffer.reshape(-1)] + list(scalars))
    local, payload = lax.optimization_barrier((local, payload))
    for axis, dim in (("ga", 1), ("gz", 2)):
        if lax.axis_size(axis) == 4:
            payload, local = fold_four(payload, local, axis, dim, width)
        else:
            payload = butterfly(payload, (axis,))
            local = pad_side(local, axis, dim, width)
        local, payload = lax.optimization_barrier((local, payload))
    size = payload.shape[0] - count
    whole = payload[:size].reshape(buffer.shape)
    if lax.axis_size("gx") == 2:
        first = lax.axis_index("gx") == 0
        length = local.shape[0]
        slab = jnp.where(first, local[length - width :], local[:width])
        message = jnp.concatenate([payload, slab.reshape(-1)])
        got = lax.ppermute(message, "gx", [(0, 1), (1, 0)])
        total = payload[size:] + got[size : size + count]
        other = got[:size].reshape(buffer.shape)
        beside = got[size + count :].reshape(slab.shape)
        zero = jnp.zeros_like(other)
        lo, hi = jnp.where(first, zero, other), jnp.where(first, other, zero)
        flat = jnp.zeros_like(beside)
        local = jnp.concatenate(
            [jnp.where(first, flat, beside), local, jnp.where(first, beside, flat)], axis=0
        )
    else:
        total = butterfly(payload[size:], ("gx",))
        gx = lax.axis_size("gx")
        up = [(i, i + 1) for i in range(gx - 1)]
        lo = lax.ppermute(whole, "gx", up)
        hi = lax.ppermute(whole, "gx", [(j, i) for i, j in up])
        local = pad_side(local, "gx", 0, width)
    return local, (lo, whole, hi), finish(total, len(scalars))


def body(right_side, diagonal, basis_tables, eigenvalues, coarse_blocks, coarse_columns):
    blocks = coarse_blocks.reshape(coarse_blocks.shape[3:])
    columns = coarse_columns.reshape(coarse_columns.shape[3])
    count = blocks.shape[0]
    group = lax.axis_size(("ga", "gz"))
    selector = (columns[:, None] == jnp.arange(group, dtype=jnp.int32)[None, :]).astype(jnp.float32)
    selector = lax.optimization_barrier(selector)
    shape = right_side.shape
    wide_pair = jnp.stack([diagonal, right_side])
    table = element_table(blocks, columns, shape)
    for axis, dim in SIDES:
        wide_pair, table = pad_together([wide_pair, table], axis, (dim + 1, dim), (RIM, 1))
    wide_diagonal, wide_residual = wide_pair[0], wide_pair[1]
    inside = inside_grid(shape, RIM)

    def precondition_rim(wide_field, field):
        local = schwarz_part(wide_field, basis_tables, eigenvalues)
        return local, coarse_terms(field, blocks, selector)

    def coarse_on_rim(wholes):
        return spread_rim(coarse_rim(wholes, table, count, group), RIM + 1, shape)

    solution = jnp.zeros_like(right_side)
    residual = interior(wide_residual, RIM)
    wide_local, terms = precondition_rim(wide_residual, residual)
    wide_local, wholes, (square,) = reduce_coarse(wide_local, terms, [lane_sums(residual, residual)])
    for restart in range(CYCLES):
        residual = interior(wide_residual, RIM)
        initial_norm = jnp.sqrt(square)
        first_vector = residual / initial_norm
        wide_local_r, wholes_r = wide_local, wholes
        wide_zed = (wide_local_r + coarse_on_rim(wholes_r)) / initial_norm
        first_zed = interior(wide_zed, RIM + 1)
        wide_first = operate_rim(wide_zed, wide_diagonal, inside)
        first_image = interior(wide_first, RIM)
        wide_local, terms = precondition_rim(wide_first, first_image)
        wide_local_w, wholes_w, (first_proj, image_square) = reduce_coarse(
            wide_local, terms, [lane_sums(first_vector, first_image), lane_sums(first_image, first_image)]
        )
        first_len = jnp.sqrt(image_square - first_proj * first_proj)
        second_vector = (first_image - first_proj * first_vector) / first_len
        wide_second_zed = (wide_local_w + coarse_on_rim(wholes_w) - first_proj * wide_zed) / first_len
        second_zed = interior(wide_second_zed, RIM + 1)
        wide_second = operate_rim(wide_second_zed, wide_diagonal, inside)
        second_image = interior(wide_second, RIM)
        products = [
            lane_sums(first_vector, second_image),
            lane_sums(second_vector, second_image),
            lane_sums(second_image, second_image),
        ]
        last = restart == CYCLES - 1
        if last:
            upper_proj, lower_proj, second_square = reduce_scalars(products)
        else:
            wide_local, terms = precondition_rim(wide_second, second_image)
            wide_local_s, wholes_s, (upper_proj, lower_proj, second_square, cross) = reduce_coarse(
                wide_local, terms, products + [lane_sums(first_image, second_image)]
            )
        second_len = jnp.sqrt(second_square - upper_proj * upper_proj - lower_proj * lower_proj)
        gram_first = first_proj * first_proj + first_len * first_len
        gram_cross = first_proj * upper_proj + first_len * lower_proj
        gram_second = upper_proj * upper_proj + lower_proj * lower_proj + second_len * second_len
        target_first = initial_norm * first_proj
        target_second = initial_norm * upper_proj
        determinant = gram_first * gram_second - gram_cross * gram_cross
        weight_first = (gram_second * target_first - gram_cross * target_second) / determinant
        weight_second = (gram_first * target_second - gram_cross * target_first) / determinant
        solution = solution + weight_first * first_zed + weight_second * second_zed
        wide_residual = wide_residual - weight_first * wide_first - weight_second * wide_second
        if not last:
            wide_local = wide_local_r - weight_first * wide_local_w - weight_second * wide_local_s
            wholes = tuple(
                r - weight_first * w - weight_second * s for r, w, s in zip(wholes_r, wholes_w, wholes_s)
            )
            square = (
                square
                - 2.0 * weight_first * target_first
                - 2.0 * weight_second * target_second
                + weight_first * weight_first * image_square
                + 2.0 * weight_first * weight_second * cross
                + weight_second * weight_second * second_square
            )
    return (solution, interior(wide_residual, RIM))


def solution(mesh):
    in_specs = (
        P("gx", "ga", "gz"),
        P("gx", "ga", "gz"),
        P(),
        P(),
        P("gx", "ga", "gz", None, None, None),
        P("gx", "ga", "gz", None),
    )
    out_specs = (P("gx", "ga", "gz"), P("gx", "ga", "gz"))
    return jax.shard_map(body, mesh=mesh, in_specs=in_specs, out_specs=out_specs, check_vma=False)
```

```python
import functools

import jax
import jax.numpy as jnp
from jax import lax
from jax.sharding import PartitionSpec as P

PTS = 8
RIM = 2
WIDE = 12
CYCLES = 2


PRECISE = lax.Precision.HIGHEST
TRANSFORM = lax.Precision.HIGH


def pad_side(value, axis, dim, width):
    size, length = (lax.axis_size(axis), value.shape[dim])
    last = lax.slice_in_dim(value, length - width, length, axis=dim)
    leading = lax.slice_in_dim(value, 0, width, axis=dim)
    if size == 2:
        first = lax.axis_index(axis) == 0
        got = lax.ppermute(jnp.where(first, last, leading), axis, [(0, 1), (1, 0)])
        zero = jnp.zeros_like(got)
        before = jnp.where(first, zero, got)
        after = jnp.where(first, got, zero)
    else:
        up = [(i, (i + 1) % size) for i in range(size - 1)]
        down = [(j, i) for i, j in up]
        before = lax.ppermute(last, axis, up)
        after = lax.ppermute(leading, axis, down)
    return jnp.concatenate([before, value, after], axis=dim)


def padded_2(value, sides, width):
    for axis, dim in sides:
        value = pad_side(value, axis, dim, width)
    return value


def pad_together(values, axis, dims, widths):
    lasts, leads = [], []
    for value, dim, width in zip(values, dims, widths):
        length = value.shape[dim]
        lasts.append(lax.slice_in_dim(value, length - width, length, axis=dim))
        leads.append(lax.slice_in_dim(value, 0, width, axis=dim))

    def pack(slabs):
        return jnp.concatenate([slab.reshape(-1) for slab in slabs])

    def unpack(flat):
        pieces, at = [], 0
        for slab in lasts:
            pieces.append(flat[at : at + slab.size].reshape(slab.shape))
            at += slab.size
        return pieces

    size = lax.axis_size(axis)
    if size == 2:
        first = lax.axis_index(axis) == 0
        got = unpack(lax.ppermute(jnp.where(first, pack(lasts), pack(leads)), axis, [(0, 1), (1, 0)]))
        befores = [jnp.where(first, jnp.zeros_like(g), g) for g in got]
        afters = [jnp.where(first, g, jnp.zeros_like(g)) for g in got]
    elif size == 4:
        me = lax.axis_index(axis)
        even = me % 2 == 0
        to_one = jnp.where(even, pack(lasts), pack(leads))
        to_three = jnp.where(me == 1, pack(lasts), pack(leads))
        from_one = unpack(lax.ppermute(to_one, axis, [(i, i ^ 1) for i in range(4)]))
        from_three = unpack(lax.ppermute(to_three, axis, [(i, i ^ 3) for i in range(4)]))
        befores = [
            jnp.where(even, jnp.where(me == 2, t, jnp.zeros_like(t)), o)
            for o, t in zip(from_one, from_three)
        ]
        afters = [
            jnp.where(even, o, jnp.where(me == 1, t, jnp.zeros_like(t)))
            for o, t in zip(from_one, from_three)
        ]
    else:
        up = [(i, (i + 1) % size) for i in range(size - 1)]
        befores = unpack(lax.ppermute(pack(lasts), axis, up))
        afters = unpack(lax.ppermute(pack(leads), axis, [(j, i) for i, j in up]))
    return [
        jnp.concatenate([before, value, after], axis=dim)
        for before, value, after, dim in zip(befores, values, afters, dims)
    ]


SIDES = (("gx", 0), ("ga", 1), ("gz", 2))


def operate_rim(zed, diagonal, inside):
    centre = zed[1:-1, 1:-1, 1:-1]
    beside = zed[2:, 1:-1, 1:-1] + zed[:-2, 1:-1, 1:-1]
    beside = beside + zed[1:-1, 2:, 1:-1] + zed[1:-1, :-2, 1:-1]
    beside = beside + zed[1:-1, 1:-1, 2:] + zed[1:-1, 1:-1, :-2]
    return ((6.0 + diagonal) * centre - beside) * inside


def inside_grid(shape, width):
    result = None
    for axis, dim in SIDES:
        length = shape[dim]
        place = lax.axis_index(axis) * length - width + jnp.arange(length + 2 * width, dtype=jnp.int32)
        line = ((place >= 0) & (place < lax.axis_size(axis) * length)).astype(jnp.float32)
        view = [1, 1, 1]
        view[dim] = length + 2 * width
        line = line.reshape(view)
        result = line if result is None else result * line
    return result


def interior(value, width):
    return value[width:-width, width:-width, width:-width]


def forward_table(count, basis):
    row_index = jnp.arange(PTS * count + 2 * RIM, dtype=jnp.int32)
    element = jnp.arange(count, dtype=jnp.int32)
    offset = jnp.arange(WIDE, dtype=jnp.int32)
    select = (
        row_index[:, None, None] == PTS * element[None, :, None] + offset[None, None, :]
    ).astype(jnp.float32)
    table = jnp.einsum("rcj,jm->rcm", select, basis, precision=PRECISE)
    return table.reshape(PTS * count + 2 * RIM, count * WIDE)


def backward_table(count, basis):
    same = jnp.eye(count, dtype=jnp.float32)
    table = jnp.einsum("cd,im->cmdi", same, basis[RIM : RIM + PTS], precision=PRECISE)
    return table.reshape(count * WIDE, count * PTS)


def schwarz_part(padded, basis_tables, eigenvalues):
    count_x = (padded.shape[0] - 2 * RIM) // PTS
    count_y = (padded.shape[1] - 2 * RIM) // PTS
    count_z = (padded.shape[2] - 2 * RIM) // PTS
    spectral = jnp.einsum(
        "pqr,rc->pqc", padded, forward_table(count_z, basis_tables[2]), precision=TRANSFORM
    )
    spectral = jnp.einsum(
        "pqc,pa->aqc", spectral, forward_table(count_x, basis_tables[0]), precision=TRANSFORM
    )
    spectral = jnp.einsum(
        "aqc,qb->abc", spectral, forward_table(count_y, basis_tables[1]), precision=TRANSFORM
    )
    denominator = (
        jnp.tile(eigenvalues[0], count_x)[:, None, None]
        + jnp.tile(eigenvalues[1], count_y)[None, :, None]
    )
    denominator = denominator + jnp.tile(eigenvalues[2], count_z)[None, None, :]
    spectral = spectral / denominator
    local_part = jnp.einsum(
        "abc,cr->abr", spectral, backward_table(count_z, basis_tables[2]), precision=TRANSFORM
    )
    local_part = jnp.einsum(
        "abr,ap->pbr", local_part, backward_table(count_x, basis_tables[0]), precision=TRANSFORM
    )
    local_part = jnp.einsum(
        "pbr,bq->pqr", local_part, backward_table(count_y, basis_tables[1]), precision=TRANSFORM
    )
    return local_part


def coarse_terms(field, blocks, selector):
    count_x = field.shape[0] // PTS
    count_y = field.shape[1] // PTS
    count_z = field.shape[2] // PTS
    cells = count_x * count_y * count_z
    point = jnp.arange(field.shape[2], dtype=jnp.int32)
    along = (point[:, None] // PTS == jnp.arange(count_z, dtype=jnp.int32)[None, :]).astype(jnp.float32)
    sums = jnp.einsum("pqr,rc->pqc", field, along, precision=PRECISE)
    sums = jnp.sum(sums.reshape(count_x, PTS, count_y, PTS, count_z), axis=(1, 3))
    restricted = sums.reshape(cells) * (1.0 / PTS**3)
    terms = jnp.einsum("kpq,p->kq", blocks, restricted, precision=PRECISE)
    return jnp.einsum("kj,kq->jq", selector, terms, precision=PRECISE)


def element_table(blocks, columns, shape):
    count = blocks.shape[0]
    grid = (shape[0] // PTS, shape[1] // PTS, shape[2] // PTS)
    rows = jnp.transpose(blocks, (1, 0, 2)).reshape(grid + (count * blocks.shape[2],))
    cols = jnp.broadcast_to(columns.astype(jnp.float32), grid + (count,))
    return jnp.concatenate([rows, cols], axis=-1)


def coarse_rim(wholes, table, count, group):
    lo, whole, hi = wholes
    grid = table.shape[:3]
    width = (table.shape[3] - count) // count
    rows = table[..., : count * width].reshape(grid + (count, width))
    cols = table[..., count * width :]
    onehot = (cols[..., None] == jnp.arange(group, dtype=jnp.float32)).astype(jnp.float32)
    stacked = jnp.stack([lo] + [whole] * (grid[0] - 2) + [hi])
    picked = jnp.einsum("abckg,agq->abckq", onehot, stacked, precision=PRECISE)
    return jnp.sum(rows * picked, axis=(3, 4))


def spread_rim(values, width, shape):
    def table(length, count):
        point = jnp.arange(length + 2 * width, dtype=jnp.int32) - width + PTS
        element = jnp.arange(count, dtype=jnp.int32)
        return (point[:, None] // PTS == element[None, :]).astype(jnp.float32)

    grid = values.shape
    out = jnp.einsum("abc,rc->abr", values, table(shape[2], grid[2]), precision=PRECISE)
    out = jnp.einsum("abr,pa->pbr", out, table(shape[0], grid[0]), precision=PRECISE)
    return jnp.einsum("pbr,qb->pqr", out, table(shape[1], grid[1]), precision=PRECISE)


ALL = ("gx", "ga", "gz")


def butterfly_stages(axes):
    stages = []
    for axis in axes:
        size = lax.axis_size(axis)
        if size & (size - 1):
            stages.append(lambda value, axis=axis: lax.psum(value, axis))
            continue
        if size == 4:
            stages.append(functools.partial(sum_of_four, axis=axis))
            continue
        step = 1
        while step < size:
            pairs = [(i, i ^ step) for i in range(size)]
            stages.append(lambda value, axis=axis, pairs=pairs: value + lax.ppermute(value, axis, pairs))
            step *= 2
    return stages


def sum_of_four(value, axis):
    got = [value] + [lax.ppermute(value, axis, [(i, i ^ s) for i in range(4)]) for s in (1, 2, 3)]
    return (got[0] + got[1]) + (got[2] + got[3])


def butterfly(value, axes):
    for stage in butterfly_stages(axes):
        value = stage(value)
    return value


def lane_sums(a, b):
    return jnp.sum((a * b).reshape(-1, a.shape[-1]), axis=0)


def finish(total, count):
    return [jnp.sum(part) for part in jnp.split(total, count)]


def reduce_scalars(scalars):
    total = butterfly(lax.optimization_barrier(jnp.concatenate(scalars)), ALL)
    return finish(total, len(scalars))


def fold_four(payload, local, axis, dim, width):
    me = lax.axis_index(axis)
    length = local.shape[dim]
    last = lax.slice_in_dim(local, length - width, length, axis=dim)
    leading = lax.slice_in_dim(local, 0, width, axis=dim)
    even = me % 2 == 0
    count = payload.shape[0]

    def send(slab, step):
        message = jnp.concatenate([payload, slab.reshape(-1)])
        return lax.ppermute(message, axis, [(i, i ^ step) for i in range(4)])

    got_one = send(jnp.where(even, last, leading), 1)
    got_two = lax.ppermute(payload, axis, [(i, i ^ 2) for i in range(4)])
    got_three = send(jnp.where(me == 1, last, leading), 3)
    total = (payload + got_one[:count]) + (got_two + got_three[:count])
    from_one = got_one[count:].reshape(last.shape)
    from_three = got_three[count:].reshape(last.shape)
    zero = jnp.zeros_like(from_one)
    before = jnp.where(even, jnp.where(me == 2, from_three, zero), from_one)
    after = jnp.where(even, from_one, jnp.where(me == 1, from_three, zero))
    return total, jnp.concatenate([before, local, after], axis=dim)


def reduce_coarse(local, buffer, scalars):
    count = sum(part.shape[0] for part in scalars)
    width = RIM + 1
    payload = jnp.concatenate([buffer.reshape(-1)] + list(scalars))
    local, payload = lax.optimization_barrier((local, payload))
    for axis, dim in (("ga", 1), ("gz", 2)):
        if lax.axis_size(axis) == 4:
            payload, local = fold_four(payload, local, axis, dim, width)
        else:
            payload = butterfly(payload, (axis,))
            local = pad_side(local, axis, dim, width)
        local, payload = lax.optimization_barrier((local, payload))
    size = payload.shape[0] - count
    whole = payload[:size].reshape(buffer.shape)
    if lax.axis_size("gx") == 2:
        first = lax.axis_index("gx") == 0
        length = local.shape[0]
        slab = jnp.where(first, local[length - width :], local[:width])
        got = lax.ppermute(payload, "gx", [(0, 1), (1, 0)])
        beside = lax.ppermute(slab, "gx", [(0, 1), (1, 0)])
        total = payload[size:] + got[size:]
        other = got[:size].reshape(buffer.shape)
        zero = jnp.zeros_like(other)
        lo, hi = jnp.where(first, zero, other), jnp.where(first, other, zero)
        flat = jnp.zeros_like(beside)
        local = jnp.concatenate(
            [jnp.where(first, flat, beside), local, jnp.where(first, beside, flat)], axis=0
        )
    else:
        total = butterfly(payload[size:], ("gx",))
        gx = lax.axis_size("gx")
        up = [(i, i + 1) for i in range(gx - 1)]
        lo = lax.ppermute(whole, "gx", up)
        hi = lax.ppermute(whole, "gx", [(j, i) for i, j in up])
        local = pad_side(local, "gx", 0, width)
    return local, (lo, whole, hi), finish(total, len(scalars))


def body(right_side, diagonal, basis_tables, eigenvalues, coarse_blocks, coarse_columns):
    blocks = coarse_blocks.reshape(coarse_blocks.shape[3:])
    columns = coarse_columns.reshape(coarse_columns.shape[3])
    count = blocks.shape[0]
    group = lax.axis_size(("ga", "gz"))
    selector = (columns[:, None] == jnp.arange(group, dtype=jnp.int32)[None, :]).astype(jnp.float32)
    shape = right_side.shape
    wide_pair = jnp.stack([diagonal, right_side])
    table = element_table(blocks, columns, shape)
    for axis, dim in SIDES:
        wide_pair, table = pad_together([wide_pair, table], axis, (dim + 1, dim), (RIM, 1))
    wide_diagonal, wide_residual = wide_pair[0], wide_pair[1]
    inside = inside_grid(shape, RIM)

    def precondition_rim(wide_field, field):
        local = schwarz_part(wide_field, basis_tables, eigenvalues)
        return local, coarse_terms(field, blocks, selector)

    def coarse_on_rim(wholes):
        return spread_rim(coarse_rim(wholes, table, count, group), RIM + 1, shape)

    solution = jnp.zeros_like(right_side)
    residual = interior(wide_residual, RIM)
    wide_local, terms = precondition_rim(wide_residual, residual)
    wide_local, wholes, (square,) = reduce_coarse(wide_local, terms, [lane_sums(residual, residual)])
    for restart in range(CYCLES):
        residual = interior(wide_residual, RIM)
        initial_norm = jnp.sqrt(square)
        first_vector = residual / initial_norm
        wide_local_r, wholes_r = wide_local, wholes
        wide_zed = (wide_local_r + coarse_on_rim(wholes_r)) / initial_norm
        first_zed = interior(wide_zed, RIM + 1)
        wide_first = operate_rim(wide_zed, wide_diagonal, inside)
        first_image = interior(wide_first, RIM)
        wide_local, terms = precondition_rim(wide_first, first_image)
        wide_local_w, wholes_w, (first_proj, image_square) = reduce_coarse(
            wide_local, terms, [lane_sums(first_vector, first_image), lane_sums(first_image, first_image)]
        )
        first_len = jnp.sqrt(image_square - first_proj * first_proj)
        second_vector = (first_image - first_proj * first_vector) / first_len
        wide_second_zed = (wide_local_w + coarse_on_rim(wholes_w) - first_proj * wide_zed) / first_len
        second_zed = interior(wide_second_zed, RIM + 1)
        wide_second = operate_rim(wide_second_zed, wide_diagonal, inside)
        second_image = interior(wide_second, RIM)
        products = [
            lane_sums(first_vector, second_image),
            lane_sums(second_vector, second_image),
            lane_sums(second_image, second_image),
        ]
        last = restart == CYCLES - 1
        if last:
            upper_proj, lower_proj, second_square = reduce_scalars(products)
        else:
            wide_local, terms = precondition_rim(wide_second, second_image)
            wide_local_s, wholes_s, (upper_proj, lower_proj, second_square, cross) = reduce_coarse(
                wide_local, terms, products + [lane_sums(first_image, second_image)]
            )
        second_len = jnp.sqrt(second_square - upper_proj * upper_proj - lower_proj * lower_proj)
        gram_first = first_proj * first_proj + first_len * first_len
        gram_cross = first_proj * upper_proj + first_len * lower_proj
        gram_second = upper_proj * upper_proj + lower_proj * lower_proj + second_len * second_len
        target_first = initial_norm * first_proj
        target_second = initial_norm * upper_proj
        determinant = gram_first * gram_second - gram_cross * gram_cross
        weight_first = (gram_second * target_first - gram_cross * target_second) / determinant
        weight_second = (gram_first * target_second - gram_cross * target_first) / determinant
        solution = solution + weight_first * first_zed + weight_second * second_zed
        wide_residual = wide_residual - weight_first * wide_first - weight_second * wide_second
        if not last:
            wide_local = wide_local_r - weight_first * wide_local_w - weight_second * wide_local_s
            wholes = tuple(
                r - weight_first * w - weight_second * s for r, w, s in zip(wholes_r, wholes_w, wholes_s)
            )
            square = (
                square
                - 2.0 * weight_first * target_first
                - 2.0 * weight_second * target_second
                + weight_first * weight_first * image_square
                + 2.0 * weight_first * weight_second * cross
                + weight_second * weight_second * second_square
            )
    return (solution, interior(wide_residual, RIM))


def solution(mesh):
    in_specs = (
        P("gx", "ga", "gz"),
        P("gx", "ga", "gz"),
        P(),
        P(),
        P("gx", "ga", "gz", None, None, None),
        P("gx", "ga", "gz", None),
    )
    out_specs = (P("gx", "ga", "gz"), P("gx", "ga", "gz"))
    return jax.shard_map(body, mesh=mesh, in_specs=in_specs, out_specs=out_specs, check_vma=False)
```

```python
import functools

import jax
import jax.numpy as jnp
from jax import lax
from jax.sharding import PartitionSpec as P

PTS = 8
RIM = 2
WIDE = 12
CYCLES = 2


PRECISE = lax.Precision.HIGHEST
TRANSFORM = lax.Precision.HIGH


def pad_side(value, axis, dim, width):
    size, length = (lax.axis_size(axis), value.shape[dim])
    last = lax.slice_in_dim(value, length - width, length, axis=dim)
    leading = lax.slice_in_dim(value, 0, width, axis=dim)
    if size == 2:
        first = lax.axis_index(axis) == 0
        got = lax.ppermute(jnp.where(first, last, leading), axis, [(0, 1), (1, 0)])
        zero = jnp.zeros_like(got)
        before = jnp.where(first, zero, got)
        after = jnp.where(first, got, zero)
    else:
        up = [(i, (i + 1) % size) for i in range(size - 1)]
        down = [(j, i) for i, j in up]
        before = lax.ppermute(last, axis, up)
        after = lax.ppermute(leading, axis, down)
    return jnp.concatenate([before, value, after], axis=dim)


def padded_2(value, sides, width):
    for axis, dim in sides:
        value = pad_side(value, axis, dim, width)
    return value


def pad_together(values, axis, dims, widths):
    lasts, leads = [], []
    for value, dim, width in zip(values, dims, widths):
        length = value.shape[dim]
        lasts.append(lax.slice_in_dim(value, length - width, length, axis=dim))
        leads.append(lax.slice_in_dim(value, 0, width, axis=dim))

    def pack(slabs):
        return jnp.concatenate([slab.reshape(-1) for slab in slabs])

    def unpack(flat):
        pieces, at = [], 0
        for slab in lasts:
            pieces.append(flat[at : at + slab.size].reshape(slab.shape))
            at += slab.size
        return pieces

    size = lax.axis_size(axis)
    if size == 2:
        first = lax.axis_index(axis) == 0
        got = unpack(lax.ppermute(jnp.where(first, pack(lasts), pack(leads)), axis, [(0, 1), (1, 0)]))
        befores = [jnp.where(first, jnp.zeros_like(g), g) for g in got]
        afters = [jnp.where(first, g, jnp.zeros_like(g)) for g in got]
    elif size == 4:
        me = lax.axis_index(axis)
        even = me % 2 == 0
        to_one = jnp.where(even, pack(lasts), pack(leads))
        to_three = jnp.where(me == 1, pack(lasts), pack(leads))
        from_one = unpack(lax.ppermute(to_one, axis, [(i, i ^ 1) for i in range(4)]))
        from_three = unpack(lax.ppermute(to_three, axis, [(i, i ^ 3) for i in range(4)]))
        befores = [
            jnp.where(even, jnp.where(me == 2, t, jnp.zeros_like(t)), o)
            for o, t in zip(from_one, from_three)
        ]
        afters = [
            jnp.where(even, o, jnp.where(me == 1, t, jnp.zeros_like(t)))
            for o, t in zip(from_one, from_three)
        ]
    else:
        up = [(i, (i + 1) % size) for i in range(size - 1)]
        befores = unpack(lax.ppermute(pack(lasts), axis, up))
        afters = unpack(lax.ppermute(pack(leads), axis, [(j, i) for i, j in up]))
    return [
        jnp.concatenate([before, value, after], axis=dim)
        for before, value, after, dim in zip(befores, values, afters, dims)
    ]


SIDES = (("gx", 0), ("ga", 1), ("gz", 2))


def operate_rim(zed, diagonal, inside):
    centre = zed[1:-1, 1:-1, 1:-1]
    beside = zed[2:, 1:-1, 1:-1] + zed[:-2, 1:-1, 1:-1]
    beside = beside + zed[1:-1, 2:, 1:-1] + zed[1:-1, :-2, 1:-1]
    beside = beside + zed[1:-1, 1:-1, 2:] + zed[1:-1, 1:-1, :-2]
    return ((6.0 + diagonal) * centre - beside) * inside


def inside_grid(shape, width):
    result = None
    for axis, dim in SIDES:
        length = shape[dim]
        place = lax.axis_index(axis) * length - width + jnp.arange(length + 2 * width, dtype=jnp.int32)
        line = ((place >= 0) & (place < lax.axis_size(axis) * length)).astype(jnp.float32)
        view = [1, 1, 1]
        view[dim] = length + 2 * width
        line = line.reshape(view)
        result = line if result is None else result * line
    return result


def interior(value, width):
    return value[width:-width, width:-width, width:-width]


def forward_table(count, basis):
    row_index = jnp.arange(PTS * count + 2 * RIM, dtype=jnp.int32)
    element = jnp.arange(count, dtype=jnp.int32)
    offset = jnp.arange(WIDE, dtype=jnp.int32)
    select = (
        row_index[:, None, None] == PTS * element[None, :, None] + offset[None, None, :]
    ).astype(jnp.float32)
    table = jnp.einsum("rcj,jm->rcm", select, basis, precision=PRECISE)
    return table.reshape(PTS * count + 2 * RIM, count * WIDE)


def backward_table(count, basis):
    same = jnp.eye(count, dtype=jnp.float32)
    table = jnp.einsum("cd,im->cmdi", same, basis[RIM : RIM + PTS], precision=PRECISE)
    return table.reshape(count * WIDE, count * PTS)


def schwarz_part(padded, basis_tables, eigenvalues):
    count_x = (padded.shape[0] - 2 * RIM) // PTS
    count_y = (padded.shape[1] - 2 * RIM) // PTS
    count_z = (padded.shape[2] - 2 * RIM) // PTS
    spectral = jnp.einsum(
        "pqr,rc->pqc", padded, forward_table(count_z, basis_tables[2]), precision=TRANSFORM
    )
    spectral = jnp.einsum(
        "pqc,pa->aqc", spectral, forward_table(count_x, basis_tables[0]), precision=TRANSFORM
    )
    spectral = jnp.einsum(
        "aqc,qb->abc", spectral, forward_table(count_y, basis_tables[1]), precision=TRANSFORM
    )
    denominator = (
        jnp.tile(eigenvalues[0], count_x)[:, None, None]
        + jnp.tile(eigenvalues[1], count_y)[None, :, None]
    )
    denominator = denominator + jnp.tile(eigenvalues[2], count_z)[None, None, :]
    spectral = spectral / denominator
    local_part = jnp.einsum(
        "abc,cr->abr", spectral, backward_table(count_z, basis_tables[2]), precision=TRANSFORM
    )
    local_part = jnp.einsum(
        "abr,ap->pbr", local_part, backward_table(count_x, basis_tables[0]), precision=TRANSFORM
    )
    local_part = jnp.einsum(
        "pbr,bq->pqr", local_part, backward_table(count_y, basis_tables[1]), precision=TRANSFORM
    )
    return local_part


def coarse_terms(field, blocks, selector):
    count_x = field.shape[0] // PTS
    count_y = field.shape[1] // PTS
    count_z = field.shape[2] // PTS
    cells = count_x * count_y * count_z
    point = jnp.arange(field.shape[2], dtype=jnp.int32)
    along = (point[:, None] // PTS == jnp.arange(count_z, dtype=jnp.int32)[None, :]).astype(jnp.float32)
    sums = jnp.einsum("pqr,rc->pqc", field, along, precision=PRECISE)
    sums = jnp.sum(sums.reshape(count_x, PTS, count_y, PTS, count_z), axis=(1, 3))
    restricted = sums.reshape(cells) * (1.0 / PTS**3)
    terms = jnp.einsum("kpq,p->kq", blocks, restricted, precision=PRECISE)
    return jnp.einsum("kj,kq->jq", selector, terms, precision=PRECISE)


def element_table(blocks, columns, shape):
    count = blocks.shape[0]
    grid = (shape[0] // PTS, shape[1] // PTS, shape[2] // PTS)
    rows = jnp.transpose(blocks, (1, 0, 2)).reshape(grid + (count * blocks.shape[2],))
    cols = jnp.broadcast_to(columns.astype(jnp.float32), grid + (count,))
    return jnp.concatenate([rows, cols], axis=-1)


def coarse_rim(wholes, table, count, group):
    lo, whole, hi = wholes
    grid = table.shape[:3]
    width = (table.shape[3] - count) // count
    rows = table[..., : count * width].reshape(grid + (count, width))
    cols = table[..., count * width :]
    onehot = (cols[..., None] == jnp.arange(group, dtype=jnp.float32)).astype(jnp.float32)
    stacked = jnp.stack([lo] + [whole] * (grid[0] - 2) + [hi])
    picked = jnp.einsum("abckg,agq->abckq", onehot, stacked, precision=PRECISE)
    return jnp.sum(rows * picked, axis=(3, 4))


def spread_rim(values, width, shape):
    def table(length, count):
        point = jnp.arange(length + 2 * width, dtype=jnp.int32) - width + PTS
        element = jnp.arange(count, dtype=jnp.int32)
        return (point[:, None] // PTS == element[None, :]).astype(jnp.float32)

    grid = values.shape
    out = jnp.einsum("abc,rc->abr", values, table(shape[2], grid[2]), precision=PRECISE)
    out = jnp.einsum("abr,pa->pbr", out, table(shape[0], grid[0]), precision=PRECISE)
    return jnp.einsum("pbr,qb->pqr", out, table(shape[1], grid[1]), precision=PRECISE)


ALL = ("gx", "ga", "gz")


def butterfly_stages(axes):
    stages = []
    for axis in axes:
        size = lax.axis_size(axis)
        if size & (size - 1):
            stages.append(lambda value, axis=axis: lax.psum(value, axis))
            continue
        if size == 4:
            stages.append(functools.partial(sum_of_four, axis=axis))
            continue
        step = 1
        while step < size:
            pairs = [(i, i ^ step) for i in range(size)]
            stages.append(lambda value, axis=axis, pairs=pairs: value + lax.ppermute(value, axis, pairs))
            step *= 2
    return stages


def sum_of_four(value, axis):
    got = [value] + [lax.ppermute(value, axis, [(i, i ^ s) for i in range(4)]) for s in (1, 2, 3)]
    return (got[0] + got[1]) + (got[2] + got[3])


def butterfly(value, axes):
    for stage in butterfly_stages(axes):
        value = stage(value)
    return value


def lane_sums(a, b):
    return jnp.sum((a * b).reshape(-1, a.shape[-1]), axis=0)


def finish(total, count):
    return [jnp.sum(part) for part in jnp.split(total, count)]


def reduce_scalars(scalars):
    total = butterfly(lax.optimization_barrier(jnp.concatenate(scalars)), ALL)
    return finish(total, len(scalars))


def fold_four(payload, local, axis, dim, width):
    me = lax.axis_index(axis)
    length = local.shape[dim]
    last = lax.slice_in_dim(local, length - width, length, axis=dim)
    leading = lax.slice_in_dim(local, 0, width, axis=dim)
    even = me % 2 == 0
    count = payload.shape[0]

    def send(slab, step):
        message = jnp.concatenate([payload, slab.reshape(-1)])
        return lax.ppermute(message, axis, [(i, i ^ step) for i in range(4)])

    got_one = send(jnp.where(even, last, leading), 1)
    got_two = lax.ppermute(payload, axis, [(i, i ^ 2) for i in range(4)])
    got_three = send(jnp.where(me == 1, last, leading), 3)
    total = (payload + got_one[:count]) + (got_two + got_three[:count])
    from_one = got_one[count:].reshape(last.shape)
    from_three = got_three[count:].reshape(last.shape)
    zero = jnp.zeros_like(from_one)
    before = jnp.where(even, jnp.where(me == 2, from_three, zero), from_one)
    after = jnp.where(even, from_one, jnp.where(me == 1, from_three, zero))
    return total, jnp.concatenate([before, local, after], axis=dim)


def reduce_coarse(local, buffer, scalars):
    count = sum(part.shape[0] for part in scalars)
    width = RIM + 1
    payload = jnp.concatenate([buffer.reshape(-1)] + list(scalars))
    for axis, dim in (("ga", 1), ("gz", 2)):
        if lax.axis_size(axis) == 4:
            payload, local = fold_four(payload, local, axis, dim, width)
        else:
            payload = butterfly(payload, (axis,))
            local = pad_side(local, axis, dim, width)
        local, payload = lax.optimization_barrier((local, payload))
    size = payload.shape[0] - count
    whole = payload[:size].reshape(buffer.shape)
    if lax.axis_size("gx") == 2:
        first = lax.axis_index("gx") == 0
        length = local.shape[0]
        slab = jnp.where(first, local[length - width :], local[:width])
        message = jnp.concatenate([payload, slab.reshape(-1)])
        got = lax.ppermute(message, "gx", [(0, 1), (1, 0)])
        total = payload[size:] + got[size : size + count]
        other = got[:size].reshape(buffer.shape)
        beside = got[size + count :].reshape(slab.shape)
        zero = jnp.zeros_like(other)
        lo, hi = jnp.where(first, zero, other), jnp.where(first, other, zero)
        flat = jnp.zeros_like(beside)
        local = jnp.concatenate(
            [jnp.where(first, flat, beside), local, jnp.where(first, beside, flat)], axis=0
        )
    else:
        total = butterfly(payload[size:], ("gx",))
        gx = lax.axis_size("gx")
        up = [(i, i + 1) for i in range(gx - 1)]
        lo = lax.ppermute(whole, "gx", up)
        hi = lax.ppermute(whole, "gx", [(j, i) for i, j in up])
        local = pad_side(local, "gx", 0, width)
    return local, (lo, whole, hi), finish(total, len(scalars))


def body(right_side, diagonal, basis_tables, eigenvalues, coarse_blocks, coarse_columns):
    blocks = coarse_blocks.reshape(coarse_blocks.shape[3:])
    columns = coarse_columns.reshape(coarse_columns.shape[3])
    count = blocks.shape[0]
    group = lax.axis_size(("ga", "gz"))
    selector = (columns[:, None] == jnp.arange(group, dtype=jnp.int32)[None, :]).astype(jnp.float32)
    shape = right_side.shape
    wide_pair = jnp.stack([diagonal, right_side])
    table = element_table(blocks, columns, shape)
    for axis, dim in SIDES:
        wide_pair, table = pad_together([wide_pair, table], axis, (dim + 1, dim), (RIM, 1))
    wide_diagonal, wide_residual = wide_pair[0], wide_pair[1]
    inside = inside_grid(shape, RIM)

    def precondition_rim(wide_field, field):
        local = schwarz_part(wide_field, basis_tables, eigenvalues)
        return local, coarse_terms(field, blocks, selector)

    def coarse_on_rim(wholes):
        return spread_rim(coarse_rim(wholes, table, count, group), RIM + 1, shape)

    solution = jnp.zeros_like(right_side)
    residual = interior(wide_residual, RIM)
    wide_local, terms = precondition_rim(wide_residual, residual)
    wide_local, wholes, (square,) = reduce_coarse(wide_local, terms, [lane_sums(residual, residual)])
    for restart in range(CYCLES):
        residual = interior(wide_residual, RIM)
        initial_norm = jnp.sqrt(square)
        first_vector = residual / initial_norm
        wide_local_r, wholes_r = wide_local, wholes
        wide_zed = (wide_local_r + coarse_on_rim(wholes_r)) / initial_norm
        first_zed = interior(wide_zed, RIM + 1)
        wide_first = operate_rim(wide_zed, wide_diagonal, inside)
        first_image = interior(wide_first, RIM)
        wide_local, terms = precondition_rim(wide_first, first_image)
        wide_local_w, wholes_w, (first_proj, image_square) = reduce_coarse(
            wide_local, terms, [lane_sums(first_vector, first_image), lane_sums(first_image, first_image)]
        )
        first_len = jnp.sqrt(image_square - first_proj * first_proj)
        second_vector = (first_image - first_proj * first_vector) / first_len
        wide_second_zed = (wide_local_w + coarse_on_rim(wholes_w) - first_proj * wide_zed) / first_len
        second_zed = interior(wide_second_zed, RIM + 1)
        wide_second = operate_rim(wide_second_zed, wide_diagonal, inside)
        second_image = interior(wide_second, RIM)
        products = [
            lane_sums(first_vector, second_image),
            lane_sums(second_vector, second_image),
            lane_sums(second_image, second_image),
        ]
        last = restart == CYCLES - 1
        if last:
            upper_proj, lower_proj, second_square = reduce_scalars(products)
        else:
            wide_local, terms = precondition_rim(wide_second, second_image)
            wide_local_s, wholes_s, (upper_proj, lower_proj, second_square, cross) = reduce_coarse(
                wide_local, terms, products + [lane_sums(first_image, second_image)]
            )
        second_len = jnp.sqrt(second_square - upper_proj * upper_proj - lower_proj * lower_proj)
        gram_first = first_proj * first_proj + first_len * first_len
        gram_cross = first_proj * upper_proj + first_len * lower_proj
        gram_second = upper_proj * upper_proj + lower_proj * lower_proj + second_len * second_len
        target_first = initial_norm * first_proj
        target_second = initial_norm * upper_proj
        determinant = gram_first * gram_second - gram_cross * gram_cross
        weight_first = (gram_second * target_first - gram_cross * target_second) / determinant
        weight_second = (gram_first * target_second - gram_cross * target_first) / determinant
        solution = solution + weight_first * first_zed + weight_second * second_zed
        wide_residual = wide_residual - weight_first * wide_first - weight_second * wide_second
        if not last:
            wide_local = wide_local_r - weight_first * wide_local_w - weight_second * wide_local_s
            wholes = tuple(
                r - weight_first * w - weight_second * s for r, w, s in zip(wholes_r, wholes_w, wholes_s)
            )
            square = (
                square
                - 2.0 * weight_first * target_first
                - 2.0 * weight_second * target_second
                + weight_first * weight_first * image_square
                + 2.0 * weight_first * weight_second * cross
                + weight_second * weight_second * second_square
            )
    return (solution, interior(wide_residual, RIM))


def solution(mesh):
    in_specs = (
        P("gx", "ga", "gz"),
        P("gx", "ga", "gz"),
        P(),
        P(),
        P("gx", "ga", "gz", None, None, None),
        P("gx", "ga", "gz", None),
    )
    out_specs = (P("gx", "ga", "gz"), P("gx", "ga", "gz"))
    return jax.shard_map(body, mesh=mesh, in_specs=in_specs, out_specs=out_specs, check_vma=False)
```

```python
import functools

import jax
import jax.numpy as jnp
from jax import lax
from jax.sharding import PartitionSpec as P

PTS = 8
RIM = 2
WIDE = 12
CYCLES = 2


PRECISE = lax.Precision.HIGHEST
TRANSFORM = lax.Precision.HIGH


def pad_side(value, axis, dim, width):
    size, length = (lax.axis_size(axis), value.shape[dim])
    last = lax.slice_in_dim(value, length - width, length, axis=dim)
    leading = lax.slice_in_dim(value, 0, width, axis=dim)
    if size == 2:
        first = lax.axis_index(axis) == 0
        got = lax.ppermute(jnp.where(first, last, leading), axis, [(0, 1), (1, 0)])
        zero = jnp.zeros_like(got)
        before = jnp.where(first, zero, got)
        after = jnp.where(first, got, zero)
    else:
        up = [(i, (i + 1) % size) for i in range(size - 1)]
        down = [(j, i) for i, j in up]
        before = lax.ppermute(last, axis, up)
        after = lax.ppermute(leading, axis, down)
    return jnp.concatenate([before, value, after], axis=dim)


def padded_2(value, sides, width):
    for axis, dim in sides:
        value = pad_side(value, axis, dim, width)
    return value


def pad_together(values, axis, dims, widths):
    lasts, leads = [], []
    for value, dim, width in zip(values, dims, widths):
        length = value.shape[dim]
        lasts.append(lax.slice_in_dim(value, length - width, length, axis=dim))
        leads.append(lax.slice_in_dim(value, 0, width, axis=dim))

    def pack(slabs):
        return jnp.concatenate([slab.reshape(-1) for slab in slabs])

    def unpack(flat):
        pieces, at = [], 0
        for slab in lasts:
            pieces.append(flat[at : at + slab.size].reshape(slab.shape))
            at += slab.size
        return pieces

    size = lax.axis_size(axis)
    if size == 2:
        first = lax.axis_index(axis) == 0
        got = unpack(lax.ppermute(jnp.where(first, pack(lasts), pack(leads)), axis, [(0, 1), (1, 0)]))
        befores = [jnp.where(first, jnp.zeros_like(g), g) for g in got]
        afters = [jnp.where(first, g, jnp.zeros_like(g)) for g in got]
    elif size == 4:
        me = lax.axis_index(axis)
        even = me % 2 == 0
        to_one = jnp.where(even, pack(lasts), pack(leads))
        to_three = jnp.where(me == 1, pack(lasts), pack(leads))
        from_one = unpack(lax.ppermute(to_one, axis, [(i, i ^ 1) for i in range(4)]))
        from_three = unpack(lax.ppermute(to_three, axis, [(i, i ^ 3) for i in range(4)]))
        befores = [
            jnp.where(even, jnp.where(me == 2, t, jnp.zeros_like(t)), o)
            for o, t in zip(from_one, from_three)
        ]
        afters = [
            jnp.where(even, o, jnp.where(me == 1, t, jnp.zeros_like(t)))
            for o, t in zip(from_one, from_three)
        ]
    else:
        up = [(i, (i + 1) % size) for i in range(size - 1)]
        befores = unpack(lax.ppermute(pack(lasts), axis, up))
        afters = unpack(lax.ppermute(pack(leads), axis, [(j, i) for i, j in up]))
    return [
        jnp.concatenate([before, value, after], axis=dim)
        for before, value, after, dim in zip(befores, values, afters, dims)
    ]


SIDES = (("gx", 0), ("ga", 1), ("gz", 2))


def operate_rim(zed, diagonal, inside):
    centre = zed[1:-1, 1:-1, 1:-1]
    beside = zed[2:, 1:-1, 1:-1] + zed[:-2, 1:-1, 1:-1]
    beside = beside + zed[1:-1, 2:, 1:-1] + zed[1:-1, :-2, 1:-1]
    beside = beside + zed[1:-1, 1:-1, 2:] + zed[1:-1, 1:-1, :-2]
    return ((6.0 + diagonal) * centre - beside) * inside


def inside_grid(shape, width):
    result = None
    for axis, dim in SIDES:
        length = shape[dim]
        place = lax.axis_index(axis) * length - width + jnp.arange(length + 2 * width, dtype=jnp.int32)
        line = ((place >= 0) & (place < lax.axis_size(axis) * length)).astype(jnp.float32)
        view = [1, 1, 1]
        view[dim] = length + 2 * width
        line = line.reshape(view)
        result = line if result is None else result * line
    return result


def interior(value, width):
    return value[width:-width, width:-width, width:-width]


def forward_table(count, basis):
    row_index = jnp.arange(PTS * count + 2 * RIM, dtype=jnp.int32)
    element = jnp.arange(count, dtype=jnp.int32)
    offset = jnp.arange(WIDE, dtype=jnp.int32)
    select = (
        row_index[:, None, None] == PTS * element[None, :, None] + offset[None, None, :]
    ).astype(jnp.float32)
    table = jnp.einsum("rcj,jm->rcm", select, basis, precision=PRECISE)
    return table.reshape(PTS * count + 2 * RIM, count * WIDE)


def backward_table(count, basis):
    same = jnp.eye(count, dtype=jnp.float32)
    table = jnp.einsum("cd,im->cmdi", same, basis[RIM : RIM + PTS], precision=PRECISE)
    return table.reshape(count * WIDE, count * PTS)


def schwarz_part(padded, basis_tables, eigenvalues):
    count_x = (padded.shape[0] - 2 * RIM) // PTS
    count_y = (padded.shape[1] - 2 * RIM) // PTS
    count_z = (padded.shape[2] - 2 * RIM) // PTS
    spectral = jnp.einsum(
        "pqr,rc->pqc", padded, forward_table(count_z, basis_tables[2]), precision=TRANSFORM
    )
    spectral = jnp.einsum(
        "pqc,pa->aqc", spectral, forward_table(count_x, basis_tables[0]), precision=TRANSFORM
    )
    spectral = jnp.einsum(
        "aqc,qb->abc", spectral, forward_table(count_y, basis_tables[1]), precision=TRANSFORM
    )
    denominator = (
        jnp.tile(eigenvalues[0], count_x)[:, None, None]
        + jnp.tile(eigenvalues[1], count_y)[None, :, None]
    )
    denominator = denominator + jnp.tile(eigenvalues[2], count_z)[None, None, :]
    spectral = spectral / denominator
    local_part = jnp.einsum(
        "abc,cr->abr", spectral, backward_table(count_z, basis_tables[2]), precision=TRANSFORM
    )
    local_part = jnp.einsum(
        "abr,ap->pbr", local_part, backward_table(count_x, basis_tables[0]), precision=TRANSFORM
    )
    local_part = jnp.einsum(
        "pbr,bq->pqr", local_part, backward_table(count_y, basis_tables[1]), precision=TRANSFORM
    )
    return local_part


def coarse_terms(field, blocks, selector):
    count_x = field.shape[0] // PTS
    count_y = field.shape[1] // PTS
    count_z = field.shape[2] // PTS
    cells = count_x * count_y * count_z
    point = jnp.arange(field.shape[2], dtype=jnp.int32)
    along = (point[:, None] // PTS == jnp.arange(count_z, dtype=jnp.int32)[None, :]).astype(jnp.float32)
    sums = jnp.einsum("pqr,rc->pqc", field, along, precision=PRECISE)
    sums = jnp.sum(sums.reshape(count_x, PTS, count_y, PTS, count_z), axis=(1, 3))
    restricted = sums.reshape(cells) * (1.0 / PTS**3)
    terms = jnp.einsum("kpq,p->kq", blocks, restricted, precision=PRECISE)
    return jnp.einsum("kj,kq->jq", selector, terms, precision=PRECISE)


def element_table(blocks, columns, shape):
    count = blocks.shape[0]
    grid = (shape[0] // PTS, shape[1] // PTS, shape[2] // PTS)
    rows = jnp.transpose(blocks, (1, 0, 2)).reshape(grid + (count * blocks.shape[2],))
    cols = jnp.broadcast_to(columns.astype(jnp.float32), grid + (count,))
    return jnp.concatenate([rows, cols], axis=-1)


def coarse_rim(wholes, table, count, group):
    lo, whole, hi = wholes
    grid = table.shape[:3]
    width = (table.shape[3] - count) // count
    rows = table[..., : count * width].reshape(grid + (count, width))
    cols = table[..., count * width :]
    onehot = (cols[..., None] == jnp.arange(group, dtype=jnp.float32)).astype(jnp.float32)
    stacked = jnp.stack([lo] + [whole] * (grid[0] - 2) + [hi])
    picked = jnp.einsum("abckg,agq->abckq", onehot, stacked, precision=PRECISE)
    return jnp.sum(rows * picked, axis=(3, 4))


def spread_rim(values, width, shape):
    def table(length, count):
        point = jnp.arange(length + 2 * width, dtype=jnp.int32) - width + PTS
        element = jnp.arange(count, dtype=jnp.int32)
        return (point[:, None] // PTS == element[None, :]).astype(jnp.float32)

    grid = values.shape
    out = jnp.einsum("abc,rc->abr", values, table(shape[2], grid[2]), precision=PRECISE)
    out = jnp.einsum("abr,pa->pbr", out, table(shape[0], grid[0]), precision=PRECISE)
    return jnp.einsum("pbr,qb->pqr", out, table(shape[1], grid[1]), precision=PRECISE)


ALL = ("gx", "ga", "gz")


def butterfly_stages(axes):
    stages = []
    for axis in axes:
        size = lax.axis_size(axis)
        if size & (size - 1):
            stages.append(lambda value, axis=axis: lax.psum(value, axis))
            continue
        if size == 4:
            stages.append(functools.partial(sum_of_four, axis=axis))
            continue
        step = 1
        while step < size:
            pairs = [(i, i ^ step) for i in range(size)]
            stages.append(lambda value, axis=axis, pairs=pairs: value + lax.ppermute(value, axis, pairs))
            step *= 2
    return stages


def sum_of_four(value, axis):
    got = [value] + [lax.ppermute(value, axis, [(i, i ^ s) for i in range(4)]) for s in (1, 2, 3)]
    return (got[0] + got[1]) + (got[2] + got[3])


def butterfly(value, axes):
    for stage in butterfly_stages(axes):
        value = stage(value)
    return value


def lane_sums(a, b):
    return jnp.sum((a * b).reshape(-1, a.shape[-1]), axis=0)


def finish(total, count):
    return [jnp.sum(part) for part in jnp.split(total, count)]


def reduce_scalars(scalars):
    total = butterfly(lax.optimization_barrier(jnp.concatenate(scalars)), ALL)
    return finish(total, len(scalars))


def fold_four(payload, local, axis, dim, width):
    me = lax.axis_index(axis)
    length = local.shape[dim]
    last = lax.slice_in_dim(local, length - width, length, axis=dim)
    leading = lax.slice_in_dim(local, 0, width, axis=dim)
    even = me % 2 == 0
    count = payload.shape[0]

    def send(slab, step):
        message = jnp.concatenate([payload, slab.reshape(-1)])
        return lax.ppermute(message, axis, [(i, i ^ step) for i in range(4)])

    got_one = send(jnp.where(even, last, leading), 1)
    got_two = lax.ppermute(payload, axis, [(i, i ^ 2) for i in range(4)])
    got_three = send(jnp.where(me == 1, last, leading), 3)
    total = (payload + got_one[:count]) + (got_two + got_three[:count])
    from_one = got_one[count:].reshape(last.shape)
    from_three = got_three[count:].reshape(last.shape)
    zero = jnp.zeros_like(from_one)
    before = jnp.where(even, jnp.where(me == 2, from_three, zero), from_one)
    after = jnp.where(even, from_one, jnp.where(me == 1, from_three, zero))
    return total, jnp.concatenate([before, local, after], axis=dim)


def reduce_coarse(local, buffer, scalars):
    count = sum(part.shape[0] for part in scalars)
    width = RIM + 1
    payload = jnp.concatenate([buffer.reshape(-1)] + list(scalars))
    local, payload = lax.optimization_barrier((local, payload))
    for axis, dim in (("gz", 2), ("ga", 1)):
        if lax.axis_size(axis) == 4:
            payload, local = fold_four(payload, local, axis, dim, width)
        else:
            payload = butterfly(payload, (axis,))
            local = pad_side(local, axis, dim, width)
        local, payload = lax.optimization_barrier((local, payload))
    size = payload.shape[0] - count
    whole = payload[:size].reshape(buffer.shape)
    if lax.axis_size("gx") == 2:
        first = lax.axis_index("gx") == 0
        length = local.shape[0]
        slab = jnp.where(first, local[length - width :], local[:width])
        message = jnp.concatenate([payload, slab.reshape(-1)])
        got = lax.ppermute(message, "gx", [(0, 1), (1, 0)])
        total = payload[size:] + got[size : size + count]
        other = got[:size].reshape(buffer.shape)
        beside = got[size + count :].reshape(slab.shape)
        zero = jnp.zeros_like(other)
        lo, hi = jnp.where(first, zero, other), jnp.where(first, other, zero)
        flat = jnp.zeros_like(beside)
        local = jnp.concatenate(
            [jnp.where(first, flat, beside), local, jnp.where(first, beside, flat)], axis=0
        )
    else:
        total = butterfly(payload[size:], ("gx",))
        gx = lax.axis_size("gx")
        up = [(i, i + 1) for i in range(gx - 1)]
        lo = lax.ppermute(whole, "gx", up)
        hi = lax.ppermute(whole, "gx", [(j, i) for i, j in up])
        local = pad_side(local, "gx", 0, width)
    return local, (lo, whole, hi), finish(total, len(scalars))


def body(right_side, diagonal, basis_tables, eigenvalues, coarse_blocks, coarse_columns):
    blocks = coarse_blocks.reshape(coarse_blocks.shape[3:])
    columns = coarse_columns.reshape(coarse_columns.shape[3])
    count = blocks.shape[0]
    group = lax.axis_size(("ga", "gz"))
    selector = (columns[:, None] == jnp.arange(group, dtype=jnp.int32)[None, :]).astype(jnp.float32)
    shape = right_side.shape
    wide_pair = jnp.stack([diagonal, right_side])
    table = element_table(blocks, columns, shape)
    for axis, dim in SIDES:
        wide_pair, table = pad_together([wide_pair, table], axis, (dim + 1, dim), (RIM, 1))
    wide_diagonal, wide_residual = wide_pair[0], wide_pair[1]
    inside = inside_grid(shape, RIM)

    def precondition_rim(wide_field, field):
        local = schwarz_part(wide_field, basis_tables, eigenvalues)
        return local, coarse_terms(field, blocks, selector)

    def coarse_on_rim(wholes):
        return spread_rim(coarse_rim(wholes, table, count, group), RIM + 1, shape)

    solution = jnp.zeros_like(right_side)
    residual = interior(wide_residual, RIM)
    wide_local, terms = precondition_rim(wide_residual, residual)
    wide_local, wholes, (square,) = reduce_coarse(wide_local, terms, [lane_sums(residual, residual)])
    for restart in range(CYCLES):
        residual = interior(wide_residual, RIM)
        initial_norm = jnp.sqrt(square)
        first_vector = residual / initial_norm
        wide_local_r, wholes_r = wide_local, wholes
        wide_zed = (wide_local_r + coarse_on_rim(wholes_r)) / initial_norm
        first_zed = interior(wide_zed, RIM + 1)
        wide_first = operate_rim(wide_zed, wide_diagonal, inside)
        first_image = interior(wide_first, RIM)
        wide_local, terms = precondition_rim(wide_first, first_image)
        wide_local_w, wholes_w, (first_proj, image_square) = reduce_coarse(
            wide_local, terms, [lane_sums(first_vector, first_image), lane_sums(first_image, first_image)]
        )
        first_len = jnp.sqrt(image_square - first_proj * first_proj)
        second_vector = (first_image - first_proj * first_vector) / first_len
        wide_second_zed = (wide_local_w + coarse_on_rim(wholes_w) - first_proj * wide_zed) / first_len
        second_zed = interior(wide_second_zed, RIM + 1)
        wide_second = operate_rim(wide_second_zed, wide_diagonal, inside)
        second_image = interior(wide_second, RIM)
        products = [
            lane_sums(first_vector, second_image),
            lane_sums(second_vector, second_image),
            lane_sums(second_image, second_image),
        ]
        last = restart == CYCLES - 1
        if last:
            upper_proj, lower_proj, second_square = reduce_scalars(products)
        else:
            wide_local, terms = precondition_rim(wide_second, second_image)
            wide_local_s, wholes_s, (upper_proj, lower_proj, second_square, cross) = reduce_coarse(
                wide_local, terms, products + [lane_sums(first_image, second_image)]
            )
        second_len = jnp.sqrt(second_square - upper_proj * upper_proj - lower_proj * lower_proj)
        gram_first = first_proj * first_proj + first_len * first_len
        gram_cross = first_proj * upper_proj + first_len * lower_proj
        gram_second = upper_proj * upper_proj + lower_proj * lower_proj + second_len * second_len
        target_first = initial_norm * first_proj
        target_second = initial_norm * upper_proj
        determinant = gram_first * gram_second - gram_cross * gram_cross
        weight_first = (gram_second * target_first - gram_cross * target_second) / determinant
        weight_second = (gram_first * target_second - gram_cross * target_first) / determinant
        solution = solution + weight_first * first_zed + weight_second * second_zed
        wide_residual = wide_residual - weight_first * wide_first - weight_second * wide_second
        if not last:
            wide_local = wide_local_r - weight_first * wide_local_w - weight_second * wide_local_s
            wholes = tuple(
                r - weight_first * w - weight_second * s for r, w, s in zip(wholes_r, wholes_w, wholes_s)
            )
            square = (
                square
                - 2.0 * weight_first * target_first
                - 2.0 * weight_second * target_second
                + weight_first * weight_first * image_square
                + 2.0 * weight_first * weight_second * cross
                + weight_second * weight_second * second_square
            )
    return (solution, interior(wide_residual, RIM))


def solution(mesh):
    in_specs = (
        P("gx", "ga", "gz"),
        P("gx", "ga", "gz"),
        P(),
        P(),
        P("gx", "ga", "gz", None, None, None),
        P("gx", "ga", "gz", None),
    )
    out_specs = (P("gx", "ga", "gz"), P("gx", "ga", "gz"))
    return jax.shard_map(body, mesh=mesh, in_specs=in_specs, out_specs=out_specs, check_vma=False)
```

```python
import functools

import jax
import jax.numpy as jnp
from jax import lax
from jax.sharding import PartitionSpec as P

PTS = 8
RIM = 2
WIDE = 12
CYCLES = 2


PRECISE = lax.Precision.HIGHEST
TRANSFORM = lax.Precision.HIGH


def pad_side(value, axis, dim, width):
    size, length = (lax.axis_size(axis), value.shape[dim])
    last = lax.slice_in_dim(value, length - width, length, axis=dim)
    leading = lax.slice_in_dim(value, 0, width, axis=dim)
    if size == 2:
        first = lax.axis_index(axis) == 0
        got = lax.ppermute(jnp.where(first, last, leading), axis, [(0, 1), (1, 0)])
        zero = jnp.zeros_like(got)
        before = jnp.where(first, zero, got)
        after = jnp.where(first, got, zero)
    else:
        up = [(i, (i + 1) % size) for i in range(size - 1)]
        down = [(j, i) for i, j in up]
        before = lax.ppermute(last, axis, up)
        after = lax.ppermute(leading, axis, down)
    return jnp.concatenate([before, value, after], axis=dim)


def padded_2(value, sides, width):
    for axis, dim in sides:
        value = pad_side(value, axis, dim, width)
    return value


def pad_together(values, axis, dims, widths):
    lasts, leads = [], []
    for value, dim, width in zip(values, dims, widths):
        length = value.shape[dim]
        lasts.append(lax.slice_in_dim(value, length - width, length, axis=dim))
        leads.append(lax.slice_in_dim(value, 0, width, axis=dim))

    def pack(slabs):
        return jnp.concatenate([slab.reshape(-1) for slab in slabs])

    def unpack(flat):
        pieces, at = [], 0
        for slab in lasts:
            pieces.append(flat[at : at + slab.size].reshape(slab.shape))
            at += slab.size
        return pieces

    size = lax.axis_size(axis)
    if size == 2:
        first = lax.axis_index(axis) == 0
        got = unpack(lax.ppermute(jnp.where(first, pack(lasts), pack(leads)), axis, [(0, 1), (1, 0)]))
        befores = [jnp.where(first, jnp.zeros_like(g), g) for g in got]
        afters = [jnp.where(first, g, jnp.zeros_like(g)) for g in got]
    elif size == 4:
        me = lax.axis_index(axis)
        even = me % 2 == 0
        to_one = jnp.where(even, pack(lasts), pack(leads))
        to_three = jnp.where(me == 1, pack(lasts), pack(leads))
        from_one = unpack(lax.ppermute(to_one, axis, [(i, i ^ 1) for i in range(4)]))
        from_three = unpack(lax.ppermute(to_three, axis, [(i, i ^ 3) for i in range(4)]))
        befores = [
            jnp.where(even, jnp.where(me == 2, t, jnp.zeros_like(t)), o)
            for o, t in zip(from_one, from_three)
        ]
        afters = [
            jnp.where(even, o, jnp.where(me == 1, t, jnp.zeros_like(t)))
            for o, t in zip(from_one, from_three)
        ]
    else:
        up = [(i, (i + 1) % size) for i in range(size - 1)]
        befores = unpack(lax.ppermute(pack(lasts), axis, up))
        afters = unpack(lax.ppermute(pack(leads), axis, [(j, i) for i, j in up]))
    return [
        jnp.concatenate([before, value, after], axis=dim)
        for before, value, after, dim in zip(befores, values, afters, dims)
    ]


SIDES = (("gx", 0), ("ga", 1), ("gz", 2))


def operate_rim(zed, diagonal, inside):
    centre = zed[1:-1, 1:-1, 1:-1]
    beside = zed[2:, 1:-1, 1:-1] + zed[:-2, 1:-1, 1:-1]
    beside = beside + zed[1:-1, 2:, 1:-1] + zed[1:-1, :-2, 1:-1]
    beside = beside + zed[1:-1, 1:-1, 2:] + zed[1:-1, 1:-1, :-2]
    return ((6.0 + diagonal) * centre - beside) * inside


def inside_grid(shape, width):
    result = None
    for axis, dim in SIDES:
        length = shape[dim]
        place = lax.axis_index(axis) * length - width + jnp.arange(length + 2 * width, dtype=jnp.int32)
        line = ((place >= 0) & (place < lax.axis_size(axis) * length)).astype(jnp.float32)
        view = [1, 1, 1]
        view[dim] = length + 2 * width
        line = line.reshape(view)
        result = line if result is None else result * line
    return result


def interior(value, width):
    return value[width:-width, width:-width, width:-width]


def forward_table(count, basis):
    row_index = jnp.arange(PTS * count + 2 * RIM, dtype=jnp.int32)
    element = jnp.arange(count, dtype=jnp.int32)
    offset = jnp.arange(WIDE, dtype=jnp.int32)
    select = (
        row_index[:, None, None] == PTS * element[None, :, None] + offset[None, None, :]
    ).astype(jnp.float32)
    table = jnp.einsum("rcj,jm->rcm", select, basis, precision=PRECISE)
    return table.reshape(PTS * count + 2 * RIM, count * WIDE)


def backward_table(count, basis):
    same = jnp.eye(count, dtype=jnp.float32)
    table = jnp.einsum("cd,im->cmdi", same, basis[RIM : RIM + PTS], precision=PRECISE)
    return table.reshape(count * WIDE, count * PTS)


def schwarz_part(padded, basis_tables, eigenvalues):
    count_x = (padded.shape[0] - 2 * RIM) // PTS
    count_y = (padded.shape[1] - 2 * RIM) // PTS
    count_z = (padded.shape[2] - 2 * RIM) // PTS
    spectral = jnp.einsum(
        "pqr,rc->pqc", padded, forward_table(count_z, basis_tables[2]), precision=TRANSFORM
    )
    spectral = jnp.einsum(
        "pqc,pa->aqc", spectral, forward_table(count_x, basis_tables[0]), precision=TRANSFORM
    )
    spectral = jnp.einsum(
        "aqc,qb->abc", spectral, forward_table(count_y, basis_tables[1]), precision=TRANSFORM
    )
    denominator = (
        jnp.tile(eigenvalues[0], count_x)[:, None, None]
        + jnp.tile(eigenvalues[1], count_y)[None, :, None]
    )
    denominator = denominator + jnp.tile(eigenvalues[2], count_z)[None, None, :]
    spectral = spectral / denominator
    local_part = jnp.einsum(
        "abc,cr->abr", spectral, backward_table(count_z, basis_tables[2]), precision=TRANSFORM
    )
    local_part = jnp.einsum(
        "abr,ap->pbr", local_part, backward_table(count_x, basis_tables[0]), precision=TRANSFORM
    )
    local_part = jnp.einsum(
        "pbr,bq->pqr", local_part, backward_table(count_y, basis_tables[1]), precision=TRANSFORM
    )
    return local_part


def coarse_terms(field, blocks, selector):
    count_x = field.shape[0] // PTS
    count_y = field.shape[1] // PTS
    count_z = field.shape[2] // PTS
    cells = count_x * count_y * count_z
    point = jnp.arange(field.shape[2], dtype=jnp.int32)
    along = (point[:, None] // PTS == jnp.arange(count_z, dtype=jnp.int32)[None, :]).astype(jnp.float32)
    sums = jnp.einsum("pqr,rc->pqc", field, along, precision=PRECISE)
    sums = jnp.sum(sums.reshape(count_x, PTS, count_y, PTS, count_z), axis=(1, 3))
    restricted = sums.reshape(cells) * (1.0 / PTS**3)
    terms = jnp.einsum("kpq,p->kq", blocks, restricted, precision=PRECISE)
    return jnp.einsum("kj,kq->jq", selector, terms, precision=PRECISE)


def element_table(blocks, columns, shape):
    count = blocks.shape[0]
    grid = (shape[0] // PTS, shape[1] // PTS, shape[2] // PTS)
    rows = jnp.transpose(blocks, (1, 0, 2)).reshape(grid + (count * blocks.shape[2],))
    cols = jnp.broadcast_to(columns.astype(jnp.float32), grid + (count,))
    return jnp.concatenate([rows, cols], axis=-1)


def coarse_rim(wholes, table, count, group):
    lo, whole, hi = wholes
    grid = table.shape[:3]
    width = (table.shape[3] - count) // count
    rows = table[..., : count * width].reshape(grid + (count, width))
    cols = table[..., count * width :]
    onehot = (cols[..., None] == jnp.arange(group, dtype=jnp.float32)).astype(jnp.float32)
    stacked = jnp.stack([lo] + [whole] * (grid[0] - 2) + [hi])
    picked = jnp.einsum("abckg,agq->abckq", onehot, stacked, precision=PRECISE)
    return jnp.sum(rows * picked, axis=(3, 4))


def spread_rim(values, width, shape):
    def table(length, count):
        point = jnp.arange(length + 2 * width, dtype=jnp.int32) - width + PTS
        element = jnp.arange(count, dtype=jnp.int32)
        return (point[:, None] // PTS == element[None, :]).astype(jnp.float32)

    grid = values.shape
    out = jnp.einsum("abc,rc->abr", values, table(shape[2], grid[2]), precision=PRECISE)
    out = jnp.einsum("abr,pa->pbr", out, table(shape[0], grid[0]), precision=PRECISE)
    return jnp.einsum("pbr,qb->pqr", out, table(shape[1], grid[1]), precision=PRECISE)


ALL = ("gx", "ga", "gz")


def butterfly_stages(axes):
    stages = []
    for axis in axes:
        size = lax.axis_size(axis)
        if size & (size - 1):
            stages.append(lambda value, axis=axis: lax.psum(value, axis))
            continue
        if size == 4:
            stages.append(functools.partial(sum_of_four, axis=axis))
            continue
        step = 1
        while step < size:
            pairs = [(i, i ^ step) for i in range(size)]
            stages.append(lambda value, axis=axis, pairs=pairs: value + lax.ppermute(value, axis, pairs))
            step *= 2
    return stages


def sum_of_four(value, axis):
    got = [value] + [lax.ppermute(value, axis, [(i, i ^ s) for i in range(4)]) for s in (1, 2, 3)]
    return (got[0] + got[1]) + (got[2] + got[3])


def butterfly(value, axes):
    for stage in butterfly_stages(axes):
        value = stage(value)
    return value


def lane_sums(a, b):
    return jnp.sum((a * b).reshape(-1, a.shape[-1]), axis=0)


def finish(total, count):
    return [jnp.sum(part) for part in jnp.split(total, count)]


def reduce_scalars(scalars):
    total = butterfly(lax.optimization_barrier(jnp.concatenate(scalars)), ("ga", "gz", "gx"))
    return finish(total, len(scalars))


def fold_four(payload, local, axis, dim, width):
    me = lax.axis_index(axis)
    length = local.shape[dim]
    last = lax.slice_in_dim(local, length - width, length, axis=dim)
    leading = lax.slice_in_dim(local, 0, width, axis=dim)
    even = me % 2 == 0
    count = payload.shape[0]

    def send(slab, step):
        message = jnp.concatenate([payload, slab.reshape(-1)])
        return lax.ppermute(message, axis, [(i, i ^ step) for i in range(4)])

    got_one = send(jnp.where(even, last, leading), 1)
    got_two = lax.ppermute(payload, axis, [(i, i ^ 2) for i in range(4)])
    got_three = send(jnp.where(me == 1, last, leading), 3)
    total = (payload + got_one[:count]) + (got_two + got_three[:count])
    from_one = got_one[count:].reshape(last.shape)
    from_three = got_three[count:].reshape(last.shape)
    zero = jnp.zeros_like(from_one)
    before = jnp.where(even, jnp.where(me == 2, from_three, zero), from_one)
    after = jnp.where(even, from_one, jnp.where(me == 1, from_three, zero))
    return total, jnp.concatenate([before, local, after], axis=dim)


def reduce_coarse(local, buffer, scalars):
    count = sum(part.shape[0] for part in scalars)
    width = RIM + 1
    payload = jnp.concatenate([buffer.reshape(-1)] + list(scalars))
    local, payload = lax.optimization_barrier((local, payload))
    for axis, dim in (("ga", 1), ("gz", 2)):
        if lax.axis_size(axis) == 4:
            payload, local = fold_four(payload, local, axis, dim, width)
        else:
            payload = butterfly(payload, (axis,))
            local = pad_side(local, axis, dim, width)
        local, payload = lax.optimization_barrier((local, payload))
    size = payload.shape[0] - count
    whole = payload[:size].reshape(buffer.shape)
    if lax.axis_size("gx") == 2:
        first = lax.axis_index("gx") == 0
        length = local.shape[0]
        slab = jnp.where(first, local[length - width :], local[:width])
        message = jnp.concatenate([payload, slab.reshape(-1)])
        got = lax.ppermute(message, "gx", [(0, 1), (1, 0)])
        total = payload[size:] + got[size : size + count]
        other = got[:size].reshape(buffer.shape)
        beside = got[size + count :].reshape(slab.shape)
        zero = jnp.zeros_like(other)
        lo, hi = jnp.where(first, zero, other), jnp.where(first, other, zero)
        flat = jnp.zeros_like(beside)
        local = jnp.concatenate(
            [jnp.where(first, flat, beside), local, jnp.where(first, beside, flat)], axis=0
        )
    else:
        total = butterfly(payload[size:], ("gx",))
        gx = lax.axis_size("gx")
        up = [(i, i + 1) for i in range(gx - 1)]
        lo = lax.ppermute(whole, "gx", up)
        hi = lax.ppermute(whole, "gx", [(j, i) for i, j in up])
        local = pad_side(local, "gx", 0, width)
    return local, (lo, whole, hi), finish(total, len(scalars))


def body(right_side, diagonal, basis_tables, eigenvalues, coarse_blocks, coarse_columns):
    blocks = coarse_blocks.reshape(coarse_blocks.shape[3:])
    columns = coarse_columns.reshape(coarse_columns.shape[3])
    count = blocks.shape[0]
    group = lax.axis_size(("ga", "gz"))
    selector = (columns[:, None] == jnp.arange(group, dtype=jnp.int32)[None, :]).astype(jnp.float32)
    shape = right_side.shape
    wide_pair = jnp.stack([diagonal, right_side])
    table = element_table(blocks, columns, shape)
    for axis, dim in SIDES:
        wide_pair, table = pad_together([wide_pair, table], axis, (dim + 1, dim), (RIM, 1))
    wide_diagonal, wide_residual = wide_pair[0], wide_pair[1]
    inside = inside_grid(shape, RIM)

    def precondition_rim(wide_field, field):
        local = schwarz_part(wide_field, basis_tables, eigenvalues)
        return local, coarse_terms(field, blocks, selector)

    def coarse_on_rim(wholes):
        return spread_rim(coarse_rim(wholes, table, count, group), RIM + 1, shape)

    solution = jnp.zeros_like(right_side)
    residual = interior(wide_residual, RIM)
    wide_local, terms = precondition_rim(wide_residual, residual)
    wide_local, wholes, (square,) = reduce_coarse(wide_local, terms, [lane_sums(residual, residual)])
    for restart in range(CYCLES):
        residual = interior(wide_residual, RIM)
        initial_norm = jnp.sqrt(square)
        first_vector = residual / initial_norm
        wide_local_r, wholes_r = wide_local, wholes
        wide_zed = (wide_local_r + coarse_on_rim(wholes_r)) / initial_norm
        first_zed = interior(wide_zed, RIM + 1)
        wide_first = operate_rim(wide_zed, wide_diagonal, inside)
        first_image = interior(wide_first, RIM)
        wide_local, terms = precondition_rim(wide_first, first_image)
        wide_local_w, wholes_w, (first_proj, image_square) = reduce_coarse(
            wide_local, terms, [lane_sums(first_vector, first_image), lane_sums(first_image, first_image)]
        )
        first_len = jnp.sqrt(image_square - first_proj * first_proj)
        second_vector = (first_image - first_proj * first_vector) / first_len
        wide_second_zed = (wide_local_w + coarse_on_rim(wholes_w) - first_proj * wide_zed) / first_len
        second_zed = interior(wide_second_zed, RIM + 1)
        wide_second = operate_rim(wide_second_zed, wide_diagonal, inside)
        second_image = interior(wide_second, RIM)
        products = [
            lane_sums(first_vector, second_image),
            lane_sums(second_vector, second_image),
            lane_sums(second_image, second_image),
        ]
        last = restart == CYCLES - 1
        if last:
            upper_proj, lower_proj, second_square = reduce_scalars(products)
        else:
            wide_local, terms = precondition_rim(wide_second, second_image)
            wide_local_s, wholes_s, (upper_proj, lower_proj, second_square, cross) = reduce_coarse(
                wide_local, terms, products + [lane_sums(first_image, second_image)]
            )
        second_len = jnp.sqrt(second_square - upper_proj * upper_proj - lower_proj * lower_proj)
        gram_first = first_proj * first_proj + first_len * first_len
        gram_cross = first_proj * upper_proj + first_len * lower_proj
        gram_second = upper_proj * upper_proj + lower_proj * lower_proj + second_len * second_len
        target_first = initial_norm * first_proj
        target_second = initial_norm * upper_proj
        determinant = gram_first * gram_second - gram_cross * gram_cross
        weight_first = (gram_second * target_first - gram_cross * target_second) / determinant
        weight_second = (gram_first * target_second - gram_cross * target_first) / determinant
        solution = solution + weight_first * first_zed + weight_second * second_zed
        wide_residual = wide_residual - weight_first * wide_first - weight_second * wide_second
        if not last:
            wide_local = wide_local_r - weight_first * wide_local_w - weight_second * wide_local_s
            wholes = tuple(
                r - weight_first * w - weight_second * s for r, w, s in zip(wholes_r, wholes_w, wholes_s)
            )
            square = (
                square
                - 2.0 * weight_first * target_first
                - 2.0 * weight_second * target_second
                + weight_first * weight_first * image_square
                + 2.0 * weight_first * weight_second * cross
                + weight_second * weight_second * second_square
            )
    return (solution, interior(wide_residual, RIM))


def solution(mesh):
    in_specs = (
        P("gx", "ga", "gz"),
        P("gx", "ga", "gz"),
        P(),
        P(),
        P("gx", "ga", "gz", None, None, None),
        P("gx", "ga", "gz", None),
    )
    out_specs = (P("gx", "ga", "gz"), P("gx", "ga", "gz"))
    return jax.shard_map(body, mesh=mesh, in_specs=in_specs, out_specs=out_specs, check_vma=False)
```
